32 devices in a mesh: dp: 4 (over x, core), seq: 2 (over y), head: 4 (over z).
Axes of the slice: x: 2, y: 2, z: 4, core: 2. Of those that a mesh axis runs over, the one named last changes fastest.
Arguments:
- embed: bfloat16 [4, 1024, 1536], P('dp', 'seq', 'head'), may hold values from -6 to 6
- donor_pos: int32 [4, 256], P('dp', 'seq'), may hold values from -1 to 1023, as said below
- acceptor_pos: int32 [4, 256], P('dp', 'seq'), may hold values from -1 to 1023, as said below
- target: bfloat16 [4, 256, 256], P('dp', 'seq'), may hold values from 0 to 4
- donor_w: bfloat16 [1536, 384], P('head'), may hold values from -0.15625 to 0.15625
- acceptor_w: bfloat16 [1536, 384], P('head'), may hold values from -0.15625 to 0.15625
Outputs:
- grad_embed: bfloat16 [4, 1024, 1536], P('dp', 'seq', 'head')
- grad_donor_w: float32 [1536, 384], P('head', 'seq')
- grad_acceptor_w: float32 [1536, 384], P('head', 'seq')
The draws below stay inside these ranges and needn't reach their ends.
Inputs may be any that keep to these rules, and one draw needn't show every extreme that they name: `donor_pos`: slots k * 128 to (k + 1) * 128 - 1 belong to slab k: they hold one or more positions of k * 512 to (k + 1) * 512 - 1 first, then -1 in the remaining slots. Positions may repeat. `acceptor_pos`: as for donor_pos, drawn independently.
All inputs are finite; a program needn't handle non-finite values.
Results may differ from the reference program's by a relative error of at most 0.02.
Values may be sent and summed in bfloat16 or wider, within the bound.
No kernel may reach another device: no remote copies, remote signals or barrier semaphores. Data moves between devices by JAX's collectives and lax.ppermute only.
A program may use at most 64 MiB of HBM per device.

```python
import math
import jax
import jax.numpy as jnp
from jax import lax

CHANNELS = 1536
PROJ = 384
SLAB_ROWS = 512
SLAB_SITES = 128
SEQS = 4
LENGTH = 1024
SITES = 256
N_SEQ = 2
N_HEAD = 4


def draw_site_list(key, slab_sites, slab_rows, seqs, slabs):
    count_key, place_key = jax.random.split(key)
    counts = jax.random.randint(count_key, (seqs, slabs, 1), 1, slab_sites + 1)
    offsets = jax.random.randint(place_key, (seqs, slabs, slab_sites), 0, slab_rows)
    base = (jnp.arange(slabs, dtype=jnp.int32) * slab_rows)[None, :, None]
    slot = jnp.arange(slab_sites, dtype=jnp.int32)[None, None, :]
    placed = jnp.where(slot < counts, offsets + base, -1)
    return placed.reshape(seqs, slabs * slab_sites).astype(jnp.int32)


def draw_donor_pos(key, part):
    return draw_site_list(jax.random.fold_in(key, 11), SLAB_SITES, SLAB_ROWS, SEQS, SITES // SLAB_SITES)


def draw_acceptor_pos(key, part):
    return draw_site_list(jax.random.fold_in(key, 23), SLAB_SITES, SLAB_ROWS, SEQS, SITES // SLAB_SITES)


def level_of(own_key, shape, cuts, least, top_value):
    factor_of, own = 1.0, jax.random.fold_in(own_key, 6)
    for axis_at, blocks in cuts:
        steps = jnp.exp(jax.random.uniform(jax.random.fold_in(own, axis_at), (blocks,), jnp.float32, least / len(cuts), top_value / len(cuts)))
        factor_of = factor_of * jnp.repeat(steps, shape[axis_at] // blocks).reshape([-1 if axis == axis_at else 1 for axis in range(len(shape))])
    return factor_of


def centred(key, dims, deviation, most, cuts=(), held_as=jnp.bfloat16):
    array = deviation * jax.random.normal(key, dims, jnp.float32)
    if cuts:
        array = array * level_of(key, dims, cuts, -0.22, 0.18)
    return jnp.clip(array, -most, most).astype(held_as)


def setup_inputs(seed: int = 0) -> dict:
    seeds = jax.random.split(jax.random.key(seed), 7)
    embed = centred(seeds[0], (SEQS, LENGTH, CHANNELS), 1.0, 6.0, ((0, 4), (1, 2), (2, 4)))
    donor_pos = draw_donor_pos(jax.random.fold_in(seeds[6], 71), 0)
    acceptor_pos = draw_acceptor_pos(jax.random.fold_in(seeds[6], 71), 0)
    target = jnp.clip(4.0 * jax.random.uniform(seeds[3], (SEQS, SITES, SITES), jnp.float32) ** level_of(seeds[3], (SEQS, SITES, SITES), ((0, 4), (1, 2)), -0.2, 0.2), 0.0, 4.0).astype(jnp.bfloat16)
    donor_w = centred(seeds[4], (CHANNELS, PROJ), CHANNELS ** -0.5, 0.15625, ((0, 4),))
    acceptor_w = centred(seeds[5], (CHANNELS, PROJ), CHANNELS ** -0.5, 0.15625, ((0, 4),))
    return {"embed": embed, "donor_pos": donor_pos, "acceptor_pos": acceptor_pos, "target": target, "donor_w": donor_w, "acceptor_w": acceptor_w}


def split_project(rows, weight):
    width = rows.shape[1] // N_HEAD
    total = jnp.zeros((rows.shape[0], weight.shape[1]), jnp.float32)
    for block in range(N_HEAD):
        part = jnp.dot(rows[:, block * width:(block + 1) * width], weight[block * width:(block + 1) * width], preferred_element_type=jnp.float32)
        rounded = lax.optimization_barrier(part.astype(jnp.bfloat16))
        total = total + rounded.astype(jnp.float32)
    return total.astype(jnp.bfloat16)

def one_sequence(embed_seq, donor_at, acceptor_at, target_seq, donor_w, acceptor_w):
    scale = 1.0 / math.sqrt(PROJ)
    donor_ok = donor_at >= 0
    acceptor_ok = acceptor_at >= 0
    donor_idx = jnp.maximum(donor_at, 0).astype(jnp.int32)
    acceptor_idx = jnp.maximum(acceptor_at, 0).astype(jnp.int32)
    nothing = jnp.zeros((), embed_seq.dtype)
    donor_rows = jnp.where(donor_ok[:, None], embed_seq[donor_idx], nothing)
    acceptor_rows = jnp.where(acceptor_ok[:, None], embed_seq[acceptor_idx], nothing)
    donor_feat = split_project(donor_rows, donor_w)
    acceptor_feat = split_project(acceptor_rows, acceptor_w)
    scores = jnp.dot(donor_feat, acceptor_feat.T, preferred_element_type=jnp.float32) * scale
    allowed = donor_ok[:, None] & (acceptor_at[None, :] > donor_at[:, None])
    rate = jax.nn.softplus(scores) + 1.0
    slope = jnp.where(allowed, (1.0 - target_seq.astype(jnp.float32) / rate) * jax.nn.sigmoid(scores), 0.0).astype(jnp.bfloat16)
    donor_grad = (jnp.dot(slope, acceptor_feat, preferred_element_type=jnp.float32) * scale).astype(jnp.bfloat16)
    blocks = N_SEQ * N_HEAD
    quarter = SLAB_SITES // N_HEAD

    def add_block(total, pair):
        term = jnp.dot(pair[0].T, pair[1], preferred_element_type=jnp.float32) * scale
        rounded = lax.optimization_barrier(term.astype(jnp.bfloat16))
        return (total + rounded.astype(jnp.float32), None)
    total, _ = lax.scan(add_block, jnp.zeros((SITES, PROJ), jnp.float32), (slope.reshape(blocks, quarter, SITES), donor_feat.reshape(blocks, quarter, PROJ)))
    acceptor_grad = total.astype(jnp.bfloat16)
    donor_site = jnp.dot(donor_grad, donor_w.T, preferred_element_type=jnp.float32)
    acceptor_site = jnp.dot(acceptor_grad, acceptor_w.T, preferred_element_type=jnp.float32)
    grad_rows = jnp.zeros((LENGTH, CHANNELS), jnp.float32)
    grad_rows = grad_rows.at[donor_idx].add(jnp.where(donor_ok[:, None], donor_site, 0.0))
    grad_rows = grad_rows.at[acceptor_idx].add(jnp.where(acceptor_ok[:, None], acceptor_site, 0.0))
    grad_dw = jnp.dot(donor_rows.T, donor_grad, preferred_element_type=jnp.float32)
    grad_aw = jnp.dot(acceptor_rows.T, acceptor_grad, preferred_element_type=jnp.float32)
    return (grad_rows.astype(jnp.bfloat16), grad_dw, grad_aw)

def reference(embed, donor_pos, acceptor_pos, target, donor_w, acceptor_w):

    def step(carry, item):
        grad_rows, grad_dw, grad_aw = one_sequence(item[0], item[1], item[2], item[3], donor_w, acceptor_w)
        return ((carry[0] + grad_dw, carry[1] + grad_aw), grad_rows)
    start = (jnp.zeros((CHANNELS, PROJ), jnp.float32), jnp.zeros((CHANNELS, PROJ), jnp.float32))
    totals, grad_embed = lax.scan(step, start, (embed, donor_pos, acceptor_pos, target))
    return (grad_embed, totals[0], totals[1])
```

```python
import math

import jax
import jax.numpy as jnp
from jax import lax
from jax.sharding import PartitionSpec as P


def site_match(positions, slab_rows, slab_index):
    local_pos = positions - slab_index * slab_rows
    return local_pos[:, :, None] == jnp.arange(slab_rows, dtype=jnp.int32)[None, None, :]


def pair_slope(scores, target, allowed):
    rate = jax.nn.softplus(scores) + 1.0
    return jnp.where(
        allowed, (1.0 - target.astype(jnp.float32) / rate) * jax.nn.sigmoid(scores), 0.0
    ).astype(jnp.bfloat16)


def place_rows(match_bf, values):
    upper = values.astype(jnp.bfloat16)
    lower = (values - upper.astype(jnp.float32)).astype(jnp.bfloat16)
    placed = jnp.einsum("bnr,bnc->brc", match_bf, upper, preferred_element_type=jnp.float32)
    return placed + jnp.einsum("bnr,bnc->brc", match_bf, lower, preferred_element_type=jnp.float32)


def shards(embed, donor_pos, acceptor_pos, target, donor_w, acceptor_w):
    batch, slab_rows, _ = embed.shape
    slab_sites = donor_pos.shape[1]
    width = donor_w.shape[1]
    scale = 1.0 / math.sqrt(width)
    n_seq = lax.axis_size("seq")
    n_head = lax.axis_size("head")
    slab = lax.axis_index("seq")
    sites = slab_sites * n_seq

    target_all = lax.all_gather(target, "seq", axis=1, tiled=True)

    donor_match = site_match(donor_pos, slab_rows, slab).astype(jnp.bfloat16)
    acceptor_match = site_match(acceptor_pos, slab_rows, slab).astype(jnp.bfloat16)
    donor_rows = jnp.einsum(
        "bnr,brc->bnc", donor_match, embed, preferred_element_type=jnp.float32
    ).astype(jnp.bfloat16)
    acceptor_rows = jnp.einsum(
        "bnr,brc->bnc", acceptor_match, embed, preferred_element_type=jnp.float32
    ).astype(jnp.bfloat16)
    donor_part = jnp.einsum(
        "bnc,cp->bnp", donor_rows, donor_w, preferred_element_type=jnp.float32
    ).astype(jnp.bfloat16)
    acceptor_part = jnp.einsum(
        "bnc,cp->bnp", acceptor_rows, acceptor_w, preferred_element_type=jnp.float32
    ).astype(jnp.bfloat16)

    assert slab_sites <= width
    flags = jnp.zeros((batch, 8, width), jnp.bfloat16)
    flags = flags.at[:, 0, :slab_sites].set((donor_pos >= 0).astype(jnp.bfloat16))
    flags = flags.at[:, 1, :slab_sites].set((acceptor_pos >= 0).astype(jnp.bfloat16))
    packed = jnp.concatenate([donor_part, acceptor_part, flags], axis=1)
    gathered = lax.all_gather(packed, ("seq", "head"), axis=1, tiled=False)
    gathered = gathered.reshape(batch, n_seq, n_head, 2 * slab_sites + 8, width)

    donor_total = jnp.zeros((batch, n_seq, slab_sites, width), jnp.float32)
    acceptor_total = jnp.zeros((batch, n_seq, slab_sites, width), jnp.float32)
    for h in range(n_head):
        donor_total = donor_total + gathered[:, :, h, :slab_sites].astype(jnp.float32)
        acceptor_total = acceptor_total + gathered[:, :, h, slab_sites : 2 * slab_sites].astype(
            jnp.float32
        )
    donor_feat_all = donor_total.astype(jnp.bfloat16).reshape(batch, sites, width)
    acceptor_feat_all = acceptor_total.astype(jnp.bfloat16).reshape(batch, sites, width)
    donor_ok_all = (gathered[:, :, 0, 2 * slab_sites, :slab_sites] > 0).reshape(batch, sites)
    acceptor_ok_all = (gathered[:, :, 0, 2 * slab_sites + 1, :slab_sites] > 0).reshape(batch, sites)

    site_slab = jnp.arange(sites, dtype=jnp.int32) // slab_sites
    big = jnp.int32(1 << 30)
    acceptor_tiled = jnp.tile(acceptor_pos, (1, n_seq))
    acceptor_eff = jnp.where(
        site_slab[None, :] == slab,
        acceptor_tiled,
        jnp.where(
            (site_slab[None, :] > slab) & acceptor_ok_all, (slab + 1) * slab_rows, -1
        ),
    )
    donor_tiled = jnp.tile(donor_pos, (1, n_seq))
    donor_eff = jnp.where(
        site_slab[None, :] == slab,
        donor_tiled,
        jnp.where(
            site_slab[None, :] > slab,
            big,
            jnp.where(donor_ok_all, slab * slab_rows - 1, -1),
        ),
    )

    donor_feat = lax.dynamic_slice_in_dim(donor_feat_all, slab * slab_sites, slab_sites, 1)
    acceptor_feat = lax.dynamic_slice_in_dim(acceptor_feat_all, slab * slab_sites, slab_sites, 1)

    scores_row = (
        jnp.einsum("bip,bjp->bij", donor_feat, acceptor_feat_all, preferred_element_type=jnp.float32)
        * scale
    )
    allowed_row = (donor_pos[:, :, None] >= 0) & (acceptor_eff[:, None, :] > donor_pos[:, :, None])
    slope_row = pair_slope(scores_row, target, allowed_row)
    donor_grad = (
        jnp.einsum("bij,bjp->bip", slope_row, acceptor_feat_all, preferred_element_type=jnp.float32)
        * scale
    ).astype(jnp.bfloat16)

    target_col = lax.dynamic_slice_in_dim(target_all, slab * slab_sites, slab_sites, 2)
    scores_col = (
        jnp.einsum("bip,bjp->bij", donor_feat_all, acceptor_feat, preferred_element_type=jnp.float32)
        * scale
    )
    allowed_col = (donor_eff[:, :, None] >= 0) & (acceptor_pos[:, None, :] > donor_eff[:, :, None])
    slope_col = pair_slope(scores_col, target_col, allowed_col)
    acceptor_grad = (
        jnp.einsum("bij,bip->bjp", slope_col, donor_feat_all, preferred_element_type=jnp.float32)
        * scale
    ).astype(jnp.bfloat16)

    donor_site = jnp.einsum("bnp,cp->bnc", donor_grad, donor_w, preferred_element_type=jnp.float32)
    acceptor_site = jnp.einsum(
        "bnp,cp->bnc", acceptor_grad, acceptor_w, preferred_element_type=jnp.float32
    )
    row_grad = place_rows(donor_match, donor_site) + place_rows(acceptor_match, acceptor_site)

    local_dw = jnp.einsum("bnc,bnp->cp", donor_rows, donor_grad, preferred_element_type=jnp.float32)
    local_aw = jnp.einsum(
        "bnc,bnp->cp", acceptor_rows, acceptor_grad, preferred_element_type=jnp.float32
    )
    summed = lax.psum(jnp.stack([local_dw, local_aw]).astype(jnp.bfloat16), ("dp", "seq"))
    part = width // n_seq
    mine = lax.dynamic_slice_in_dim(summed, slab * part, part, 2).astype(jnp.float32)
    return (row_grad.astype(jnp.bfloat16), mine[0], mine[1])


def solution(mesh):
    in_specs = (
        P("dp", "seq", "head"),
        P("dp", "seq"),
        P("dp", "seq"),
        P("dp", "seq", None),
        P("head", None),
        P("head", None),
    )
    out_specs = (P("dp", "seq", "head"), P("head", "seq"), P("head", "seq"))
    return jax.shard_map(shards, mesh=mesh, in_specs=in_specs, out_specs=out_specs, check_vma=False)
```

```python
import math

import jax
import jax.numpy as jnp
from jax import lax
from jax.sharding import PartitionSpec as P


def site_match(positions, slab_rows, slab_index):
    local_pos = positions - slab_index * slab_rows
    return local_pos[:, :, None] == jnp.arange(slab_rows, dtype=jnp.int32)[None, None, :]


def pair_slope(scores, target, allowed):
    rate = jax.nn.softplus(scores) + 1.0
    return jnp.where(
        allowed, (1.0 - target.astype(jnp.float32) / rate) * jax.nn.sigmoid(scores), 0.0
    ).astype(jnp.bfloat16)


def place_rows(match_bf, values):
    upper = values.astype(jnp.bfloat16)
    lower = (values - upper.astype(jnp.float32)).astype(jnp.bfloat16)
    placed = jnp.einsum("bnr,bnc->brc", match_bf, upper, preferred_element_type=jnp.float32)
    return placed + jnp.einsum("bnr,bnc->brc", match_bf, lower, preferred_element_type=jnp.float32)


def gather_by_permute(x, axes, count, me):
    pieces = [x]
    for k in range(1, count):
        perm = [(i, (i + k) % count) for i in range(count)]
        pieces.append(lax.ppermute(x, axes, perm))
    by_offset = jnp.stack(pieces)
    order = (me - jnp.arange(count, dtype=jnp.int32)) % count
    return jnp.take(by_offset, order, axis=0)


def shards(embed, donor_pos, acceptor_pos, target, donor_w, acceptor_w):
    batch, slab_rows, _ = embed.shape
    slab_sites = donor_pos.shape[1]
    width = donor_w.shape[1]
    scale = 1.0 / math.sqrt(width)
    n_seq = lax.axis_size("seq")
    n_head = lax.axis_size("head")
    slab = lax.axis_index("seq")
    sites = slab_sites * n_seq

    target_all = gather_by_permute(target, ("seq",), n_seq, slab)
    target_all = jnp.moveaxis(target_all, 0, 1).reshape(batch, sites, target.shape[2])

    donor_match = site_match(donor_pos, slab_rows, slab).astype(jnp.bfloat16)
    acceptor_match = site_match(acceptor_pos, slab_rows, slab).astype(jnp.bfloat16)
    donor_rows = jnp.einsum(
        "bnr,brc->bnc", donor_match, embed, preferred_element_type=jnp.float32
    ).astype(jnp.bfloat16)
    acceptor_rows = jnp.einsum(
        "bnr,brc->bnc", acceptor_match, embed, preferred_element_type=jnp.float32
    ).astype(jnp.bfloat16)
    donor_part = jnp.einsum(
        "bnc,cp->bnp", donor_rows, donor_w, preferred_element_type=jnp.float32
    ).astype(jnp.bfloat16)
    acceptor_part = jnp.einsum(
        "bnc,cp->bnp", acceptor_rows, acceptor_w, preferred_element_type=jnp.float32
    ).astype(jnp.bfloat16)

    assert slab_sites <= width
    flags = jnp.zeros((batch, 8, width), jnp.bfloat16)
    flags = flags.at[:, 0, :slab_sites].set((donor_pos >= 0).astype(jnp.bfloat16))
    flags = flags.at[:, 1, :slab_sites].set((acceptor_pos >= 0).astype(jnp.bfloat16))
    packed = jnp.concatenate([donor_part, acceptor_part, flags], axis=1)
    me = slab * n_head + lax.axis_index("head")
    gathered = gather_by_permute(packed, ("seq", "head"), n_seq * n_head, me)
    gathered = jnp.moveaxis(gathered, 0, 1).reshape(batch, n_seq, n_head, 2 * slab_sites + 8, width)

    donor_total = jnp.zeros((batch, n_seq, slab_sites, width), jnp.float32)
    acceptor_total = jnp.zeros((batch, n_seq, slab_sites, width), jnp.float32)
    for h in range(n_head):
        donor_total = donor_total + gathered[:, :, h, :slab_sites].astype(jnp.float32)
        acceptor_total = acceptor_total + gathered[:, :, h, slab_sites : 2 * slab_sites].astype(
            jnp.float32
        )
    donor_feat_all = donor_total.astype(jnp.bfloat16).reshape(batch, sites, width)
    acceptor_feat_all = acceptor_total.astype(jnp.bfloat16).reshape(batch, sites, width)
    donor_ok_all = (gathered[:, :, 0, 2 * slab_sites, :slab_sites] > 0).reshape(batch, sites)
    acceptor_ok_all = (gathered[:, :, 0, 2 * slab_sites + 1, :slab_sites] > 0).reshape(batch, sites)

    site_slab = jnp.arange(sites, dtype=jnp.int32) // slab_sites
    big = jnp.int32(1 << 30)
    acceptor_tiled = jnp.tile(acceptor_pos, (1, n_seq))
    acceptor_eff = jnp.where(
        site_slab[None, :] == slab,
        acceptor_tiled,
        jnp.where(
            (site_slab[None, :] > slab) & acceptor_ok_all, (slab + 1) * slab_rows, -1
        ),
    )
    donor_tiled = jnp.tile(donor_pos, (1, n_seq))
    donor_eff = jnp.where(
        site_slab[None, :] == slab,
        donor_tiled,
        jnp.where(
            site_slab[None, :] > slab,
            big,
            jnp.where(donor_ok_all, slab * slab_rows - 1, -1),
        ),
    )

    donor_feat = lax.dynamic_slice_in_dim(donor_feat_all, slab * slab_sites, slab_sites, 1)
    acceptor_feat = lax.dynamic_slice_in_dim(acceptor_feat_all, slab * slab_sites, slab_sites, 1)

    scores_row = (
        jnp.einsum("bip,bjp->bij", donor_feat, acceptor_feat_all, preferred_element_type=jnp.float32)
        * scale
    )
    allowed_row = (donor_pos[:, :, None] >= 0) & (acceptor_eff[:, None, :] > donor_pos[:, :, None])
    slope_row = pair_slope(scores_row, target, allowed_row)
    donor_grad = (
        jnp.einsum("bij,bjp->bip", slope_row, acceptor_feat_all, preferred_element_type=jnp.float32)
        * scale
    ).astype(jnp.bfloat16)

    target_col = lax.dynamic_slice_in_dim(target_all, slab * slab_sites, slab_sites, 2)
    scores_col = (
        jnp.einsum("bip,bjp->bij", donor_feat_all, acceptor_feat, preferred_element_type=jnp.float32)
        * scale
    )
    allowed_col = (donor_eff[:, :, None] >= 0) & (acceptor_pos[:, None, :] > donor_eff[:, :, None])
    slope_col = pair_slope(scores_col, target_col, allowed_col)
    acceptor_grad = (
        jnp.einsum("bij,bip->bjp", slope_col, donor_feat_all, preferred_element_type=jnp.float32)
        * scale
    ).astype(jnp.bfloat16)

    donor_site = jnp.einsum("bnp,cp->bnc", donor_grad, donor_w, preferred_element_type=jnp.float32)
    acceptor_site = jnp.einsum(
        "bnp,cp->bnc", acceptor_grad, acceptor_w, preferred_element_type=jnp.float32
    )
    row_grad = place_rows(donor_match, donor_site) + place_rows(acceptor_match, acceptor_site)

    local_dw = jnp.einsum("bnc,bnp->cp", donor_rows, donor_grad, preferred_element_type=jnp.float32)
    local_aw = jnp.einsum(
        "bnc,bnp->cp", acceptor_rows, acceptor_grad, preferred_element_type=jnp.float32
    )
    part = width // n_seq
    blocks = jnp.stack([local_dw, local_aw]).astype(jnp.bfloat16)
    mine = lax.dynamic_slice_in_dim(blocks, slab * part, part, 2).astype(jnp.float32)
    for k in range(1, n_seq):
        dest = (slab + k) % n_seq
        outgoing = lax.dynamic_slice_in_dim(blocks, dest * part, part, 2)
        perm = [(i, (i + k) % n_seq) for i in range(n_seq)]
        mine = mine + lax.ppermute(outgoing, "seq", perm).astype(jnp.float32)
    n_dp = lax.axis_size("dp")
    assert n_dp & (n_dp - 1) == 0
    bit = 1
    while bit < n_dp:
        held = mine.astype(jnp.bfloat16)
        perm = [(i, i ^ bit) for i in range(n_dp)]
        mine = held.astype(jnp.float32) + lax.ppermute(held, "dp", perm).astype(jnp.float32)
        bit *= 2
    return (row_grad.astype(jnp.bfloat16), mine[0], mine[1])


def solution(mesh):
    in_specs = (
        P("dp", "seq", "head"),
        P("dp", "seq"),
        P("dp", "seq"),
        P("dp", "seq", None),
        P("head", None),
        P("head", None),
    )
    out_specs = (P("dp", "seq", "head"), P("head", "seq"), P("head", "seq"))
    return jax.shard_map(shards, mesh=mesh, in_specs=in_specs, out_specs=out_specs, check_vma=False)
```

```python
import math

import jax
import jax.numpy as jnp
from jax import lax
from jax.sharding import PartitionSpec as P


def site_match(positions, slab_rows, slab_index):
    local_pos = positions - slab_index * slab_rows
    return local_pos[:, :, None] == jnp.arange(slab_rows, dtype=jnp.int32)[None, None, :]


def pair_slope(scores, target, allowed):
    rate = jax.nn.softplus(scores) + 1.0
    return jnp.where(
        allowed, (1.0 - target.astype(jnp.float32) / rate) * jax.nn.sigmoid(scores), 0.0
    ).astype(jnp.bfloat16)


def place_rows(match_bf, values):
    upper = values.astype(jnp.bfloat16)
    lower = (values - upper.astype(jnp.float32)).astype(jnp.bfloat16)
    placed = jnp.einsum("bnr,bnc->brc", match_bf, upper, preferred_element_type=jnp.float32)
    return placed + jnp.einsum("bnr,bnc->brc", match_bf, lower, preferred_element_type=jnp.float32)


def gather_by_permute(x, axes, count, me):
    pieces = [x]
    for k in range(1, count):
        perm = [(i, (i + k) % count) for i in range(count)]
        pieces.append(lax.ppermute(x, axes, perm))
    by_offset = jnp.stack(pieces)
    order = (me - jnp.arange(count, dtype=jnp.int32)) % count
    return jnp.take(by_offset, order, axis=0)


def shards(embed, donor_pos, acceptor_pos, target, donor_w, acceptor_w):
    batch, slab_rows, _ = embed.shape
    slab_sites = donor_pos.shape[1]
    width = donor_w.shape[1]
    scale = 1.0 / math.sqrt(width)
    n_seq = lax.axis_size("seq")
    n_head = lax.axis_size("head")
    slab = lax.axis_index("seq")
    sites = slab_sites * n_seq

    head = lax.axis_index("head")
    me = slab * n_head + head

    target_col = jnp.zeros((batch, sites, slab_sites), target.dtype)
    own_cols = lax.dynamic_slice_in_dim(target, slab * slab_sites, slab_sites, 2)
    target_col = lax.dynamic_update_slice_in_dim(target_col, own_cols, slab * slab_sites, 1)
    for k in range(1, n_seq):
        outgoing = lax.dynamic_slice_in_dim(
            target, jnp.minimum(slab + k, n_seq - 1) * slab_sites, slab_sites, 2
        )
        perm = [(i, i + k) for i in range(n_seq - k)]
        arrived = lax.ppermute(outgoing, "seq", perm)
        source = jnp.maximum(slab - k, 0)
        placed = lax.dynamic_update_slice_in_dim(target_col, arrived, source * slab_sites, 1)
        target_col = jnp.where(slab >= k, placed, target_col)

    donor_match = site_match(donor_pos, slab_rows, slab).astype(jnp.bfloat16)
    acceptor_match = site_match(acceptor_pos, slab_rows, slab).astype(jnp.bfloat16)
    donor_rows = jnp.einsum(
        "bnr,brc->bnc", donor_match, embed, preferred_element_type=jnp.float32
    ).astype(jnp.bfloat16)
    acceptor_rows = jnp.einsum(
        "bnr,brc->bnc", acceptor_match, embed, preferred_element_type=jnp.float32
    ).astype(jnp.bfloat16)
    donor_part = jnp.einsum(
        "bnc,cp->bnp", donor_rows, donor_w, preferred_element_type=jnp.float32
    ).astype(jnp.bfloat16)
    acceptor_part = jnp.einsum(
        "bnc,cp->bnp", acceptor_rows, acceptor_w, preferred_element_type=jnp.float32
    ).astype(jnp.bfloat16)

    both = 2 * slab_sites
    assert both % n_head == 0
    quarter = both // n_head
    parts = jnp.concatenate([donor_part, acceptor_part], axis=1)
    pieces = [lax.dynamic_slice_in_dim(parts, head * quarter, quarter, 1)]
    for k in range(1, n_head):
        outgoing = lax.dynamic_slice_in_dim(parts, ((head + k) % n_head) * quarter, quarter, 1)
        perm = [(i, (i + k) % n_head) for i in range(n_head)]
        pieces.append(lax.ppermute(outgoing, "head", perm))
    by_offset = jnp.stack(pieces)
    by_head = jnp.take(by_offset, (head - jnp.arange(n_head, dtype=jnp.int32)) % n_head, axis=0)
    total = jnp.zeros((batch, quarter, width), jnp.float32)
    for h in range(n_head):
        total = total + by_head[h].astype(jnp.float32)
    feat_quarter = total.astype(jnp.bfloat16)

    assert slab_sites <= width
    flags = jnp.zeros((batch, 8, width), jnp.bfloat16)
    flags = flags.at[:, 0, :slab_sites].set((donor_pos >= 0).astype(jnp.bfloat16))
    flags = flags.at[:, 1, :slab_sites].set((acceptor_pos >= 0).astype(jnp.bfloat16))
    packed = jnp.concatenate([feat_quarter, flags], axis=1)
    gathered = gather_by_permute(packed, ("seq", "head"), n_seq * n_head, me)
    gathered = jnp.moveaxis(gathered, 0, 1).reshape(batch, n_seq, n_head, quarter + 8, width)
    feats = gathered[:, :, :, :quarter].reshape(batch, n_seq, both, width)
    donor_feat_all = feats[:, :, :slab_sites].reshape(batch, sites, width)
    acceptor_feat_all = feats[:, :, slab_sites:].reshape(batch, sites, width)
    donor_ok_all = (gathered[:, :, 0, quarter, :slab_sites] > 0).reshape(batch, sites)
    acceptor_ok_all = (gathered[:, :, 0, quarter + 1, :slab_sites] > 0).reshape(batch, sites)

    site_slab = jnp.arange(sites, dtype=jnp.int32) // slab_sites
    big = jnp.int32(1 << 30)
    acceptor_tiled = jnp.tile(acceptor_pos, (1, n_seq))
    acceptor_eff = jnp.where(
        site_slab[None, :] == slab,
        acceptor_tiled,
        jnp.where(
            (site_slab[None, :] > slab) & acceptor_ok_all, (slab + 1) * slab_rows, -1
        ),
    )
    donor_tiled = jnp.tile(donor_pos, (1, n_seq))
    donor_eff = jnp.where(
        site_slab[None, :] == slab,
        donor_tiled,
        jnp.where(
            site_slab[None, :] > slab,
            big,
            jnp.where(donor_ok_all, slab * slab_rows - 1, -1),
        ),
    )

    donor_feat = lax.dynamic_slice_in_dim(donor_feat_all, slab * slab_sites, slab_sites, 1)
    acceptor_feat = lax.dynamic_slice_in_dim(acceptor_feat_all, slab * slab_sites, slab_sites, 1)

    scores_row = (
        jnp.einsum("bip,bjp->bij", donor_feat, acceptor_feat_all, preferred_element_type=jnp.float32)
        * scale
    )
    allowed_row = (donor_pos[:, :, None] >= 0) & (acceptor_eff[:, None, :] > donor_pos[:, :, None])
    slope_row = pair_slope(scores_row, target, allowed_row)
    donor_grad = (
        jnp.einsum("bij,bjp->bip", slope_row, acceptor_feat_all, preferred_element_type=jnp.float32)
        * scale
    ).astype(jnp.bfloat16)

    scores_col = (
        jnp.einsum("bip,bjp->bij", donor_feat_all, acceptor_feat, preferred_element_type=jnp.float32)
        * scale
    )
    allowed_col = (donor_eff[:, :, None] >= 0) & (acceptor_pos[:, None, :] > donor_eff[:, :, None])
    slope_col = pair_slope(scores_col, target_col, allowed_col)
    acceptor_grad = (
        jnp.einsum("bij,bip->bjp", slope_col, donor_feat_all, preferred_element_type=jnp.float32)
        * scale
    ).astype(jnp.bfloat16)

    donor_site = jnp.einsum("bnp,cp->bnc", donor_grad, donor_w, preferred_element_type=jnp.float32)
    acceptor_site = jnp.einsum(
        "bnp,cp->bnc", acceptor_grad, acceptor_w, preferred_element_type=jnp.float32
    )
    row_grad = place_rows(donor_match, donor_site) + place_rows(acceptor_match, acceptor_site)

    local_dw = jnp.einsum("bnc,bnp->cp", donor_rows, donor_grad, preferred_element_type=jnp.float32)
    local_aw = jnp.einsum(
        "bnc,bnp->cp", acceptor_rows, acceptor_grad, preferred_element_type=jnp.float32
    )
    n_dp = lax.axis_size("dp")
    assert n_dp & (n_dp - 1) == 0 and n_dp >= 2
    dp = lax.axis_index("dp")
    pair = dp % 2
    channels = local_dw.shape[0]
    half = channels // 2
    part = width // n_seq
    blocks = jnp.stack([local_dw, local_aw]).astype(jnp.bfloat16)
    mine = lax.dynamic_slice_in_dim(blocks, pair * half, half, 1).astype(jnp.float32)
    outgoing = lax.dynamic_slice_in_dim(blocks, (1 - pair) * half, half, 1)
    mine = mine + lax.ppermute(outgoing, "dp", [(i, i ^ 1) for i in range(n_dp)]).astype(jnp.float32)
    held = mine.astype(jnp.bfloat16)
    mine = lax.dynamic_slice_in_dim(held, slab * part, part, 2).astype(jnp.float32)
    for k in range(1, n_seq):
        outgoing = lax.dynamic_slice_in_dim(held, ((slab + k) % n_seq) * part, part, 2)
        perm = [(i, (i + k) % n_seq) for i in range(n_seq)]
        mine = mine + lax.ppermute(outgoing, "seq", perm).astype(jnp.float32)
    bit = 2
    while bit < n_dp:
        held = mine.astype(jnp.bfloat16)
        perm = [(i, i ^ bit) for i in range(n_dp)]
        mine = held.astype(jnp.float32) + lax.ppermute(held, "dp", perm).astype(jnp.float32)
        bit *= 2
    other = lax.ppermute(mine, "dp", [(i, i ^ 1) for i in range(n_dp)])
    mine = jnp.where(pair == 0, jnp.concatenate([mine, other], 1), jnp.concatenate([other, mine], 1))
    return (row_grad.astype(jnp.bfloat16), mine[0], mine[1])


def solution(mesh):
    in_specs = (
        P("dp", "seq", "head"),
        P("dp", "seq"),
        P("dp", "seq"),
        P("dp", "seq", None),
        P("head", None),
        P("head", None),
    )
    out_specs = (P("dp", "seq", "head"), P("head", "seq"), P("head", "seq"))
    return jax.shard_map(shards, mesh=mesh, in_specs=in_specs, out_specs=out_specs, check_vma=False)
```

```python
import math

import jax
import jax.numpy as jnp
from jax import lax
from jax.sharding import PartitionSpec as P


def site_match(positions, slab_rows, slab_index):
    local_pos = positions - slab_index * slab_rows
    return local_pos[:, :, None] == jnp.arange(slab_rows, dtype=jnp.int32)[None, None, :]


def pair_slope(scores, target, allowed):
    rate = jax.nn.softplus(scores) + 1.0
    return jnp.where(
        allowed, (1.0 - target.astype(jnp.float32) / rate) * jax.nn.sigmoid(scores), 0.0
    ).astype(jnp.bfloat16)


def place_rows(match_bf, values):
    upper = values.astype(jnp.bfloat16)
    lower = (values - upper.astype(jnp.float32)).astype(jnp.bfloat16)
    placed = jnp.einsum("bnr,bnc->brc", match_bf, upper, preferred_element_type=jnp.float32)
    return placed + jnp.einsum("bnr,bnc->brc", match_bf, lower, preferred_element_type=jnp.float32)


def gather_by_permute(x, axes, count, me):
    pieces = [x]
    for k in range(1, count):
        perm = [(i, (i + k) % count) for i in range(count)]
        pieces.append(lax.ppermute(x, axes, perm))
    by_offset = jnp.stack(pieces)
    order = (me - jnp.arange(count, dtype=jnp.int32)) % count
    return jnp.take(by_offset, order, axis=0)


def shards(embed, donor_pos, acceptor_pos, target, donor_w, acceptor_w):
    batch, slab_rows, _ = embed.shape
    slab_sites = donor_pos.shape[1]
    width = donor_w.shape[1]
    scale = 1.0 / math.sqrt(width)
    n_seq = lax.axis_size("seq")
    n_head = lax.axis_size("head")
    slab = lax.axis_index("seq")
    sites = slab_sites * n_seq

    head = lax.axis_index("head")
    me = slab * n_head + head

    target_col = jnp.zeros((batch, sites, slab_sites), target.dtype)
    own_cols = lax.dynamic_slice_in_dim(target, slab * slab_sites, slab_sites, 2)
    target_col = lax.dynamic_update_slice_in_dim(target_col, own_cols, slab * slab_sites, 1)
    for k in range(1, n_seq):
        outgoing = lax.dynamic_slice_in_dim(
            target, jnp.minimum(slab + k, n_seq - 1) * slab_sites, slab_sites, 2
        )
        perm = [(i, i + k) for i in range(n_seq - k)]
        arrived = lax.ppermute(outgoing, "seq", perm)
        source = jnp.maximum(slab - k, 0)
        placed = lax.dynamic_update_slice_in_dim(target_col, arrived, source * slab_sites, 1)
        target_col = jnp.where(slab >= k, placed, target_col)

    donor_match = site_match(donor_pos, slab_rows, slab).astype(jnp.bfloat16)
    acceptor_match = site_match(acceptor_pos, slab_rows, slab).astype(jnp.bfloat16)
    donor_rows = jnp.einsum(
        "bnr,brc->bnc", donor_match, embed, preferred_element_type=jnp.float32
    ).astype(jnp.bfloat16)
    acceptor_rows = jnp.einsum(
        "bnr,brc->bnc", acceptor_match, embed, preferred_element_type=jnp.float32
    ).astype(jnp.bfloat16)
    donor_part = jnp.einsum(
        "bnc,cp->bnp", donor_rows, donor_w, preferred_element_type=jnp.float32
    ).astype(jnp.bfloat16)
    acceptor_part = jnp.einsum(
        "bnc,cp->bnp", acceptor_rows, acceptor_w, preferred_element_type=jnp.float32
    ).astype(jnp.bfloat16)

    both = 2 * slab_sites
    assert both % n_head == 0
    quarter = both // n_head
    parts = jnp.concatenate([donor_part, acceptor_part], axis=1)
    by_head = lax.all_to_all(
        parts.reshape(batch, n_head, quarter, width), "head", 1, 1, tiled=False
    )
    by_head = jnp.moveaxis(by_head, 1, 0)
    total = jnp.zeros((batch, quarter, width), jnp.float32)
    for h in range(n_head):
        total = total + by_head[h].astype(jnp.float32)
    feat_quarter = total.astype(jnp.bfloat16)

    assert slab_sites <= width
    flags = jnp.zeros((batch, 8, width), jnp.bfloat16)
    flags = flags.at[:, 0, :slab_sites].set((donor_pos >= 0).astype(jnp.bfloat16))
    flags = flags.at[:, 1, :slab_sites].set((acceptor_pos >= 0).astype(jnp.bfloat16))
    packed = jnp.concatenate([feat_quarter, flags], axis=1)
    count = n_seq * n_head
    copies = jnp.broadcast_to(packed[:, None], (batch, count) + packed.shape[1:])
    gathered = lax.all_to_all(copies, ("seq", "head"), 1, 1, tiled=False)
    gathered = gathered.reshape(batch, n_seq, n_head, quarter + 8, width)
    feats = gathered[:, :, :, :quarter].reshape(batch, n_seq, both, width)
    donor_feat_all = feats[:, :, :slab_sites].reshape(batch, sites, width)
    acceptor_feat_all = feats[:, :, slab_sites:].reshape(batch, sites, width)
    donor_ok_all = (gathered[:, :, 0, quarter, :slab_sites] > 0).reshape(batch, sites)
    acceptor_ok_all = (gathered[:, :, 0, quarter + 1, :slab_sites] > 0).reshape(batch, sites)

    site_slab = jnp.arange(sites, dtype=jnp.int32) // slab_sites
    big = jnp.int32(1 << 30)
    acceptor_tiled = jnp.tile(acceptor_pos, (1, n_seq))
    acceptor_eff = jnp.where(
        site_slab[None, :] == slab,
        acceptor_tiled,
        jnp.where(
            (site_slab[None, :] > slab) & acceptor_ok_all, (slab + 1) * slab_rows, -1
        ),
    )
    donor_tiled = jnp.tile(donor_pos, (1, n_seq))
    donor_eff = jnp.where(
        site_slab[None, :] == slab,
        donor_tiled,
        jnp.where(
            site_slab[None, :] > slab,
            big,
            jnp.where(donor_ok_all, slab * slab_rows - 1, -1),
        ),
    )

    donor_feat = lax.dynamic_slice_in_dim(donor_feat_all, slab * slab_sites, slab_sites, 1)
    acceptor_feat = lax.dynamic_slice_in_dim(acceptor_feat_all, slab * slab_sites, slab_sites, 1)

    scores_row = (
        jnp.einsum("bip,bjp->bij", donor_feat, acceptor_feat_all, preferred_element_type=jnp.float32)
        * scale
    )
    allowed_row = (donor_pos[:, :, None] >= 0) & (acceptor_eff[:, None, :] > donor_pos[:, :, None])
    slope_row = pair_slope(scores_row, target, allowed_row)
    donor_grad = (
        jnp.einsum("bij,bjp->bip", slope_row, acceptor_feat_all, preferred_element_type=jnp.float32)
        * scale
    ).astype(jnp.bfloat16)

    scores_col = (
        jnp.einsum("bip,bjp->bij", donor_feat_all, acceptor_feat, preferred_element_type=jnp.float32)
        * scale
    )
    allowed_col = (donor_eff[:, :, None] >= 0) & (acceptor_pos[:, None, :] > donor_eff[:, :, None])
    slope_col = pair_slope(scores_col, target_col, allowed_col)
    acceptor_grad = (
        jnp.einsum("bij,bip->bjp", slope_col, donor_feat_all, preferred_element_type=jnp.float32)
        * scale
    ).astype(jnp.bfloat16)

    donor_site = jnp.einsum("bnp,cp->bnc", donor_grad, donor_w, preferred_element_type=jnp.float32)
    acceptor_site = jnp.einsum(
        "bnp,cp->bnc", acceptor_grad, acceptor_w, preferred_element_type=jnp.float32
    )
    row_grad = place_rows(donor_match, donor_site) + place_rows(acceptor_match, acceptor_site)

    local_dw = jnp.einsum("bnc,bnp->cp", donor_rows, donor_grad, preferred_element_type=jnp.float32)
    local_aw = jnp.einsum(
        "bnc,bnp->cp", acceptor_rows, acceptor_grad, preferred_element_type=jnp.float32
    )
    n_dp = lax.axis_size("dp")
    assert n_dp & (n_dp - 1) == 0 and n_dp >= 2
    dp = lax.axis_index("dp")
    pair = dp % 2
    channels = local_dw.shape[0]
    half = channels // 2
    part = width // n_seq
    blocks = jnp.stack([local_dw, local_aw]).astype(jnp.bfloat16)
    mine = lax.dynamic_slice_in_dim(blocks, pair * half, half, 1).astype(jnp.float32)
    outgoing = lax.dynamic_slice_in_dim(blocks, (1 - pair) * half, half, 1)
    mine = mine + lax.ppermute(outgoing, "dp", [(i, i ^ 1) for i in range(n_dp)]).astype(jnp.float32)
    held = mine.astype(jnp.bfloat16)
    mine = lax.dynamic_slice_in_dim(held, slab * part, part, 2).astype(jnp.float32)
    for k in range(1, n_seq):
        outgoing = lax.dynamic_slice_in_dim(held, ((slab + k) % n_seq) * part, part, 2)
        perm = [(i, (i + k) % n_seq) for i in range(n_seq)]
        mine = mine + lax.ppermute(outgoing, "seq", perm).astype(jnp.float32)
    bit = 2
    while bit < n_dp:
        held = mine.astype(jnp.bfloat16)
        perm = [(i, i ^ bit) for i in range(n_dp)]
        mine = held.astype(jnp.float32) + lax.ppermute(held, "dp", perm).astype(jnp.float32)
        bit *= 2
    other = lax.ppermute(mine, "dp", [(i, i ^ 1) for i in range(n_dp)])
    mine = jnp.where(pair == 0, jnp.concatenate([mine, other], 1), jnp.concatenate([other, mine], 1))
    return (row_grad.astype(jnp.bfloat16), mine[0], mine[1])


def solution(mesh):
    in_specs = (
        P("dp", "seq", "head"),
        P("dp", "seq"),
        P("dp", "seq"),
        P("dp", "seq", None),
        P("head", None),
        P("head", None),
    )
    out_specs = (P("dp", "seq", "head"), P("head", "seq"), P("head", "seq"))
    return jax.shard_map(shards, mesh=mesh, in_specs=in_specs, out_specs=out_specs, check_vma=False)
```

```python
import math

import jax
import jax.numpy as jnp
from jax import lax
from jax.experimental.layout import Layout, with_layout_constraint
from jax.sharding import PartitionSpec as P


def site_match(positions, slab_rows, slab_index):
    local_pos = positions - slab_index * slab_rows
    return local_pos[:, :, None] == jnp.arange(slab_rows, dtype=jnp.int32)[None, None, :]


def pair_slope(scores, target, allowed):
    rate = jax.nn.softplus(scores) + 1.0
    return jnp.where(
        allowed, (1.0 - target.astype(jnp.float32) / rate) * jax.nn.sigmoid(scores), 0.0
    ).astype(jnp.bfloat16)


def place_rows(match_bf, values):
    upper = values.astype(jnp.bfloat16)
    lower = (values - upper.astype(jnp.float32)).astype(jnp.bfloat16)
    placed = jnp.einsum("bnr,bnc->brc", match_bf, upper, preferred_element_type=jnp.float32)
    return placed + jnp.einsum("bnr,bnc->brc", match_bf, lower, preferred_element_type=jnp.float32)


def gather_by_permute(x, axes, count, me, keep=lambda i, j: True):
    pieces = [x]
    for k in range(1, count):
        perm = [(i, (i + k) % count) for i in range(count) if keep(i, (i + k) % count)]
        pieces.append(lax.ppermute(x, axes, perm))
    by_offset = jnp.stack(pieces)
    order = (me - jnp.arange(count, dtype=jnp.int32)) % count
    return jnp.take(by_offset, order, axis=0)


def shards(embed, donor_pos, acceptor_pos, target, donor_w, acceptor_w):
    batch, slab_rows, _ = embed.shape
    slab_sites = donor_pos.shape[1]
    width = donor_w.shape[1]
    scale = 1.0 / math.sqrt(width)
    n_seq = lax.axis_size("seq")
    n_head = lax.axis_size("head")
    slab = lax.axis_index("seq")
    sites = slab_sites * n_seq

    head = lax.axis_index("head")
    me = slab * n_head + head

    target_col = jnp.zeros((batch, sites, slab_sites), target.dtype)
    own_cols = lax.dynamic_slice_in_dim(target, slab * slab_sites, slab_sites, 2)
    target_col = lax.dynamic_update_slice_in_dim(target_col, own_cols, slab * slab_sites, 1)
    for k in range(1, n_seq):
        outgoing = lax.dynamic_slice_in_dim(
            target, jnp.minimum(slab + k, n_seq - 1) * slab_sites, slab_sites, 2
        )
        perm = [(i, i + k) for i in range(n_seq - k)]
        arrived = lax.ppermute(outgoing, "seq", perm)
        source = jnp.maximum(slab - k, 0)
        placed = lax.dynamic_update_slice_in_dim(target_col, arrived, source * slab_sites, 1)
        target_col = jnp.where(slab >= k, placed, target_col)

    donor_match = site_match(donor_pos, slab_rows, slab).astype(jnp.bfloat16)
    acceptor_match = site_match(acceptor_pos, slab_rows, slab).astype(jnp.bfloat16)
    donor_rows = jnp.einsum(
        "bnr,brc->bnc", donor_match, embed, preferred_element_type=jnp.float32
    ).astype(jnp.bfloat16)
    acceptor_rows = jnp.einsum(
        "bnr,brc->bnc", acceptor_match, embed, preferred_element_type=jnp.float32
    ).astype(jnp.bfloat16)
    donor_part = jnp.einsum(
        "bnc,cp->bnp", donor_rows, donor_w, preferred_element_type=jnp.float32
    ).astype(jnp.bfloat16)
    acceptor_part = jnp.einsum(
        "bnc,cp->bnp", acceptor_rows, acceptor_w, preferred_element_type=jnp.float32
    ).astype(jnp.bfloat16)

    both = 2 * slab_sites
    assert both % n_head == 0
    quarter = both // n_head
    parts = jnp.concatenate([donor_part, acceptor_part], axis=1)
    pieces = [lax.dynamic_slice_in_dim(parts, head * quarter, quarter, 1)]
    for k in range(1, n_head):
        outgoing = lax.dynamic_slice_in_dim(parts, ((head + k) % n_head) * quarter, quarter, 1)
        perm = [(i, (i + k) % n_head) for i in range(n_head)]
        pieces.append(lax.ppermute(outgoing, "head", perm))
    by_offset = jnp.stack(pieces)
    by_head = jnp.take(by_offset, (head - jnp.arange(n_head, dtype=jnp.int32)) % n_head, axis=0)
    total = jnp.zeros((batch, quarter, width), jnp.float32)
    for h in range(n_head):
        total = total + by_head[h].astype(jnp.float32)
    feat_quarter = total.astype(jnp.bfloat16)

    assert slab_sites <= width
    flags = jnp.zeros((batch, 8, width), jnp.bfloat16)
    flags = flags.at[:, 0, :slab_sites].set((donor_pos >= 0).astype(jnp.bfloat16))
    flags = flags.at[:, 1, :slab_sites].set((acceptor_pos >= 0).astype(jnp.bfloat16))
    packed = jnp.concatenate([feat_quarter, flags], axis=1)
    keep = lambda i, j: (
        i // n_head == j // n_head
        or (i // n_head < j // n_head and (i % n_head) * quarter < slab_sites)
        or (i // n_head > j // n_head and (i % n_head) * quarter >= slab_sites)
    )
    gathered = gather_by_permute(packed, ("seq", "head"), n_seq * n_head, me, keep)
    gathered = jnp.moveaxis(gathered, 0, 1).reshape(batch, n_seq, n_head, quarter + 8, width)
    feats = gathered[:, :, :, :quarter].reshape(batch, n_seq, both, width)
    donor_feat_all = feats[:, :, :slab_sites].reshape(batch, sites, width)
    acceptor_feat_all = feats[:, :, slab_sites:].reshape(batch, sites, width)
    donor_ok_all = (gathered[:, :, 0, quarter, :slab_sites] > 0).reshape(batch, sites)
    acceptor_ok_all = (gathered[:, :, n_head - 1, quarter + 1, :slab_sites] > 0).reshape(batch, sites)

    site_slab = jnp.arange(sites, dtype=jnp.int32) // slab_sites
    big = jnp.int32(1 << 30)
    acceptor_tiled = jnp.tile(acceptor_pos, (1, n_seq))
    acceptor_eff = jnp.where(
        site_slab[None, :] == slab,
        acceptor_tiled,
        jnp.where(
            (site_slab[None, :] > slab) & acceptor_ok_all, (slab + 1) * slab_rows, -1
        ),
    )
    donor_tiled = jnp.tile(donor_pos, (1, n_seq))
    donor_eff = jnp.where(
        site_slab[None, :] == slab,
        donor_tiled,
        jnp.where(
            site_slab[None, :] > slab,
            big,
            jnp.where(donor_ok_all, slab * slab_rows - 1, -1),
        ),
    )

    donor_feat = lax.dynamic_slice_in_dim(donor_feat_all, slab * slab_sites, slab_sites, 1)
    acceptor_feat = lax.dynamic_slice_in_dim(acceptor_feat_all, slab * slab_sites, slab_sites, 1)

    scores_row = (
        jnp.einsum("bip,bjp->bij", donor_feat, acceptor_feat_all, preferred_element_type=jnp.float32)
        * scale
    )
    allowed_row = (donor_pos[:, :, None] >= 0) & (acceptor_eff[:, None, :] > donor_pos[:, :, None])
    slope_row = pair_slope(scores_row, target, allowed_row)
    donor_grad = (
        jnp.einsum("bij,bjp->bip", slope_row, acceptor_feat_all, preferred_element_type=jnp.float32)
        * scale
    ).astype(jnp.bfloat16)

    scores_col = (
        jnp.einsum("bip,bjp->bij", donor_feat_all, acceptor_feat, preferred_element_type=jnp.float32)
        * scale
    )
    allowed_col = (donor_eff[:, :, None] >= 0) & (acceptor_pos[:, None, :] > donor_eff[:, :, None])
    slope_col = pair_slope(scores_col, target_col, allowed_col)
    acceptor_grad = (
        jnp.einsum("bij,bip->bjp", slope_col, donor_feat_all, preferred_element_type=jnp.float32)
        * scale
    ).astype(jnp.bfloat16)

    donor_site = jnp.einsum("bnp,cp->bnc", donor_grad, donor_w, preferred_element_type=jnp.float32)
    acceptor_site = jnp.einsum(
        "bnp,cp->bnc", acceptor_grad, acceptor_w, preferred_element_type=jnp.float32
    )
    row_grad = place_rows(donor_match, donor_site) + place_rows(acceptor_match, acceptor_site)

    local_dw = jnp.einsum("bnc,bnp->pc", donor_rows, donor_grad, preferred_element_type=jnp.float32)
    local_aw = jnp.einsum(
        "bnc,bnp->pc", acceptor_rows, acceptor_grad, preferred_element_type=jnp.float32
    )
    n_dp = lax.axis_size("dp")
    assert n_dp & (n_dp - 1) == 0 and n_dp >= 2
    dp = lax.axis_index("dp")
    pair = dp % 2
    channels = local_dw.shape[1]
    half = channels // 2
    part = width // n_seq
    blocks = jnp.stack([local_dw, local_aw]).astype(jnp.bfloat16)
    mine = lax.dynamic_slice_in_dim(blocks, pair * half, half, 2).astype(jnp.float32)
    outgoing = lax.dynamic_slice_in_dim(blocks, (1 - pair) * half, half, 2)
    mine = mine + lax.ppermute(outgoing, "dp", [(i, i ^ 1) for i in range(n_dp)]).astype(jnp.float32)
    held = mine.astype(jnp.bfloat16)
    mine = lax.dynamic_slice_in_dim(held, slab * part, part, 1).astype(jnp.float32)
    for k in range(1, n_seq):
        outgoing = lax.dynamic_slice_in_dim(held, ((slab + k) % n_seq) * part, part, 1)
        perm = [(i, (i + k) % n_seq) for i in range(n_seq)]
        mine = mine + lax.ppermute(outgoing, "seq", perm).astype(jnp.float32)
    bit = 2
    while bit < n_dp:
        held = mine.astype(jnp.bfloat16)
        perm = [(i, i ^ bit) for i in range(n_dp)]
        mine = held.astype(jnp.float32) + lax.ppermute(held, "dp", perm).astype(jnp.float32)
        bit *= 2
    other = lax.ppermute(mine, "dp", [(i, i ^ 1) for i in range(n_dp)])
    mine = jnp.where(pair == 0, jnp.concatenate([mine, other], 2), jnp.concatenate([other, mine], 2))
    mine = jnp.swapaxes(mine, 1, 2)
    column_major = Layout(major_to_minor=(1, 0))
    grad_dw = with_layout_constraint(mine[0], column_major)
    grad_aw = with_layout_constraint(mine[1], column_major)
    return (row_grad.astype(jnp.bfloat16), grad_dw, grad_aw)


def solution(mesh):
    in_specs = (
        P("dp", "seq", "head"),
        P("dp", "seq"),
        P("dp", "seq"),
        P("dp", "seq", None),
        P("head", None),
        P("head", None),
    )
    out_specs = (P("dp", "seq", "head"), P("head", "seq"), P("head", "seq"))
    return jax.shard_map(shards, mesh=mesh, in_specs=in_specs, out_specs=out_specs, check_vma=False)
```

```python
import math

import jax
import jax.numpy as jnp
from jax import lax
from jax.experimental.layout import Layout, with_layout_constraint
from jax.sharding import PartitionSpec as P


def site_match(positions, slab_rows, slab_index):
    local_pos = positions - slab_index * slab_rows
    return local_pos[:, :, None] == jnp.arange(slab_rows, dtype=jnp.int32)[None, None, :]


def pair_slope(scores, target, allowed):
    rate = jax.nn.softplus(scores) + 1.0
    return jnp.where(
        allowed, (1.0 - target.astype(jnp.float32) / rate) * jax.nn.sigmoid(scores), 0.0
    ).astype(jnp.bfloat16)


def place_rows(match_bf, values):
    upper = values.astype(jnp.bfloat16)
    lower = (values - upper.astype(jnp.float32)).astype(jnp.bfloat16)
    placed = jnp.einsum("bnr,bnc->brc", match_bf, upper, preferred_element_type=jnp.float32)
    return placed + jnp.einsum("bnr,bnc->brc", match_bf, lower, preferred_element_type=jnp.float32)


def gather_by_permute(x, axes, count, me):
    pieces = [x]
    for k in range(1, count):
        perm = [(i, (i + k) % count) for i in range(count)]
        pieces.append(lax.ppermute(x, axes, perm))
    by_offset = jnp.stack(pieces)
    order = (me - jnp.arange(count, dtype=jnp.int32)) % count
    return jnp.take(by_offset, order, axis=0)


def shards(embed, donor_pos, acceptor_pos, target, donor_w, acceptor_w):
    batch, slab_rows, _ = embed.shape
    slab_sites = donor_pos.shape[1]
    width = donor_w.shape[1]
    scale = 1.0 / math.sqrt(width)
    n_seq = lax.axis_size("seq")
    n_head = lax.axis_size("head")
    slab = lax.axis_index("seq")
    sites = slab_sites * n_seq

    head = lax.axis_index("head")
    me = slab * n_head + head

    target_col = jnp.zeros((batch, sites, slab_sites), target.dtype)
    own_cols = lax.dynamic_slice_in_dim(target, slab * slab_sites, slab_sites, 2)
    target_col = lax.dynamic_update_slice_in_dim(target_col, own_cols, slab * slab_sites, 1)
    for k in range(1, n_seq):
        outgoing = lax.dynamic_slice_in_dim(
            target, jnp.minimum(slab + k, n_seq - 1) * slab_sites, slab_sites, 2
        )
        perm = [(i, i + k) for i in range(n_seq - k)]
        arrived = lax.ppermute(outgoing, "seq", perm)
        source = jnp.maximum(slab - k, 0)
        placed = lax.dynamic_update_slice_in_dim(target_col, arrived, source * slab_sites, 1)
        target_col = jnp.where(slab >= k, placed, target_col)

    donor_match = site_match(donor_pos, slab_rows, slab).astype(jnp.bfloat16)
    acceptor_match = site_match(acceptor_pos, slab_rows, slab).astype(jnp.bfloat16)
    donor_rows = jnp.einsum(
        "bnr,brc->bnc", donor_match, embed, preferred_element_type=jnp.float32
    ).astype(jnp.bfloat16)
    acceptor_rows = jnp.einsum(
        "bnr,brc->bnc", acceptor_match, embed, preferred_element_type=jnp.float32
    ).astype(jnp.bfloat16)
    donor_part = jnp.einsum(
        "bnc,cp->bnp", donor_rows, donor_w, preferred_element_type=jnp.float32
    ).astype(jnp.bfloat16)
    acceptor_part = jnp.einsum(
        "bnc,cp->bnp", acceptor_rows, acceptor_w, preferred_element_type=jnp.float32
    ).astype(jnp.bfloat16)

    both = 2 * slab_sites
    assert both % n_head == 0
    quarter = both // n_head
    parts = jnp.concatenate([donor_part, acceptor_part], axis=1)
    pieces = [lax.dynamic_slice_in_dim(parts, head * quarter, quarter, 1)]
    for k in range(1, n_head):
        outgoing = lax.dynamic_slice_in_dim(parts, ((head + k) % n_head) * quarter, quarter, 1)
        perm = [(i, (i + k) % n_head) for i in range(n_head)]
        pieces.append(lax.ppermute(outgoing, "head", perm))
    by_offset = jnp.stack(pieces)
    by_head = jnp.take(by_offset, (head - jnp.arange(n_head, dtype=jnp.int32)) % n_head, axis=0)
    total = jnp.zeros((batch, quarter, width), jnp.float32)
    for h in range(n_head):
        total = total + by_head[h].astype(jnp.float32)
    feat_quarter = total.astype(jnp.bfloat16)

    slab_feats = gather_by_permute(feat_quarter, ("head",), n_head, head)
    slab_feats = jnp.moveaxis(slab_feats, 0, 1).reshape(batch, both, width)
    own_donor = slab_feats[:, :slab_sites]
    own_acceptor = slab_feats[:, slab_sites:]

    assert slab_sites <= width
    flags = jnp.zeros((batch, 8, width), jnp.bfloat16)
    flags = flags.at[:, 0, :slab_sites].set((donor_pos >= 0).astype(jnp.bfloat16))
    flags = flags.at[:, 1, :slab_sites].set((acceptor_pos >= 0).astype(jnp.bfloat16))
    donor_feat_all = jnp.zeros((batch, sites, width), jnp.bfloat16)
    acceptor_feat_all = jnp.zeros((batch, sites, width), jnp.bfloat16)
    donor_feat_all = lax.dynamic_update_slice_in_dim(donor_feat_all, own_donor, slab * slab_sites, 1)
    acceptor_feat_all = lax.dynamic_update_slice_in_dim(
        acceptor_feat_all, own_acceptor, slab * slab_sites, 1
    )
    donor_ok_all = jnp.zeros((batch, sites), jnp.bool_)
    acceptor_ok_all = jnp.zeros((batch, sites), jnp.bool_)
    for k in range(1, n_seq):
        sent = jnp.where(slab + k < n_seq, own_donor, own_acceptor)
        perm = [(i, (i + k) % n_seq) for i in range(n_seq)]
        arrived = lax.ppermute(jnp.concatenate([sent, flags], axis=1), "seq", perm)
        source = (slab - k) % n_seq
        earlier = slab >= k
        feat_in = arrived[:, :slab_sites]
        donor_feat_all = jnp.where(
            earlier,
            lax.dynamic_update_slice_in_dim(donor_feat_all, feat_in, source * slab_sites, 1),
            donor_feat_all,
        )
        acceptor_feat_all = jnp.where(
            earlier,
            acceptor_feat_all,
            lax.dynamic_update_slice_in_dim(acceptor_feat_all, feat_in, source * slab_sites, 1),
        )
        donor_in = arrived[:, slab_sites, :slab_sites] > 0
        acceptor_in = arrived[:, slab_sites + 1, :slab_sites] > 0
        donor_ok_all = jnp.where(
            earlier,
            lax.dynamic_update_slice_in_dim(donor_ok_all, donor_in, source * slab_sites, 1),
            donor_ok_all,
        )
        acceptor_ok_all = jnp.where(
            earlier,
            acceptor_ok_all,
            lax.dynamic_update_slice_in_dim(acceptor_ok_all, acceptor_in, source * slab_sites, 1),
        )

    site_slab = jnp.arange(sites, dtype=jnp.int32) // slab_sites
    big = jnp.int32(1 << 30)
    acceptor_tiled = jnp.tile(acceptor_pos, (1, n_seq))
    acceptor_eff = jnp.where(
        site_slab[None, :] == slab,
        acceptor_tiled,
        jnp.where(
            (site_slab[None, :] > slab) & acceptor_ok_all, (slab + 1) * slab_rows, -1
        ),
    )
    donor_tiled = jnp.tile(donor_pos, (1, n_seq))
    donor_eff = jnp.where(
        site_slab[None, :] == slab,
        donor_tiled,
        jnp.where(
            site_slab[None, :] > slab,
            big,
            jnp.where(donor_ok_all, slab * slab_rows - 1, -1),
        ),
    )

    donor_feat = own_donor
    acceptor_feat = own_acceptor

    scores_row = (
        jnp.einsum("bip,bjp->bij", donor_feat, acceptor_feat_all, preferred_element_type=jnp.float32)
        * scale
    )
    allowed_row = (donor_pos[:, :, None] >= 0) & (acceptor_eff[:, None, :] > donor_pos[:, :, None])
    slope_row = pair_slope(scores_row, target, allowed_row)
    donor_grad = (
        jnp.einsum("bij,bjp->bip", slope_row, acceptor_feat_all, preferred_element_type=jnp.float32)
        * scale
    ).astype(jnp.bfloat16)

    scores_col = (
        jnp.einsum("bip,bjp->bij", donor_feat_all, acceptor_feat, preferred_element_type=jnp.float32)
        * scale
    )
    allowed_col = (donor_eff[:, :, None] >= 0) & (acceptor_pos[:, None, :] > donor_eff[:, :, None])
    slope_col = pair_slope(scores_col, target_col, allowed_col)
    acceptor_grad = (
        jnp.einsum("bij,bip->bjp", slope_col, donor_feat_all, preferred_element_type=jnp.float32)
        * scale
    ).astype(jnp.bfloat16)

    donor_site = jnp.einsum("bnp,cp->bnc", donor_grad, donor_w, preferred_element_type=jnp.float32)
    acceptor_site = jnp.einsum(
        "bnp,cp->bnc", acceptor_grad, acceptor_w, preferred_element_type=jnp.float32
    )
    row_grad = place_rows(donor_match, donor_site) + place_rows(acceptor_match, acceptor_site)

    local_dw = jnp.einsum("bnc,bnp->pc", donor_rows, donor_grad, preferred_element_type=jnp.float32)
    local_aw = jnp.einsum(
        "bnc,bnp->pc", acceptor_rows, acceptor_grad, preferred_element_type=jnp.float32
    )
    n_dp = lax.axis_size("dp")
    assert n_dp & (n_dp - 1) == 0 and n_dp >= 2
    dp = lax.axis_index("dp")
    pair = dp % 2
    channels = local_dw.shape[1]
    half = channels // 2
    part = width // n_seq
    blocks = jnp.stack([local_dw, local_aw]).astype(jnp.bfloat16)
    mine = lax.dynamic_slice_in_dim(blocks, pair * half, half, 2).astype(jnp.float32)
    outgoing = lax.dynamic_slice_in_dim(blocks, (1 - pair) * half, half, 2)
    mine = mine + lax.ppermute(outgoing, "dp", [(i, i ^ 1) for i in range(n_dp)]).astype(jnp.float32)
    held = mine.astype(jnp.bfloat16)
    mine = lax.dynamic_slice_in_dim(held, slab * part, part, 1).astype(jnp.float32)
    for k in range(1, n_seq):
        outgoing = lax.dynamic_slice_in_dim(held, ((slab + k) % n_seq) * part, part, 1)
        perm = [(i, (i + k) % n_seq) for i in range(n_seq)]
        mine = mine + lax.ppermute(outgoing, "seq", perm).astype(jnp.float32)
    bit = 2
    while bit < n_dp:
        held = mine.astype(jnp.bfloat16)
        perm = [(i, i ^ bit) for i in range(n_dp)]
        mine = held.astype(jnp.float32) + lax.ppermute(held, "dp", perm).astype(jnp.float32)
        bit *= 2
    other = lax.ppermute(mine, "dp", [(i, i ^ 1) for i in range(n_dp)])
    mine = jnp.where(pair == 0, jnp.concatenate([mine, other], 2), jnp.concatenate([other, mine], 2))
    mine = jnp.swapaxes(mine, 1, 2)
    column_major = Layout(major_to_minor=(1, 0))
    grad_dw = with_layout_constraint(mine[0], column_major)
    grad_aw = with_layout_constraint(mine[1], column_major)
    return (row_grad.astype(jnp.bfloat16), grad_dw, grad_aw)


def solution(mesh):
    in_specs = (
        P("dp", "seq", "head"),
        P("dp", "seq"),
        P("dp", "seq"),
        P("dp", "seq", None),
        P("head", None),
        P("head", None),
    )
    out_specs = (P("dp", "seq", "head"), P("head", "seq"), P("head", "seq"))
    return jax.shard_map(shards, mesh=mesh, in_specs=in_specs, out_specs=out_specs, check_vma=False)
```

```python
import math

import jax
import jax.numpy as jnp
from jax import lax
from jax.experimental.layout import Layout, with_layout_constraint
from jax.sharding import PartitionSpec as P


def site_match(positions, slab_rows, slab_index):
    local_pos = positions - slab_index * slab_rows
    return local_pos[:, :, None] == jnp.arange(slab_rows, dtype=jnp.int32)[None, None, :]


def pair_slope(scores, target, allowed):
    rate = jax.nn.softplus(scores) + 1.0
    return jnp.where(
        allowed, (1.0 - target.astype(jnp.float32) / rate) * jax.nn.sigmoid(scores), 0.0
    ).astype(jnp.bfloat16)


def place_rows(match_bf, values):
    upper = values.astype(jnp.bfloat16)
    lower = (values - upper.astype(jnp.float32)).astype(jnp.bfloat16)
    placed = jnp.einsum("bnr,bnc->brc", match_bf, upper, preferred_element_type=jnp.float32)
    return placed + jnp.einsum("bnr,bnc->brc", match_bf, lower, preferred_element_type=jnp.float32)


def gather_by_permute(x, axes, count, me):
    pieces = [x]
    for k in range(1, count):
        perm = [(i, (i + k) % count) for i in range(count)]
        pieces.append(lax.ppermute(x, axes, perm))
    by_offset = jnp.stack(pieces)
    order = (me - jnp.arange(count, dtype=jnp.int32)) % count
    return jnp.take(by_offset, order, axis=0)


def shards(embed, donor_pos, acceptor_pos, target, donor_w, acceptor_w):
    batch, slab_rows, _ = embed.shape
    slab_sites = donor_pos.shape[1]
    width = donor_w.shape[1]
    scale = 1.0 / math.sqrt(width)
    n_seq = lax.axis_size("seq")
    n_head = lax.axis_size("head")
    slab = lax.axis_index("seq")
    sites = slab_sites * n_seq

    head = lax.axis_index("head")
    me = slab * n_head + head

    target_col = jnp.zeros((batch, sites, slab_sites), target.dtype)
    own_cols = lax.dynamic_slice_in_dim(target, slab * slab_sites, slab_sites, 2)
    target_col = lax.dynamic_update_slice_in_dim(target_col, own_cols, slab * slab_sites, 1)
    for k in range(1, n_seq):
        outgoing = lax.dynamic_slice_in_dim(
            target, jnp.minimum(slab + k, n_seq - 1) * slab_sites, slab_sites, 2
        )
        perm = [(i, i + k) for i in range(n_seq - k)]
        arrived = lax.ppermute(outgoing, "seq", perm)
        source = jnp.maximum(slab - k, 0)
        placed = lax.dynamic_update_slice_in_dim(target_col, arrived, source * slab_sites, 1)
        target_col = jnp.where(slab >= k, placed, target_col)

    donor_match = site_match(donor_pos, slab_rows, slab).astype(jnp.bfloat16)
    acceptor_match = site_match(acceptor_pos, slab_rows, slab).astype(jnp.bfloat16)
    donor_rows = jnp.einsum(
        "bnr,brc->bnc", donor_match, embed, preferred_element_type=jnp.float32
    ).astype(jnp.bfloat16)
    acceptor_rows = jnp.einsum(
        "bnr,brc->bnc", acceptor_match, embed, preferred_element_type=jnp.float32
    ).astype(jnp.bfloat16)
    donor_part = jnp.einsum(
        "bnc,cp->bnp", donor_rows, donor_w, preferred_element_type=jnp.float32
    ).astype(jnp.bfloat16)
    acceptor_part = jnp.einsum(
        "bnc,cp->bnp", acceptor_rows, acceptor_w, preferred_element_type=jnp.float32
    ).astype(jnp.bfloat16)

    both = 2 * slab_sites
    assert both % n_head == 0
    quarter = both // n_head
    parts = jnp.concatenate([donor_part, acceptor_part], axis=1)
    assert n_head & (n_head - 1) == 0
    pieces = [lax.dynamic_slice_in_dim(parts, head * quarter, quarter, 1)]
    for k in range(1, n_head):
        outgoing = lax.dynamic_slice_in_dim(parts, (head ^ k) * quarter, quarter, 1)
        pieces.append(lax.ppermute(outgoing, "head", [(i, i ^ k) for i in range(n_head)]))
    by_partner = jnp.stack(pieces)
    by_head = jnp.take(by_partner, head ^ jnp.arange(n_head, dtype=jnp.int32), axis=0)
    total = jnp.zeros((batch, quarter, width), jnp.float32)
    for h in range(n_head):
        total = total + by_head[h].astype(jnp.float32)
    feat_quarter = total.astype(jnp.bfloat16)

    pieces = [feat_quarter]
    for k in range(1, n_head):
        pieces.append(lax.ppermute(feat_quarter, "head", [(i, i ^ k) for i in range(n_head)]))
    slab_feats = jnp.take(jnp.stack(pieces), head ^ jnp.arange(n_head, dtype=jnp.int32), axis=0)
    slab_feats = jnp.moveaxis(slab_feats, 0, 1).reshape(batch, both, width)
    own_donor = slab_feats[:, :slab_sites]
    own_acceptor = slab_feats[:, slab_sites:]

    assert slab_sites <= width
    flags = jnp.zeros((batch, 8, width), jnp.bfloat16)
    flags = flags.at[:, 0, :slab_sites].set((donor_pos >= 0).astype(jnp.bfloat16))
    flags = flags.at[:, 1, :slab_sites].set((acceptor_pos >= 0).astype(jnp.bfloat16))
    donor_feat_all = jnp.zeros((batch, sites, width), jnp.bfloat16)
    acceptor_feat_all = jnp.zeros((batch, sites, width), jnp.bfloat16)
    donor_feat_all = lax.dynamic_update_slice_in_dim(donor_feat_all, own_donor, slab * slab_sites, 1)
    acceptor_feat_all = lax.dynamic_update_slice_in_dim(
        acceptor_feat_all, own_acceptor, slab * slab_sites, 1
    )
    donor_ok_all = jnp.zeros((batch, sites), jnp.bool_)
    acceptor_ok_all = jnp.zeros((batch, sites), jnp.bool_)
    for k in range(1, n_seq):
        sent = jnp.where(slab + k < n_seq, own_donor, own_acceptor)
        perm = [(i, (i + k) % n_seq) for i in range(n_seq)]
        arrived = lax.ppermute(jnp.concatenate([sent, flags], axis=1), "seq", perm)
        source = (slab - k) % n_seq
        earlier = slab >= k
        feat_in = arrived[:, :slab_sites]
        donor_feat_all = jnp.where(
            earlier,
            lax.dynamic_update_slice_in_dim(donor_feat_all, feat_in, source * slab_sites, 1),
            donor_feat_all,
        )
        acceptor_feat_all = jnp.where(
            earlier,
            acceptor_feat_all,
            lax.dynamic_update_slice_in_dim(acceptor_feat_all, feat_in, source * slab_sites, 1),
        )
        donor_in = arrived[:, slab_sites, :slab_sites] > 0
        acceptor_in = arrived[:, slab_sites + 1, :slab_sites] > 0
        donor_ok_all = jnp.where(
            earlier,
            lax.dynamic_update_slice_in_dim(donor_ok_all, donor_in, source * slab_sites, 1),
            donor_ok_all,
        )
        acceptor_ok_all = jnp.where(
            earlier,
            acceptor_ok_all,
            lax.dynamic_update_slice_in_dim(acceptor_ok_all, acceptor_in, source * slab_sites, 1),
        )

    site_slab = jnp.arange(sites, dtype=jnp.int32) // slab_sites
    big = jnp.int32(1 << 30)
    acceptor_tiled = jnp.tile(acceptor_pos, (1, n_seq))
    acceptor_eff = jnp.where(
        site_slab[None, :] == slab,
        acceptor_tiled,
        jnp.where(
            (site_slab[None, :] > slab) & acceptor_ok_all, (slab + 1) * slab_rows, -1
        ),
    )
    donor_tiled = jnp.tile(donor_pos, (1, n_seq))
    donor_eff = jnp.where(
        site_slab[None, :] == slab,
        donor_tiled,
        jnp.where(
            site_slab[None, :] > slab,
            big,
            jnp.where(donor_ok_all, slab * slab_rows - 1, -1),
        ),
    )

    donor_feat = own_donor
    acceptor_feat = own_acceptor

    scores_row = (
        jnp.einsum("bip,bjp->bij", donor_feat, acceptor_feat_all, preferred_element_type=jnp.float32)
        * scale
    )
    allowed_row = (donor_pos[:, :, None] >= 0) & (acceptor_eff[:, None, :] > donor_pos[:, :, None])
    slope_row = pair_slope(scores_row, target, allowed_row)
    donor_grad = (
        jnp.einsum("bij,bjp->bip", slope_row, acceptor_feat_all, preferred_element_type=jnp.float32)
        * scale
    ).astype(jnp.bfloat16)

    scores_col = (
        jnp.einsum("bip,bjp->bij", donor_feat_all, acceptor_feat, preferred_element_type=jnp.float32)
        * scale
    )
    allowed_col = (donor_eff[:, :, None] >= 0) & (acceptor_pos[:, None, :] > donor_eff[:, :, None])
    slope_col = pair_slope(scores_col, target_col, allowed_col)
    acceptor_grad = (
        jnp.einsum("bij,bip->bjp", slope_col, donor_feat_all, preferred_element_type=jnp.float32)
        * scale
    ).astype(jnp.bfloat16)

    donor_site = jnp.einsum("bnp,cp->bnc", donor_grad, donor_w, preferred_element_type=jnp.float32)
    acceptor_site = jnp.einsum(
        "bnp,cp->bnc", acceptor_grad, acceptor_w, preferred_element_type=jnp.float32
    )
    row_grad = place_rows(donor_match, donor_site) + place_rows(acceptor_match, acceptor_site)

    local_dw = jnp.einsum("bnc,bnp->pc", donor_rows, donor_grad, preferred_element_type=jnp.float32)
    local_aw = jnp.einsum(
        "bnc,bnp->pc", acceptor_rows, acceptor_grad, preferred_element_type=jnp.float32
    )
    n_dp = lax.axis_size("dp")
    assert n_dp & (n_dp - 1) == 0 and n_dp >= 2
    dp = lax.axis_index("dp")
    pair = dp % 2
    channels = local_dw.shape[1]
    half = channels // 2
    part = width // n_seq
    blocks = jnp.stack([local_dw, local_aw]).astype(jnp.bfloat16)
    mine = lax.dynamic_slice_in_dim(blocks, pair * half, half, 2).astype(jnp.float32)
    outgoing = lax.dynamic_slice_in_dim(blocks, (1 - pair) * half, half, 2)
    mine = mine + lax.ppermute(outgoing, "dp", [(i, i ^ 1) for i in range(n_dp)]).astype(jnp.float32)
    held = mine.astype(jnp.bfloat16)
    mine = lax.dynamic_slice_in_dim(held, slab * part, part, 1).astype(jnp.float32)
    for k in range(1, n_seq):
        outgoing = lax.dynamic_slice_in_dim(held, ((slab + k) % n_seq) * part, part, 1)
        perm = [(i, (i + k) % n_seq) for i in range(n_seq)]
        mine = mine + lax.ppermute(outgoing, "seq", perm).astype(jnp.float32)
    bit = 2
    while bit < n_dp:
        held = mine.astype(jnp.bfloat16)
        perm = [(i, i ^ bit) for i in range(n_dp)]
        mine = held.astype(jnp.float32) + lax.ppermute(held, "dp", perm).astype(jnp.float32)
        bit *= 2
    other = lax.ppermute(mine, "dp", [(i, i ^ 1) for i in range(n_dp)])
    mine = jnp.where(pair == 0, jnp.concatenate([mine, other], 2), jnp.concatenate([other, mine], 2))
    mine = jnp.swapaxes(mine, 1, 2)
    column_major = Layout(major_to_minor=(1, 0))
    grad_dw = with_layout_constraint(mine[0], column_major)
    grad_aw = with_layout_constraint(mine[1], column_major)
    return (row_grad.astype(jnp.bfloat16), grad_dw, grad_aw)


def solution(mesh):
    in_specs = (
        P("dp", "seq", "head"),
        P("dp", "seq"),
        P("dp", "seq"),
        P("dp", "seq", None),
        P("head", None),
        P("head", None),
    )
    out_specs = (P("dp", "seq", "head"), P("head", "seq"), P("head", "seq"))
    return jax.shard_map(shards, mesh=mesh, in_specs=in_specs, out_specs=out_specs, check_vma=False)
```

```python
import math

import jax
import jax.numpy as jnp
from jax import lax
from jax.experimental.layout import Layout, with_layout_constraint
from jax.sharding import PartitionSpec as P


def site_match(positions, slab_rows, slab_index):
    local_pos = positions - slab_index * slab_rows
    return local_pos[:, :, None] == jnp.arange(slab_rows, dtype=jnp.int32)[None, None, :]


def pair_slope(scores, target, allowed):
    rate = jax.nn.softplus(scores) + 1.0
    return jnp.where(
        allowed, (1.0 - target.astype(jnp.float32) / rate) * jax.nn.sigmoid(scores), 0.0
    ).astype(jnp.bfloat16)


def place_rows(match_bf, values):
    upper = values.astype(jnp.bfloat16)
    lower = (values - upper.astype(jnp.float32)).astype(jnp.bfloat16)
    placed = jnp.einsum("bnr,bnc->brc", match_bf, upper, preferred_element_type=jnp.float32)
    return placed + jnp.einsum("bnr,bnc->brc", match_bf, lower, preferred_element_type=jnp.float32)


def gather_by_permute(x, axes, count, me):
    pieces = [x]
    for k in range(1, count):
        perm = [(i, (i + k) % count) for i in range(count)]
        pieces.append(lax.ppermute(x, axes, perm))
    by_offset = jnp.stack(pieces)
    order = (me - jnp.arange(count, dtype=jnp.int32)) % count
    return jnp.take(by_offset, order, axis=0)


def shards(embed, donor_pos, acceptor_pos, target, donor_w, acceptor_w):
    batch, slab_rows, _ = embed.shape
    slab_sites = donor_pos.shape[1]
    width = donor_w.shape[1]
    scale = 1.0 / math.sqrt(width)
    n_seq = lax.axis_size("seq")
    n_head = lax.axis_size("head")
    slab = lax.axis_index("seq")
    sites = slab_sites * n_seq

    head = lax.axis_index("head")
    me = slab * n_head + head

    target_col = jnp.zeros((batch, sites, slab_sites), target.dtype)
    own_cols = lax.dynamic_slice_in_dim(target, slab * slab_sites, slab_sites, 2)
    target_col = lax.dynamic_update_slice_in_dim(target_col, own_cols, slab * slab_sites, 1)
    for k in range(1, n_seq):
        outgoing = lax.dynamic_slice_in_dim(
            target, jnp.minimum(slab + k, n_seq - 1) * slab_sites, slab_sites, 2
        )
        perm = [(i, i + k) for i in range(n_seq - k)]
        arrived = lax.ppermute(outgoing, "seq", perm)
        source = jnp.maximum(slab - k, 0)
        placed = lax.dynamic_update_slice_in_dim(target_col, arrived, source * slab_sites, 1)
        target_col = jnp.where(slab >= k, placed, target_col)

    donor_match = site_match(donor_pos, slab_rows, slab).astype(jnp.bfloat16)
    acceptor_match = site_match(acceptor_pos, slab_rows, slab).astype(jnp.bfloat16)
    donor_rows = jnp.einsum(
        "bnr,brc->bnc", donor_match, embed, preferred_element_type=jnp.float32
    ).astype(jnp.bfloat16)
    acceptor_rows = jnp.einsum(
        "bnr,brc->bnc", acceptor_match, embed, preferred_element_type=jnp.float32
    ).astype(jnp.bfloat16)
    donor_part = jnp.einsum(
        "bnc,cp->bnp", donor_rows, donor_w, preferred_element_type=jnp.float32
    ).astype(jnp.bfloat16)
    acceptor_part = jnp.einsum(
        "bnc,cp->bnp", acceptor_rows, acceptor_w, preferred_element_type=jnp.float32
    ).astype(jnp.bfloat16)

    both = 2 * slab_sites
    assert both % n_head == 0
    quarter = both // n_head
    parts = jnp.concatenate([donor_part, acceptor_part], axis=1)
    assert n_head & (n_head - 1) == 0
    pieces = [lax.dynamic_slice_in_dim(parts, head * quarter, quarter, 1)]
    for k in range(1, n_head):
        outgoing = lax.dynamic_slice_in_dim(parts, (head ^ k) * quarter, quarter, 1)
        pieces.append(lax.ppermute(outgoing, "head", [(i, i ^ k) for i in range(n_head)]))
    by_partner = jnp.stack(pieces)
    by_head = jnp.take(by_partner, head ^ jnp.arange(n_head, dtype=jnp.int32), axis=0)
    total = jnp.zeros((batch, quarter, width), jnp.float32)
    for h in range(n_head):
        total = total + by_head[h].astype(jnp.float32)
    feat_quarter = total.astype(jnp.bfloat16)

    pieces = [feat_quarter]
    for k in range(1, n_head):
        pieces.append(lax.ppermute(feat_quarter, "head", [(i, i ^ k) for i in range(n_head)]))
    slab_feats = jnp.take(jnp.stack(pieces), head ^ jnp.arange(n_head, dtype=jnp.int32), axis=0)
    slab_feats = jnp.moveaxis(slab_feats, 0, 1).reshape(batch, both, width)
    own_donor = slab_feats[:, :slab_sites]
    own_acceptor = slab_feats[:, slab_sites:]

    n_dp = lax.axis_size("dp")
    assert n_dp & (n_dp - 1) == 0 and n_dp >= 2
    dp = lax.axis_index("dp")
    pair = dp % 2
    channels = embed.shape[2]
    half = channels // 2
    part = width // n_seq
    if n_seq == 2:
        target_own = lax.dynamic_slice_in_dim(target, slab * slab_sites, slab_sites, 2)
        scores_own = (
            jnp.einsum("bip,bjp->bij", own_donor, own_acceptor, preferred_element_type=jnp.float32)
            * scale
        )
        allowed_own = (donor_pos[:, :, None] >= 0) & (acceptor_pos[:, None, :] > donor_pos[:, :, None])
        slope_own = pair_slope(scores_own, target_own, allowed_own)
        early_acceptor = (
            jnp.einsum("bij,bip->bjp", slope_own, own_donor, preferred_element_type=jnp.float32) * scale
        ).astype(jnp.bfloat16)
        early_donor = (
            jnp.einsum("bij,bjp->bip", slope_own, own_acceptor, preferred_element_type=jnp.float32)
            * scale
        ).astype(jnp.bfloat16)
        first = slab == 0
        grad_early = jnp.where(first, early_acceptor, early_donor)
        rows_early = jnp.where(first, acceptor_rows, donor_rows)

        def to_seq_partner(rows, grad):
            local = jnp.einsum("bnc,bnp->pc", rows, grad, preferred_element_type=jnp.float32)
            local = local.astype(jnp.bfloat16)
            kept = lax.dynamic_slice_in_dim(local, pair * half, half, 1).astype(jnp.float32)
            outgoing = lax.dynamic_slice_in_dim(local, (1 - pair) * half, half, 1)
            kept = kept + lax.ppermute(outgoing, "dp", [(i, i ^ 1) for i in range(n_dp)]).astype(
                jnp.float32
            )
            held = kept.astype(jnp.bfloat16)
            own = lax.dynamic_slice_in_dim(held, slab * part, part, 0).astype(jnp.float32)
            outgoing = lax.dynamic_slice_in_dim(held, (1 - slab) * part, part, 0)
            return own, lax.ppermute(outgoing, "seq", [(0, 1), (1, 0)]).astype(jnp.float32)

        own_early, from_early = to_seq_partner(rows_early, grad_early)

    assert slab_sites <= width
    flags = jnp.zeros((batch, 8, width), jnp.bfloat16)
    flags = flags.at[:, 0, :slab_sites].set((donor_pos >= 0).astype(jnp.bfloat16))
    flags = flags.at[:, 1, :slab_sites].set((acceptor_pos >= 0).astype(jnp.bfloat16))
    donor_feat_all = jnp.zeros((batch, sites, width), jnp.bfloat16)
    acceptor_feat_all = jnp.zeros((batch, sites, width), jnp.bfloat16)
    donor_feat_all = lax.dynamic_update_slice_in_dim(donor_feat_all, own_donor, slab * slab_sites, 1)
    acceptor_feat_all = lax.dynamic_update_slice_in_dim(
        acceptor_feat_all, own_acceptor, slab * slab_sites, 1
    )
    donor_ok_all = jnp.zeros((batch, sites), jnp.bool_)
    acceptor_ok_all = jnp.zeros((batch, sites), jnp.bool_)
    for k in range(1, n_seq):
        sent = jnp.where(slab + k < n_seq, own_donor, own_acceptor)
        perm = [(i, (i + k) % n_seq) for i in range(n_seq)]
        arrived = lax.ppermute(jnp.concatenate([sent, flags], axis=1), "seq", perm)
        if n_seq == 2:
            arrived, from_early = lax.optimization_barrier((arrived, from_early))
        source = (slab - k) % n_seq
        earlier = slab >= k
        feat_in = arrived[:, :slab_sites]
        donor_feat_all = jnp.where(
            earlier,
            lax.dynamic_update_slice_in_dim(donor_feat_all, feat_in, source * slab_sites, 1),
            donor_feat_all,
        )
        acceptor_feat_all = jnp.where(
            earlier,
            acceptor_feat_all,
            lax.dynamic_update_slice_in_dim(acceptor_feat_all, feat_in, source * slab_sites, 1),
        )
        donor_in = arrived[:, slab_sites, :slab_sites] > 0
        acceptor_in = arrived[:, slab_sites + 1, :slab_sites] > 0
        donor_ok_all = jnp.where(
            earlier,
            lax.dynamic_update_slice_in_dim(donor_ok_all, donor_in, source * slab_sites, 1),
            donor_ok_all,
        )
        acceptor_ok_all = jnp.where(
            earlier,
            acceptor_ok_all,
            lax.dynamic_update_slice_in_dim(acceptor_ok_all, acceptor_in, source * slab_sites, 1),
        )

    site_slab = jnp.arange(sites, dtype=jnp.int32) // slab_sites
    big = jnp.int32(1 << 30)
    acceptor_tiled = jnp.tile(acceptor_pos, (1, n_seq))
    acceptor_eff = jnp.where(
        site_slab[None, :] == slab,
        acceptor_tiled,
        jnp.where(
            (site_slab[None, :] > slab) & acceptor_ok_all, (slab + 1) * slab_rows, -1
        ),
    )
    donor_tiled = jnp.tile(donor_pos, (1, n_seq))
    donor_eff = jnp.where(
        site_slab[None, :] == slab,
        donor_tiled,
        jnp.where(
            site_slab[None, :] > slab,
            big,
            jnp.where(donor_ok_all, slab * slab_rows - 1, -1),
        ),
    )

    donor_feat = own_donor
    acceptor_feat = own_acceptor

    scores_row = (
        jnp.einsum("bip,bjp->bij", donor_feat, acceptor_feat_all, preferred_element_type=jnp.float32)
        * scale
    )
    allowed_row = (donor_pos[:, :, None] >= 0) & (acceptor_eff[:, None, :] > donor_pos[:, :, None])
    slope_row = pair_slope(scores_row, target, allowed_row)
    donor_grad = (
        jnp.einsum("bij,bjp->bip", slope_row, acceptor_feat_all, preferred_element_type=jnp.float32)
        * scale
    ).astype(jnp.bfloat16)

    scores_col = (
        jnp.einsum("bip,bjp->bij", donor_feat_all, acceptor_feat, preferred_element_type=jnp.float32)
        * scale
    )
    allowed_col = (donor_eff[:, :, None] >= 0) & (acceptor_pos[:, None, :] > donor_eff[:, :, None])
    slope_col = pair_slope(scores_col, target_col, allowed_col)
    acceptor_grad = (
        jnp.einsum("bij,bip->bjp", slope_col, donor_feat_all, preferred_element_type=jnp.float32)
        * scale
    ).astype(jnp.bfloat16)


    if n_seq == 2:
        first = slab == 0
        grad_early = jnp.where(first, early_acceptor, early_donor)
        rows_early = jnp.where(first, acceptor_rows, donor_rows)
        grad_late = jnp.where(first, donor_grad, acceptor_grad)
        rows_late = jnp.where(first, donor_rows, acceptor_rows)
        donor_grad = jnp.where(first, grad_late, grad_early)
        acceptor_grad = jnp.where(first, grad_early, grad_late)

        own_late, from_late = to_seq_partner(rows_late, grad_late)
        sum_early = own_early + from_late
        sum_late = own_late + from_early
        mine = jnp.stack(
            [jnp.where(first, sum_late, sum_early), jnp.where(first, sum_early, sum_late)]
        )
    else:
        local_dw = jnp.einsum(
            "bnc,bnp->pc", donor_rows, donor_grad, preferred_element_type=jnp.float32
        )
        local_aw = jnp.einsum(
            "bnc,bnp->pc", acceptor_rows, acceptor_grad, preferred_element_type=jnp.float32
        )
        blocks = jnp.stack([local_dw, local_aw]).astype(jnp.bfloat16)
        mine = lax.dynamic_slice_in_dim(blocks, pair * half, half, 2).astype(jnp.float32)
        outgoing = lax.dynamic_slice_in_dim(blocks, (1 - pair) * half, half, 2)
        mine = mine + lax.ppermute(outgoing, "dp", [(i, i ^ 1) for i in range(n_dp)]).astype(
            jnp.float32
        )
        held = mine.astype(jnp.bfloat16)
        mine = lax.dynamic_slice_in_dim(held, slab * part, part, 1).astype(jnp.float32)
        for k in range(1, n_seq):
            outgoing = lax.dynamic_slice_in_dim(held, ((slab + k) % n_seq) * part, part, 1)
            perm = [(i, (i + k) % n_seq) for i in range(n_seq)]
            mine = mine + lax.ppermute(outgoing, "seq", perm).astype(jnp.float32)
    donor_site = jnp.einsum("bnp,cp->bnc", donor_grad, donor_w, preferred_element_type=jnp.float32)
    acceptor_site = jnp.einsum(
        "bnp,cp->bnc", acceptor_grad, acceptor_w, preferred_element_type=jnp.float32
    )
    row_grad = place_rows(donor_match, donor_site) + place_rows(acceptor_match, acceptor_site)
    bit = 2
    while bit < n_dp:
        held = mine.astype(jnp.bfloat16)
        perm = [(i, i ^ bit) for i in range(n_dp)]
        mine = held.astype(jnp.float32) + lax.ppermute(held, "dp", perm).astype(jnp.float32)
        bit *= 2
    other = lax.ppermute(mine, "dp", [(i, i ^ 1) for i in range(n_dp)])
    mine = jnp.where(pair == 0, jnp.concatenate([mine, other], 2), jnp.concatenate([other, mine], 2))
    mine = jnp.swapaxes(mine, 1, 2)
    column_major = Layout(major_to_minor=(1, 0))
    grad_dw = with_layout_constraint(mine[0], column_major)
    grad_aw = with_layout_constraint(mine[1], column_major)
    return (row_grad.astype(jnp.bfloat16), grad_dw, grad_aw)


def solution(mesh):
    in_specs = (
        P("dp", "seq", "head"),
        P("dp", "seq"),
        P("dp", "seq"),
        P("dp", "seq", None),
        P("head", None),
        P("head", None),
    )
    out_specs = (P("dp", "seq", "head"), P("head", "seq"), P("head", "seq"))
    return jax.shard_map(shards, mesh=mesh, in_specs=in_specs, out_specs=out_specs, check_vma=False)
```

```python
import math

import jax
import jax.numpy as jnp
from jax import lax
from jax.experimental.layout import Layout, with_layout_constraint
from jax.sharding import PartitionSpec as P


def site_match(positions, slab_rows, slab_index):
    local_pos = positions - slab_index * slab_rows
    return local_pos[:, :, None] == jnp.arange(slab_rows, dtype=jnp.int32)[None, None, :]


def pair_slope(scores, target, allowed):
    rate = jax.nn.softplus(scores) + 1.0
    return jnp.where(
        allowed, (1.0 - target.astype(jnp.float32) / rate) * jax.nn.sigmoid(scores), 0.0
    ).astype(jnp.bfloat16)


def place_rows(match_bf, values):
    upper = values.astype(jnp.bfloat16)
    lower = (values - upper.astype(jnp.float32)).astype(jnp.bfloat16)
    placed = jnp.einsum("bnr,bnc->brc", match_bf, upper, preferred_element_type=jnp.float32)
    return placed + jnp.einsum("bnr,bnc->brc", match_bf, lower, preferred_element_type=jnp.float32)


def gather_by_permute(x, axes, count, me):
    pieces = [x]
    for k in range(1, count):
        perm = [(i, (i + k) % count) for i in range(count)]
        pieces.append(lax.ppermute(x, axes, perm))
    by_offset = jnp.stack(pieces)
    order = (me - jnp.arange(count, dtype=jnp.int32)) % count
    return jnp.take(by_offset, order, axis=0)


def shards(embed, donor_pos, acceptor_pos, target, donor_w, acceptor_w):
    batch, slab_rows, _ = embed.shape
    slab_sites = donor_pos.shape[1]
    width = donor_w.shape[1]
    scale = 1.0 / math.sqrt(width)
    n_seq = lax.axis_size("seq")
    n_head = lax.axis_size("head")
    slab = lax.axis_index("seq")
    sites = slab_sites * n_seq

    head = lax.axis_index("head")
    me = slab * n_head + head

    donor_match = site_match(donor_pos, slab_rows, slab).astype(jnp.bfloat16)
    acceptor_match = site_match(acceptor_pos, slab_rows, slab).astype(jnp.bfloat16)
    donor_rows = jnp.einsum(
        "bnr,brc->bnc", donor_match, embed, preferred_element_type=jnp.float32
    ).astype(jnp.bfloat16)
    acceptor_rows = jnp.einsum(
        "bnr,brc->bnc", acceptor_match, embed, preferred_element_type=jnp.float32
    ).astype(jnp.bfloat16)
    donor_part = jnp.einsum(
        "bnc,cp->bnp", donor_rows, donor_w, preferred_element_type=jnp.float32
    ).astype(jnp.bfloat16)
    acceptor_part = jnp.einsum(
        "bnc,cp->bnp", acceptor_rows, acceptor_w, preferred_element_type=jnp.float32
    ).astype(jnp.bfloat16)

    both = 2 * slab_sites
    assert both % n_head == 0
    quarter = both // n_head
    parts = jnp.concatenate([donor_part, acceptor_part], axis=1)
    parts, target_late = lax.optimization_barrier((parts, target))
    target_col = jnp.zeros((batch, sites, slab_sites), target.dtype)
    own_cols = lax.dynamic_slice_in_dim(target, slab * slab_sites, slab_sites, 2)
    target_col = lax.dynamic_update_slice_in_dim(target_col, own_cols, slab * slab_sites, 1)
    for k in range(1, n_seq):
        outgoing = lax.dynamic_slice_in_dim(
            target_late, jnp.minimum(slab + k, n_seq - 1) * slab_sites, slab_sites, 2
        )
        perm = [(i, i + k) for i in range(n_seq - k)]
        arrived = lax.ppermute(outgoing, "seq", perm)
        source = jnp.maximum(slab - k, 0)
        placed = lax.dynamic_update_slice_in_dim(target_col, arrived, source * slab_sites, 1)
        target_col = jnp.where(slab >= k, placed, target_col)

    assert n_head & (n_head - 1) == 0
    pieces = [lax.dynamic_slice_in_dim(parts, head * quarter, quarter, 1)]
    for k in range(1, n_head):
        outgoing = lax.dynamic_slice_in_dim(parts, (head ^ k) * quarter, quarter, 1)
        pieces.append(lax.ppermute(outgoing, "head", [(i, i ^ k) for i in range(n_head)]))
    by_partner = jnp.stack(pieces)
    by_head = jnp.take(by_partner, head ^ jnp.arange(n_head, dtype=jnp.int32), axis=0)
    total = jnp.zeros((batch, quarter, width), jnp.float32)
    for h in range(n_head):
        total = total + by_head[h].astype(jnp.float32)
    feat_quarter = total.astype(jnp.bfloat16)

    pieces = [feat_quarter]
    for k in range(1, n_head):
        pieces.append(lax.ppermute(feat_quarter, "head", [(i, i ^ k) for i in range(n_head)]))
    slab_feats = jnp.take(jnp.stack(pieces), head ^ jnp.arange(n_head, dtype=jnp.int32), axis=0)
    slab_feats = jnp.moveaxis(slab_feats, 0, 1).reshape(batch, both, width)
    own_donor = slab_feats[:, :slab_sites]
    own_acceptor = slab_feats[:, slab_sites:]

    n_dp = lax.axis_size("dp")
    assert n_dp & (n_dp - 1) == 0 and n_dp >= 2
    dp = lax.axis_index("dp")
    pair = dp % 2
    channels = embed.shape[2]
    half = channels // 2
    part = width // n_seq
    if n_seq == 2:
        target_own = lax.dynamic_slice_in_dim(target, slab * slab_sites, slab_sites, 2)
        scores_own = (
            jnp.einsum("bip,bjp->bij", own_donor, own_acceptor, preferred_element_type=jnp.float32)
            * scale
        )
        allowed_own = (donor_pos[:, :, None] >= 0) & (acceptor_pos[:, None, :] > donor_pos[:, :, None])
        slope_own = pair_slope(scores_own, target_own, allowed_own)
        early_acceptor = (
            jnp.einsum("bij,bip->bjp", slope_own, own_donor, preferred_element_type=jnp.float32) * scale
        ).astype(jnp.bfloat16)
        early_donor = (
            jnp.einsum("bij,bjp->bip", slope_own, own_acceptor, preferred_element_type=jnp.float32)
            * scale
        ).astype(jnp.bfloat16)
        first = slab == 0
        grad_early = jnp.where(first, early_acceptor, early_donor)
        rows_early = jnp.where(first, acceptor_rows, donor_rows)

        def to_seq_partner(rows, grad):
            local = jnp.einsum("bnc,bnp->pc", rows, grad, preferred_element_type=jnp.float32)
            local = local.astype(jnp.bfloat16)
            kept = lax.dynamic_slice_in_dim(local, pair * half, half, 1).astype(jnp.float32)
            outgoing = lax.dynamic_slice_in_dim(local, (1 - pair) * half, half, 1)
            kept = kept + lax.ppermute(outgoing, "dp", [(i, i ^ 1) for i in range(n_dp)]).astype(
                jnp.float32
            )
            held = kept.astype(jnp.bfloat16)
            own = lax.dynamic_slice_in_dim(held, slab * part, part, 0).astype(jnp.float32)
            outgoing = lax.dynamic_slice_in_dim(held, (1 - slab) * part, part, 0)
            return own, lax.ppermute(outgoing, "seq", [(0, 1), (1, 0)]).astype(jnp.float32)

        own_early, from_early = to_seq_partner(rows_early, grad_early)

    assert slab_sites <= width
    flags = jnp.zeros((batch, 8, width), jnp.bfloat16)
    flags = flags.at[:, 0, :slab_sites].set((donor_pos >= 0).astype(jnp.bfloat16))
    flags = flags.at[:, 1, :slab_sites].set((acceptor_pos >= 0).astype(jnp.bfloat16))
    donor_feat_all = jnp.zeros((batch, sites, width), jnp.bfloat16)
    acceptor_feat_all = jnp.zeros((batch, sites, width), jnp.bfloat16)
    donor_feat_all = lax.dynamic_update_slice_in_dim(donor_feat_all, own_donor, slab * slab_sites, 1)
    acceptor_feat_all = lax.dynamic_update_slice_in_dim(
        acceptor_feat_all, own_acceptor, slab * slab_sites, 1
    )
    donor_ok_all = jnp.zeros((batch, sites), jnp.bool_)
    acceptor_ok_all = jnp.zeros((batch, sites), jnp.bool_)
    for k in range(1, n_seq):
        sent = jnp.where(slab + k < n_seq, own_donor, own_acceptor)
        perm = [(i, (i + k) % n_seq) for i in range(n_seq)]
        arrived = lax.ppermute(jnp.concatenate([sent, flags], axis=1), "seq", perm)
        if n_seq == 2:
            arrived, from_early = lax.optimization_barrier((arrived, from_early))
        source = (slab - k) % n_seq
        earlier = slab >= k
        feat_in = arrived[:, :slab_sites]
        donor_feat_all = jnp.where(
            earlier,
            lax.dynamic_update_slice_in_dim(donor_feat_all, feat_in, source * slab_sites, 1),
            donor_feat_all,
        )
        acceptor_feat_all = jnp.where(
            earlier,
            acceptor_feat_all,
            lax.dynamic_update_slice_in_dim(acceptor_feat_all, feat_in, source * slab_sites, 1),
        )
        donor_in = arrived[:, slab_sites, :slab_sites] > 0
        acceptor_in = arrived[:, slab_sites + 1, :slab_sites] > 0
        donor_ok_all = jnp.where(
            earlier,
            lax.dynamic_update_slice_in_dim(donor_ok_all, donor_in, source * slab_sites, 1),
            donor_ok_all,
        )
        acceptor_ok_all = jnp.where(
            earlier,
            acceptor_ok_all,
            lax.dynamic_update_slice_in_dim(acceptor_ok_all, acceptor_in, source * slab_sites, 1),
        )

    site_slab = jnp.arange(sites, dtype=jnp.int32) // slab_sites
    big = jnp.int32(1 << 30)
    acceptor_tiled = jnp.tile(acceptor_pos, (1, n_seq))
    acceptor_eff = jnp.where(
        site_slab[None, :] == slab,
        acceptor_tiled,
        jnp.where(
            (site_slab[None, :] > slab) & acceptor_ok_all, (slab + 1) * slab_rows, -1
        ),
    )
    donor_tiled = jnp.tile(donor_pos, (1, n_seq))
    donor_eff = jnp.where(
        site_slab[None, :] == slab,
        donor_tiled,
        jnp.where(
            site_slab[None, :] > slab,
            big,
            jnp.where(donor_ok_all, slab * slab_rows - 1, -1),
        ),
    )

    donor_feat = own_donor
    acceptor_feat = own_acceptor

    scores_row = (
        jnp.einsum("bip,bjp->bij", donor_feat, acceptor_feat_all, preferred_element_type=jnp.float32)
        * scale
    )
    allowed_row = (donor_pos[:, :, None] >= 0) & (acceptor_eff[:, None, :] > donor_pos[:, :, None])
    slope_row = pair_slope(scores_row, target, allowed_row)
    donor_grad = (
        jnp.einsum("bij,bjp->bip", slope_row, acceptor_feat_all, preferred_element_type=jnp.float32)
        * scale
    ).astype(jnp.bfloat16)

    scores_col = (
        jnp.einsum("bip,bjp->bij", donor_feat_all, acceptor_feat, preferred_element_type=jnp.float32)
        * scale
    )
    allowed_col = (donor_eff[:, :, None] >= 0) & (acceptor_pos[:, None, :] > donor_eff[:, :, None])
    slope_col = pair_slope(scores_col, target_col, allowed_col)
    acceptor_grad = (
        jnp.einsum("bij,bip->bjp", slope_col, donor_feat_all, preferred_element_type=jnp.float32)
        * scale
    ).astype(jnp.bfloat16)


    if n_seq == 2:
        first = slab == 0
        grad_early = jnp.where(first, early_acceptor, early_donor)
        rows_early = jnp.where(first, acceptor_rows, donor_rows)
        grad_late = jnp.where(first, donor_grad, acceptor_grad)
        rows_late = jnp.where(first, donor_rows, acceptor_rows)
        donor_grad = jnp.where(first, grad_late, grad_early)
        acceptor_grad = jnp.where(first, grad_early, grad_late)

        own_late, from_late = to_seq_partner(rows_late, grad_late)
        sum_early = own_early + from_late
        sum_late = own_late + from_early
        mine = jnp.stack(
            [jnp.where(first, sum_late, sum_early), jnp.where(first, sum_early, sum_late)]
        )
    else:
        local_dw = jnp.einsum(
            "bnc,bnp->pc", donor_rows, donor_grad, preferred_element_type=jnp.float32
        )
        local_aw = jnp.einsum(
            "bnc,bnp->pc", acceptor_rows, acceptor_grad, preferred_element_type=jnp.float32
        )
        blocks = jnp.stack([local_dw, local_aw]).astype(jnp.bfloat16)
        mine = lax.dynamic_slice_in_dim(blocks, pair * half, half, 2).astype(jnp.float32)
        outgoing = lax.dynamic_slice_in_dim(blocks, (1 - pair) * half, half, 2)
        mine = mine + lax.ppermute(outgoing, "dp", [(i, i ^ 1) for i in range(n_dp)]).astype(
            jnp.float32
        )
        held = mine.astype(jnp.bfloat16)
        mine = lax.dynamic_slice_in_dim(held, slab * part, part, 1).astype(jnp.float32)
        for k in range(1, n_seq):
            outgoing = lax.dynamic_slice_in_dim(held, ((slab + k) % n_seq) * part, part, 1)
            perm = [(i, (i + k) % n_seq) for i in range(n_seq)]
            mine = mine + lax.ppermute(outgoing, "seq", perm).astype(jnp.float32)
    donor_site = jnp.einsum("bnp,cp->bnc", donor_grad, donor_w, preferred_element_type=jnp.float32)
    acceptor_site = jnp.einsum(
        "bnp,cp->bnc", acceptor_grad, acceptor_w, preferred_element_type=jnp.float32
    )
    row_grad = place_rows(donor_match, donor_site) + place_rows(acceptor_match, acceptor_site)
    bit = 2
    while bit < n_dp:
        held = mine.astype(jnp.bfloat16)
        perm = [(i, i ^ bit) for i in range(n_dp)]
        mine = held.astype(jnp.float32) + lax.ppermute(held, "dp", perm).astype(jnp.float32)
        bit *= 2
    other = lax.ppermute(mine, "dp", [(i, i ^ 1) for i in range(n_dp)])
    mine = jnp.where(pair == 0, jnp.concatenate([mine, other], 2), jnp.concatenate([other, mine], 2))
    mine = jnp.swapaxes(mine, 1, 2)
    column_major = Layout(major_to_minor=(1, 0))
    grad_dw = with_layout_constraint(mine[0], column_major)
    grad_aw = with_layout_constraint(mine[1], column_major)
    return (row_grad.astype(jnp.bfloat16), grad_dw, grad_aw)


def solution(mesh):
    in_specs = (
        P("dp", "seq", "head"),
        P("dp", "seq"),
        P("dp", "seq"),
        P("dp", "seq", None),
        P("head", None),
        P("head", None),
    )
    out_specs = (P("dp", "seq", "head"), P("head", "seq"), P("head", "seq"))
    return jax.shard_map(shards, mesh=mesh, in_specs=in_specs, out_specs=out_specs, check_vma=False)
```

```python
import math

import jax
import jax.numpy as jnp
from jax import lax
from jax.experimental.layout import Layout, with_layout_constraint
from jax.sharding import PartitionSpec as P


def site_match(positions, slab_rows, slab_index):
    local_pos = positions - slab_index * slab_rows
    return local_pos[:, :, None] == jnp.arange(slab_rows, dtype=jnp.int32)[None, None, :]


def pair_slope(scores, target, allowed):
    rate = jax.nn.softplus(scores) + 1.0
    return jnp.where(
        allowed, (1.0 - target.astype(jnp.float32) / rate) * jax.nn.sigmoid(scores), 0.0
    ).astype(jnp.bfloat16)


def place_rows(match_bf, values):
    upper = values.astype(jnp.bfloat16)
    lower = (values - upper.astype(jnp.float32)).astype(jnp.bfloat16)
    placed = jnp.einsum("bnr,bnc->brc", match_bf, upper, preferred_element_type=jnp.float32)
    return placed + jnp.einsum("bnr,bnc->brc", match_bf, lower, preferred_element_type=jnp.float32)


def gather_by_permute(x, axes, count, me):
    pieces = [x]
    for k in range(1, count):
        perm = [(i, (i + k) % count) for i in range(count)]
        pieces.append(lax.ppermute(x, axes, perm))
    by_offset = jnp.stack(pieces)
    order = (me - jnp.arange(count, dtype=jnp.int32)) % count
    return jnp.take(by_offset, order, axis=0)


def shards(embed, donor_pos, acceptor_pos, target, donor_w, acceptor_w):
    batch, slab_rows, _ = embed.shape
    slab_sites = donor_pos.shape[1]
    width = donor_w.shape[1]
    scale = 1.0 / math.sqrt(width)
    n_seq = lax.axis_size("seq")
    n_head = lax.axis_size("head")
    slab = lax.axis_index("seq")
    sites = slab_sites * n_seq

    head = lax.axis_index("head")
    me = slab * n_head + head

    target_col = jnp.zeros((batch, sites, slab_sites), target.dtype)
    own_cols = lax.dynamic_slice_in_dim(target, slab * slab_sites, slab_sites, 2)
    target_col = lax.dynamic_update_slice_in_dim(target_col, own_cols, slab * slab_sites, 1)
    for k in range(1, n_seq):
        outgoing = lax.dynamic_slice_in_dim(
            target, jnp.minimum(slab + k, n_seq - 1) * slab_sites, slab_sites, 2
        )
        perm = [(i, i + k) for i in range(n_seq - k)]
        arrived = lax.ppermute(outgoing, "seq", perm)
        source = jnp.maximum(slab - k, 0)
        placed = lax.dynamic_update_slice_in_dim(target_col, arrived, source * slab_sites, 1)
        target_col = jnp.where(slab >= k, placed, target_col)

    donor_match = site_match(donor_pos, slab_rows, slab).astype(jnp.bfloat16)
    acceptor_match = site_match(acceptor_pos, slab_rows, slab).astype(jnp.bfloat16)
    donor_rows = jnp.einsum(
        "bnr,brc->bnc", donor_match, embed, preferred_element_type=jnp.float32
    ).astype(jnp.bfloat16)
    acceptor_rows = jnp.einsum(
        "bnr,brc->bnc", acceptor_match, embed, preferred_element_type=jnp.float32
    ).astype(jnp.bfloat16)
    donor_part = jnp.einsum(
        "bnc,cp->bnp", donor_rows, donor_w, preferred_element_type=jnp.float32
    ).astype(jnp.bfloat16)
    acceptor_part = jnp.einsum(
        "bnc,cp->bnp", acceptor_rows, acceptor_w, preferred_element_type=jnp.float32
    ).astype(jnp.bfloat16)

    both = 2 * slab_sites
    assert both % n_head == 0
    quarter = both // n_head
    parts = jnp.concatenate([donor_part, acceptor_part], axis=1)
    assert n_head & (n_head - 1) == 0
    pieces = [lax.dynamic_slice_in_dim(parts, head * quarter, quarter, 1)]
    for k in range(1, n_head):
        outgoing = lax.dynamic_slice_in_dim(parts, (head ^ k) * quarter, quarter, 1)
        pieces.append(lax.ppermute(outgoing, "head", [(i, i ^ k) for i in range(n_head)]))
    by_partner = jnp.stack(pieces)
    by_head = jnp.take(by_partner, head ^ jnp.arange(n_head, dtype=jnp.int32), axis=0)
    total = jnp.zeros((batch, quarter, width), jnp.float32)
    for h in range(n_head):
        total = total + by_head[h].astype(jnp.float32)
    feat_quarter = total.astype(jnp.bfloat16)

    pieces = [feat_quarter]
    for k in range(1, n_head):
        pieces.append(lax.ppermute(feat_quarter, "head", [(i, i ^ k) for i in range(n_head)]))
    slab_feats = jnp.take(jnp.stack(pieces), head ^ jnp.arange(n_head, dtype=jnp.int32), axis=0)
    slab_feats = jnp.moveaxis(slab_feats, 0, 1).reshape(batch, both, width)
    own_donor = slab_feats[:, :slab_sites]
    own_acceptor = slab_feats[:, slab_sites:]

    assert slab_sites <= width
    flags = jnp.zeros((batch, 8, width), jnp.bfloat16)
    flags = flags.at[:, 0, :slab_sites].set((donor_pos >= 0).astype(jnp.bfloat16))
    flags = flags.at[:, 1, :slab_sites].set((acceptor_pos >= 0).astype(jnp.bfloat16))
    donor_feat_all = jnp.zeros((batch, sites, width), jnp.bfloat16)
    acceptor_feat_all = jnp.zeros((batch, sites, width), jnp.bfloat16)
    donor_feat_all = lax.dynamic_update_slice_in_dim(donor_feat_all, own_donor, slab * slab_sites, 1)
    acceptor_feat_all = lax.dynamic_update_slice_in_dim(
        acceptor_feat_all, own_acceptor, slab * slab_sites, 1
    )
    donor_ok_all = jnp.zeros((batch, sites), jnp.bool_)
    acceptor_ok_all = jnp.zeros((batch, sites), jnp.bool_)
    for k in range(1, n_seq):
        sent = jnp.where(slab + k < n_seq, own_donor, own_acceptor)
        perm = [(i, (i + k) % n_seq) for i in range(n_seq)]
        arrived = lax.ppermute(jnp.concatenate([sent, flags], axis=1), "seq", perm)
        source = (slab - k) % n_seq
        earlier = slab >= k
        feat_in = arrived[:, :slab_sites]
        donor_feat_all = jnp.where(
            earlier,
            lax.dynamic_update_slice_in_dim(donor_feat_all, feat_in, source * slab_sites, 1),
            donor_feat_all,
        )
        acceptor_feat_all = jnp.where(
            earlier,
            acceptor_feat_all,
            lax.dynamic_update_slice_in_dim(acceptor_feat_all, feat_in, source * slab_sites, 1),
        )
        donor_in = arrived[:, slab_sites, :slab_sites] > 0
        acceptor_in = arrived[:, slab_sites + 1, :slab_sites] > 0
        donor_ok_all = jnp.where(
            earlier,
            lax.dynamic_update_slice_in_dim(donor_ok_all, donor_in, source * slab_sites, 1),
            donor_ok_all,
        )
        acceptor_ok_all = jnp.where(
            earlier,
            acceptor_ok_all,
            lax.dynamic_update_slice_in_dim(acceptor_ok_all, acceptor_in, source * slab_sites, 1),
        )

    site_slab = jnp.arange(sites, dtype=jnp.int32) // slab_sites
    big = jnp.int32(1 << 30)
    acceptor_tiled = jnp.tile(acceptor_pos, (1, n_seq))
    acceptor_eff = jnp.where(
        site_slab[None, :] == slab,
        acceptor_tiled,
        jnp.where(
            (site_slab[None, :] > slab) & acceptor_ok_all, (slab + 1) * slab_rows, -1
        ),
    )
    donor_tiled = jnp.tile(donor_pos, (1, n_seq))
    donor_eff = jnp.where(
        site_slab[None, :] == slab,
        donor_tiled,
        jnp.where(
            site_slab[None, :] > slab,
            big,
            jnp.where(donor_ok_all, slab * slab_rows - 1, -1),
        ),
    )

    donor_feat = own_donor
    acceptor_feat = own_acceptor

    scores_row = (
        jnp.einsum("bip,bjp->bij", donor_feat, acceptor_feat_all, preferred_element_type=jnp.float32)
        * scale
    )
    allowed_row = (donor_pos[:, :, None] >= 0) & (acceptor_eff[:, None, :] > donor_pos[:, :, None])
    slope_row = pair_slope(scores_row, target, allowed_row)
    donor_grad = (
        jnp.einsum("bij,bjp->bip", slope_row, acceptor_feat_all, preferred_element_type=jnp.float32)
        * scale
    ).astype(jnp.bfloat16)

    scores_col = (
        jnp.einsum("bip,bjp->bij", donor_feat_all, acceptor_feat, preferred_element_type=jnp.float32)
        * scale
    )
    allowed_col = (donor_eff[:, :, None] >= 0) & (acceptor_pos[:, None, :] > donor_eff[:, :, None])
    slope_col = pair_slope(scores_col, target_col, allowed_col)
    acceptor_grad = (
        jnp.einsum("bij,bip->bjp", slope_col, donor_feat_all, preferred_element_type=jnp.float32)
        * scale
    ).astype(jnp.bfloat16)

    donor_site = jnp.einsum("bnp,cp->bnc", donor_grad, donor_w, preferred_element_type=jnp.float32)
    acceptor_site = jnp.einsum(
        "bnp,cp->bnc", acceptor_grad, acceptor_w, preferred_element_type=jnp.float32
    )
    row_grad = place_rows(donor_match, donor_site) + place_rows(acceptor_match, acceptor_site)

    local_dw = jnp.einsum("bnc,bnp->pc", donor_rows, donor_grad, preferred_element_type=jnp.float32)
    local_aw = jnp.einsum(
        "bnc,bnp->pc", acceptor_rows, acceptor_grad, preferred_element_type=jnp.float32
    )
    n_dp = lax.axis_size("dp")
    assert n_dp & (n_dp - 1) == 0 and n_dp >= 2
    dp = lax.axis_index("dp")
    pair = dp % 2
    channels = local_dw.shape[1]
    half = channels // 2
    part = width // n_seq
    blocks = jnp.stack([local_dw, local_aw]).astype(jnp.bfloat16)
    mine = lax.dynamic_slice_in_dim(blocks, pair * half, half, 2).astype(jnp.float32)
    outgoing = lax.dynamic_slice_in_dim(blocks, (1 - pair) * half, half, 2)
    mine = mine + lax.ppermute(outgoing, "dp", [(i, i ^ 1) for i in range(n_dp)]).astype(jnp.float32)
    held = mine.astype(jnp.bfloat16)
    group = (n_dp // 2) * n_seq
    if group <= 4 and group & (group - 1) == 0:
        me_g = (dp // 2) * n_seq + slab
        pieces = [lax.dynamic_slice_in_dim(held, slab * part, part, 1)]
        for k in range(1, group):
            dest_part = (me_g ^ k) % n_seq
            outgoing = lax.dynamic_slice_in_dim(held, dest_part * part, part, 1)
            perm = []
            for d in range(n_dp):
                for s in range(n_seq):
                    g = (d // 2) * n_seq + s
                    h = g ^ k
                    perm.append((d * n_seq + s, ((h // n_seq) * 2 + d % 2) * n_seq + h % n_seq))
            pieces.append(lax.ppermute(outgoing, ("dp", "seq"), perm))
        by_source = jnp.take(jnp.stack(pieces), me_g ^ jnp.arange(group, dtype=jnp.int32), axis=0)
        mine = by_source[0].astype(jnp.float32)
        for t in range(1, group):
            mine = mine + by_source[t].astype(jnp.float32)
    else:
        mine = lax.dynamic_slice_in_dim(held, slab * part, part, 1).astype(jnp.float32)
        for k in range(1, n_seq):
            outgoing = lax.dynamic_slice_in_dim(held, ((slab + k) % n_seq) * part, part, 1)
            perm = [(i, (i + k) % n_seq) for i in range(n_seq)]
            mine = mine + lax.ppermute(outgoing, "seq", perm).astype(jnp.float32)
        bit = 2
        while bit < n_dp:
            held = mine.astype(jnp.bfloat16)
            perm = [(i, i ^ bit) for i in range(n_dp)]
            mine = held.astype(jnp.float32) + lax.ppermute(held, "dp", perm).astype(jnp.float32)
            bit *= 2
    other = lax.ppermute(mine, "dp", [(i, i ^ 1) for i in range(n_dp)])
    mine = jnp.where(pair == 0, jnp.concatenate([mine, other], 2), jnp.concatenate([other, mine], 2))
    mine = jnp.swapaxes(mine, 1, 2)
    column_major = Layout(major_to_minor=(1, 0))
    grad_dw = with_layout_constraint(mine[0], column_major)
    grad_aw = with_layout_constraint(mine[1], column_major)
    return (row_grad.astype(jnp.bfloat16), grad_dw, grad_aw)


def solution(mesh):
    in_specs = (
        P("dp", "seq", "head"),
        P("dp", "seq"),
        P("dp", "seq"),
        P("dp", "seq", None),
        P("head", None),
        P("head", None),
    )
    out_specs = (P("dp", "seq", "head"), P("head", "seq"), P("head", "seq"))
    return jax.shard_map(shards, mesh=mesh, in_specs=in_specs, out_specs=out_specs, check_vma=False)
```

```python
import math

import jax
import jax.numpy as jnp
from jax import lax
from jax.experimental.layout import Layout, with_layout_constraint
from jax.sharding import PartitionSpec as P


def site_match(positions, slab_rows, slab_index):
    local_pos = positions - slab_index * slab_rows
    return local_pos[:, :, None] == jnp.arange(slab_rows, dtype=jnp.int32)[None, None, :]


def pair_slope(scores, target, allowed):
    rate = jax.nn.softplus(scores) + 1.0
    return jnp.where(
        allowed, (1.0 - target.astype(jnp.float32) / rate) * jax.nn.sigmoid(scores), 0.0
    ).astype(jnp.bfloat16)


def place_rows(match_bf, values):
    upper = values.astype(jnp.bfloat16)
    lower = (values - upper.astype(jnp.float32)).astype(jnp.bfloat16)
    placed = jnp.einsum("bnr,bnc->brc", match_bf, upper, preferred_element_type=jnp.float32)
    return placed + jnp.einsum("bnr,bnc->brc", match_bf, lower, preferred_element_type=jnp.float32)


def gather_by_permute(x, axes, count, me):
    pieces = [x]
    for k in range(1, count):
        perm = [(i, (i + k) % count) for i in range(count)]
        pieces.append(lax.ppermute(x, axes, perm))
    by_offset = jnp.stack(pieces)
    order = (me - jnp.arange(count, dtype=jnp.int32)) % count
    return jnp.take(by_offset, order, axis=0)


def shards(embed, donor_pos, acceptor_pos, target, donor_w, acceptor_w):
    batch, slab_rows, _ = embed.shape
    slab_sites = donor_pos.shape[1]
    width = donor_w.shape[1]
    scale = 1.0 / math.sqrt(width)
    n_seq = lax.axis_size("seq")
    n_head = lax.axis_size("head")
    slab = lax.axis_index("seq")
    sites = slab_sites * n_seq

    head = lax.axis_index("head")
    me = slab * n_head + head

    donor_match = site_match(donor_pos, slab_rows, slab).astype(jnp.bfloat16)
    acceptor_match = site_match(acceptor_pos, slab_rows, slab).astype(jnp.bfloat16)
    donor_rows = jnp.einsum(
        "bnr,brc->bnc", donor_match, embed, preferred_element_type=jnp.float32
    ).astype(jnp.bfloat16)
    acceptor_rows = jnp.einsum(
        "bnr,brc->bnc", acceptor_match, embed, preferred_element_type=jnp.float32
    ).astype(jnp.bfloat16)
    donor_part = jnp.einsum(
        "bnc,cp->bnp", donor_rows, donor_w, preferred_element_type=jnp.float32
    ).astype(jnp.bfloat16)
    acceptor_part = jnp.einsum(
        "bnc,cp->bnp", acceptor_rows, acceptor_w, preferred_element_type=jnp.float32
    ).astype(jnp.bfloat16)

    both = 2 * slab_sites
    assert both % n_head == 0
    quarter = both // n_head
    parts = jnp.concatenate([donor_part, acceptor_part], axis=1)
    assert n_head & (n_head - 1) == 0
    pieces = [lax.dynamic_slice_in_dim(parts, head * quarter, quarter, 1)]
    for k in range(1, n_head):
        outgoing = lax.dynamic_slice_in_dim(parts, (head ^ k) * quarter, quarter, 1)
        pieces.append(lax.ppermute(outgoing, "head", [(i, i ^ k) for i in range(n_head)]))
    by_partner = jnp.stack(pieces)
    by_head = jnp.take(by_partner, head ^ jnp.arange(n_head, dtype=jnp.int32), axis=0)
    total = jnp.zeros((batch, quarter, width), jnp.float32)
    for h in range(n_head):
        total = total + by_head[h].astype(jnp.float32)
    feat_quarter = total.astype(jnp.bfloat16)

    pieces = [feat_quarter]
    for k in range(1, n_head):
        pieces.append(lax.ppermute(feat_quarter, "head", [(i, i ^ k) for i in range(n_head)]))
    slab_feats = jnp.take(jnp.stack(pieces), head ^ jnp.arange(n_head, dtype=jnp.int32), axis=0)
    slab_feats = jnp.moveaxis(slab_feats, 0, 1).reshape(batch, both, width)
    own_donor = slab_feats[:, :slab_sites]
    own_acceptor = slab_feats[:, slab_sites:]

    n_dp = lax.axis_size("dp")
    assert n_dp & (n_dp - 1) == 0 and n_dp >= 2
    dp = lax.axis_index("dp")
    pair = dp % 2
    channels = embed.shape[2]
    half = channels // 2
    part = width // n_seq
    if n_seq == 2:
        target_own = lax.dynamic_slice_in_dim(target, slab * slab_sites, slab_sites, 2)
        scores_own = (
            jnp.einsum("bip,bjp->bij", own_donor, own_acceptor, preferred_element_type=jnp.float32)
            * scale
        )
        allowed_own = (donor_pos[:, :, None] >= 0) & (acceptor_pos[:, None, :] > donor_pos[:, :, None])
        slope_own = pair_slope(scores_own, target_own, allowed_own)
        early_acceptor = (
            jnp.einsum("bij,bip->bjp", slope_own, own_donor, preferred_element_type=jnp.float32) * scale
        ).astype(jnp.bfloat16)
        early_donor = (
            jnp.einsum("bij,bjp->bip", slope_own, own_acceptor, preferred_element_type=jnp.float32)
            * scale
        ).astype(jnp.bfloat16)
        first = slab == 0
        grad_early = jnp.where(first, early_acceptor, early_donor)
        rows_early = jnp.where(first, acceptor_rows, donor_rows)

        def to_seq_partner(rows, grad):
            local = jnp.einsum("bnc,bnp->pc", rows, grad, preferred_element_type=jnp.float32)
            local = local.astype(jnp.bfloat16)
            kept = lax.dynamic_slice_in_dim(local, pair * half, half, 1).astype(jnp.float32)
            outgoing = lax.dynamic_slice_in_dim(local, (1 - pair) * half, half, 1)
            kept = kept + lax.ppermute(outgoing, "dp", [(i, i ^ 1) for i in range(n_dp)]).astype(
                jnp.float32
            )
            held = kept.astype(jnp.bfloat16)
            own = lax.dynamic_slice_in_dim(held, slab * part, part, 0).astype(jnp.float32)
            return own, lax.dynamic_slice_in_dim(held, (1 - slab) * part, part, 0)

        def from_seq_partner(outgoing):
            return lax.ppermute(outgoing, "seq", [(0, 1), (1, 0)]).astype(jnp.float32)

        own_early, out_early = to_seq_partner(rows_early, grad_early)

    assert slab_sites <= width
    flags = jnp.zeros((batch, 8, width), jnp.bfloat16)
    flags = flags.at[:, 0, :slab_sites].set((donor_pos >= 0).astype(jnp.bfloat16))
    flags = flags.at[:, 1, :slab_sites].set((acceptor_pos >= 0).astype(jnp.bfloat16))
    donor_feat_all = jnp.zeros((batch, sites, width), jnp.bfloat16)
    acceptor_feat_all = jnp.zeros((batch, sites, width), jnp.bfloat16)
    donor_feat_all = lax.dynamic_update_slice_in_dim(donor_feat_all, own_donor, slab * slab_sites, 1)
    acceptor_feat_all = lax.dynamic_update_slice_in_dim(
        acceptor_feat_all, own_acceptor, slab * slab_sites, 1
    )
    donor_ok_all = jnp.zeros((batch, sites), jnp.bool_)
    acceptor_ok_all = jnp.zeros((batch, sites), jnp.bool_)
    target_col = jnp.zeros((batch, sites, slab_sites), target.dtype)
    own_cols = lax.dynamic_slice_in_dim(target, slab * slab_sites, slab_sites, 2)
    target_col = lax.dynamic_update_slice_in_dim(target_col, own_cols, slab * slab_sites, 1)
    for k in range(1, n_seq):
        sent = jnp.where(slab + k < n_seq, own_donor, own_acceptor)
        target_block = lax.dynamic_slice_in_dim(
            target, jnp.minimum(slab + k, n_seq - 1) * slab_sites, slab_sites, 2
        ).reshape(batch, slab_sites * slab_sites)
        target_rows = -(-(slab_sites * slab_sites) // width)
        target_block = jnp.pad(target_block, ((0, 0), (0, target_rows * width - slab_sites * slab_sites)))
        payload = jnp.concatenate(
            [sent, flags, target_block.reshape(batch, target_rows, width).astype(jnp.bfloat16)], axis=1
        )
        perm = [(i, (i + k) % n_seq) for i in range(n_seq)]
        arrived = lax.ppermute(payload, "seq", perm)
        source = (slab - k) % n_seq
        earlier = slab >= k
        target_in = (
            arrived[:, slab_sites + 8 :]
            .reshape(batch, target_rows * width)[:, : slab_sites * slab_sites]
            .reshape(batch, slab_sites, slab_sites)
        )
        target_col = jnp.where(
            earlier,
            lax.dynamic_update_slice_in_dim(target_col, target_in, source * slab_sites, 1),
            target_col,
        )
        feat_in = arrived[:, :slab_sites]
        donor_feat_all = jnp.where(
            earlier,
            lax.dynamic_update_slice_in_dim(donor_feat_all, feat_in, source * slab_sites, 1),
            donor_feat_all,
        )
        acceptor_feat_all = jnp.where(
            earlier,
            acceptor_feat_all,
            lax.dynamic_update_slice_in_dim(acceptor_feat_all, feat_in, source * slab_sites, 1),
        )
        donor_in = arrived[:, slab_sites, :slab_sites] > 0
        acceptor_in = arrived[:, slab_sites + 1, :slab_sites] > 0
        donor_ok_all = jnp.where(
            earlier,
            lax.dynamic_update_slice_in_dim(donor_ok_all, donor_in, source * slab_sites, 1),
            donor_ok_all,
        )
        acceptor_ok_all = jnp.where(
            earlier,
            acceptor_ok_all,
            lax.dynamic_update_slice_in_dim(acceptor_ok_all, acceptor_in, source * slab_sites, 1),
        )

    if n_seq == 2:
        out_early, arrived = lax.optimization_barrier((out_early, arrived))
        from_early = from_seq_partner(out_early)

    site_slab = jnp.arange(sites, dtype=jnp.int32) // slab_sites
    big = jnp.int32(1 << 30)
    acceptor_tiled = jnp.tile(acceptor_pos, (1, n_seq))
    acceptor_eff = jnp.where(
        site_slab[None, :] == slab,
        acceptor_tiled,
        jnp.where(
            (site_slab[None, :] > slab) & acceptor_ok_all, (slab + 1) * slab_rows, -1
        ),
    )
    donor_tiled = jnp.tile(donor_pos, (1, n_seq))
    donor_eff = jnp.where(
        site_slab[None, :] == slab,
        donor_tiled,
        jnp.where(
            site_slab[None, :] > slab,
            big,
            jnp.where(donor_ok_all, slab * slab_rows - 1, -1),
        ),
    )

    donor_feat = own_donor
    acceptor_feat = own_acceptor

    scores_row = (
        jnp.einsum("bip,bjp->bij", donor_feat, acceptor_feat_all, preferred_element_type=jnp.float32)
        * scale
    )
    allowed_row = (donor_pos[:, :, None] >= 0) & (acceptor_eff[:, None, :] > donor_pos[:, :, None])
    slope_row = pair_slope(scores_row, target, allowed_row)
    donor_grad = (
        jnp.einsum("bij,bjp->bip", slope_row, acceptor_feat_all, preferred_element_type=jnp.float32)
        * scale
    ).astype(jnp.bfloat16)

    scores_col = (
        jnp.einsum("bip,bjp->bij", donor_feat_all, acceptor_feat, preferred_element_type=jnp.float32)
        * scale
    )
    allowed_col = (donor_eff[:, :, None] >= 0) & (acceptor_pos[:, None, :] > donor_eff[:, :, None])
    slope_col = pair_slope(scores_col, target_col, allowed_col)
    acceptor_grad = (
        jnp.einsum("bij,bip->bjp", slope_col, donor_feat_all, preferred_element_type=jnp.float32)
        * scale
    ).astype(jnp.bfloat16)


    if n_seq == 2:
        first = slab == 0
        grad_early = jnp.where(first, early_acceptor, early_donor)
        rows_early = jnp.where(first, acceptor_rows, donor_rows)
        grad_late = jnp.where(first, donor_grad, acceptor_grad)
        rows_late = jnp.where(first, donor_rows, acceptor_rows)
        donor_grad = jnp.where(first, grad_late, grad_early)
        acceptor_grad = jnp.where(first, grad_early, grad_late)

        own_late, out_late = to_seq_partner(rows_late, grad_late)
        from_late = from_seq_partner(out_late)
        sum_early = own_early + from_late
        sum_late = own_late + from_early
        mine = jnp.stack(
            [jnp.where(first, sum_late, sum_early), jnp.where(first, sum_early, sum_late)]
        )
    else:
        local_dw = jnp.einsum(
            "bnc,bnp->pc", donor_rows, donor_grad, preferred_element_type=jnp.float32
        )
        local_aw = jnp.einsum(
            "bnc,bnp->pc", acceptor_rows, acceptor_grad, preferred_element_type=jnp.float32
        )
        blocks = jnp.stack([local_dw, local_aw]).astype(jnp.bfloat16)
        mine = lax.dynamic_slice_in_dim(blocks, pair * half, half, 2).astype(jnp.float32)
        outgoing = lax.dynamic_slice_in_dim(blocks, (1 - pair) * half, half, 2)
        mine = mine + lax.ppermute(outgoing, "dp", [(i, i ^ 1) for i in range(n_dp)]).astype(
            jnp.float32
        )
        held = mine.astype(jnp.bfloat16)
        mine = lax.dynamic_slice_in_dim(held, slab * part, part, 1).astype(jnp.float32)
        for k in range(1, n_seq):
            outgoing = lax.dynamic_slice_in_dim(held, ((slab + k) % n_seq) * part, part, 1)
            perm = [(i, (i + k) % n_seq) for i in range(n_seq)]
            mine = mine + lax.ppermute(outgoing, "seq", perm).astype(jnp.float32)
    donor_site = jnp.einsum("bnp,cp->bnc", donor_grad, donor_w, preferred_element_type=jnp.float32)
    acceptor_site = jnp.einsum(
        "bnp,cp->bnc", acceptor_grad, acceptor_w, preferred_element_type=jnp.float32
    )
    row_grad = place_rows(donor_match, donor_site) + place_rows(acceptor_match, acceptor_site)
    bit = 2
    while bit < n_dp:
        held = mine.astype(jnp.bfloat16)
        perm = [(i, i ^ bit) for i in range(n_dp)]
        mine = held.astype(jnp.float32) + lax.ppermute(held, "dp", perm).astype(jnp.float32)
        bit *= 2
    other = lax.ppermute(mine, "dp", [(i, i ^ 1) for i in range(n_dp)])
    mine = jnp.where(pair == 0, jnp.concatenate([mine, other], 2), jnp.concatenate([other, mine], 2))
    mine = jnp.swapaxes(mine, 1, 2)
    column_major = Layout(major_to_minor=(1, 0))
    grad_dw = with_layout_constraint(mine[0], column_major)
    grad_aw = with_layout_constraint(mine[1], column_major)
    return (row_grad.astype(jnp.bfloat16), grad_dw, grad_aw)


def solution(mesh):
    in_specs = (
        P("dp", "seq", "head"),
        P("dp", "seq"),
        P("dp", "seq"),
        P("dp", "seq", None),
        P("head", None),
        P("head", None),
    )
    out_specs = (P("dp", "seq", "head"), P("head", "seq"), P("head", "seq"))
    return jax.shard_map(shards, mesh=mesh, in_specs=in_specs, out_specs=out_specs, check_vma=False)
```

```python
import math

import jax
import jax.numpy as jnp
from jax import lax
from jax.experimental.layout import Layout, with_layout_constraint
from jax.sharding import PartitionSpec as P


def site_match(positions, slab_rows, slab_index):
    local_pos = positions - slab_index * slab_rows
    return local_pos[:, :, None] == jnp.arange(slab_rows, dtype=jnp.int32)[None, None, :]


def pair_slope(scores, target, allowed):
    rate = jax.nn.softplus(scores) + 1.0
    return jnp.where(
        allowed, (1.0 - target.astype(jnp.float32) / rate) * jax.nn.sigmoid(scores), 0.0
    ).astype(jnp.bfloat16)


def place_rows(match_bf, values):
    upper = values.astype(jnp.bfloat16)
    lower = (values - upper.astype(jnp.float32)).astype(jnp.bfloat16)
    placed = jnp.einsum("bnr,bnc->brc", match_bf, upper, preferred_element_type=jnp.float32)
    return placed + jnp.einsum("bnr,bnc->brc", match_bf, lower, preferred_element_type=jnp.float32)


def gather_by_permute(x, axes, count, me):
    pieces = [x]
    for k in range(1, count):
        perm = [(i, (i + k) % count) for i in range(count)]
        pieces.append(lax.ppermute(x, axes, perm))
    by_offset = jnp.stack(pieces)
    order = (me - jnp.arange(count, dtype=jnp.int32)) % count
    return jnp.take(by_offset, order, axis=0)


def shards(embed, donor_pos, acceptor_pos, target, donor_w, acceptor_w):
    batch, slab_rows, _ = embed.shape
    slab_sites = donor_pos.shape[1]
    width = donor_w.shape[1]
    scale = 1.0 / math.sqrt(width)
    n_seq = lax.axis_size("seq")
    n_head = lax.axis_size("head")
    slab = lax.axis_index("seq")
    sites = slab_sites * n_seq

    head = lax.axis_index("head")
    me = slab * n_head + head

    donor_match = site_match(donor_pos, slab_rows, slab).astype(jnp.bfloat16)
    acceptor_match = site_match(acceptor_pos, slab_rows, slab).astype(jnp.bfloat16)
    donor_rows = jnp.einsum(
        "bnr,brc->bnc", donor_match, embed, preferred_element_type=jnp.float32
    ).astype(jnp.bfloat16)
    acceptor_rows = jnp.einsum(
        "bnr,brc->bnc", acceptor_match, embed, preferred_element_type=jnp.float32
    ).astype(jnp.bfloat16)
    donor_part = jnp.einsum(
        "bnc,cp->bnp", donor_rows, donor_w, preferred_element_type=jnp.float32
    ).astype(jnp.bfloat16)
    acceptor_part = jnp.einsum(
        "bnc,cp->bnp", acceptor_rows, acceptor_w, preferred_element_type=jnp.float32
    ).astype(jnp.bfloat16)

    both = 2 * slab_sites
    assert both % n_head == 0
    quarter = both // n_head
    parts = jnp.concatenate([donor_part, acceptor_part], axis=1)
    assert n_head & (n_head - 1) == 0
    pieces = [lax.dynamic_slice_in_dim(parts, head * quarter, quarter, 1)]
    for k in range(1, n_head):
        outgoing = lax.dynamic_slice_in_dim(parts, (head ^ k) * quarter, quarter, 1)
        pieces.append(lax.ppermute(outgoing, "head", [(i, i ^ k) for i in range(n_head)]))
    by_partner = jnp.stack(pieces)
    by_head = jnp.take(by_partner, head ^ jnp.arange(n_head, dtype=jnp.int32), axis=0)
    total = jnp.zeros((batch, quarter, width), jnp.float32)
    for h in range(n_head):
        total = total + by_head[h].astype(jnp.float32)
    feat_quarter = total.astype(jnp.bfloat16)

    pieces = [feat_quarter]
    for k in range(1, n_head):
        pieces.append(lax.ppermute(feat_quarter, "head", [(i, i ^ k) for i in range(n_head)]))
    slab_feats = jnp.take(jnp.stack(pieces), head ^ jnp.arange(n_head, dtype=jnp.int32), axis=0)
    slab_feats = jnp.moveaxis(slab_feats, 0, 1).reshape(batch, both, width)
    own_donor = slab_feats[:, :slab_sites]
    own_acceptor = slab_feats[:, slab_sites:]

    n_dp = lax.axis_size("dp")
    assert n_dp & (n_dp - 1) == 0 and n_dp >= 2
    dp = lax.axis_index("dp")
    pair = dp % 2
    channels = embed.shape[2]
    half = channels // 2
    part = width // n_seq
    if n_seq == 2:
        target_own = lax.dynamic_slice_in_dim(target, slab * slab_sites, slab_sites, 2)
        scores_own = (
            jnp.einsum("bip,bjp->bij", own_donor, own_acceptor, preferred_element_type=jnp.float32)
            * scale
        )
        allowed_own = (donor_pos[:, :, None] >= 0) & (acceptor_pos[:, None, :] > donor_pos[:, :, None])
        slope_own = pair_slope(scores_own, target_own, allowed_own)
        early_acceptor = (
            jnp.einsum("bij,bip->bjp", slope_own, own_donor, preferred_element_type=jnp.float32) * scale
        ).astype(jnp.bfloat16)
        early_donor = (
            jnp.einsum("bij,bjp->bip", slope_own, own_acceptor, preferred_element_type=jnp.float32)
            * scale
        ).astype(jnp.bfloat16)
        first = slab == 0
        grad_early = jnp.where(first, early_acceptor, early_donor)
        rows_early = jnp.where(first, acceptor_rows, donor_rows)

        def to_seq_partner(rows, grad):
            local = jnp.einsum("bnc,bnp->pc", rows, grad, preferred_element_type=jnp.float32)
            local = local.astype(jnp.bfloat16)
            kept = lax.dynamic_slice_in_dim(local, pair * half, half, 1).astype(jnp.float32)
            outgoing = lax.dynamic_slice_in_dim(local, (1 - pair) * half, half, 1)
            kept = kept + lax.ppermute(outgoing, "dp", [(i, i ^ 1) for i in range(n_dp)]).astype(
                jnp.float32
            )
            held = kept.astype(jnp.bfloat16)
            own = lax.dynamic_slice_in_dim(held, slab * part, part, 0).astype(jnp.float32)
            return own, lax.dynamic_slice_in_dim(held, (1 - slab) * part, part, 0)

        def from_seq_partner(outgoing):
            return lax.ppermute(outgoing, "seq", [(0, 1), (1, 0)]).astype(jnp.float32)

        own_early, out_early = to_seq_partner(rows_early, grad_early)

    assert slab_sites <= width
    flags = jnp.zeros((batch, 8, width), jnp.bfloat16)
    flags = flags.at[:, 0, :slab_sites].set((donor_pos >= 0).astype(jnp.bfloat16))
    flags = flags.at[:, 1, :slab_sites].set((acceptor_pos >= 0).astype(jnp.bfloat16))
    donor_feat_all = jnp.zeros((batch, sites, width), jnp.bfloat16)
    acceptor_feat_all = jnp.zeros((batch, sites, width), jnp.bfloat16)
    donor_feat_all = lax.dynamic_update_slice_in_dim(donor_feat_all, own_donor, slab * slab_sites, 1)
    acceptor_feat_all = lax.dynamic_update_slice_in_dim(
        acceptor_feat_all, own_acceptor, slab * slab_sites, 1
    )
    donor_ok_all = jnp.zeros((batch, sites), jnp.bool_)
    acceptor_ok_all = jnp.zeros((batch, sites), jnp.bool_)
    target_col = jnp.zeros((batch, sites, slab_sites), target.dtype)
    own_cols = lax.dynamic_slice_in_dim(target, slab * slab_sites, slab_sites, 2)
    target_col = lax.dynamic_update_slice_in_dim(target_col, own_cols, slab * slab_sites, 1)
    for k in range(1, n_seq):
        sent = jnp.where(slab + k < n_seq, own_donor, own_acceptor)
        target_block = lax.dynamic_slice_in_dim(
            target, jnp.minimum(slab + k, n_seq - 1) * slab_sites, slab_sites, 2
        ).reshape(batch, slab_sites * slab_sites)
        target_rows = -(-(slab_sites * slab_sites) // width)
        target_block = jnp.pad(target_block, ((0, 0), (0, target_rows * width - slab_sites * slab_sites)))
        payload = jnp.concatenate(
            [sent, flags, target_block.reshape(batch, target_rows, width).astype(jnp.bfloat16)], axis=1
        )
        perm = [(i, (i + k) % n_seq) for i in range(n_seq)]
        arrived = lax.ppermute(payload, "seq", perm)
        source = (slab - k) % n_seq
        earlier = slab >= k
        target_in = (
            arrived[:, slab_sites + 8 :]
            .reshape(batch, target_rows * width)[:, : slab_sites * slab_sites]
            .reshape(batch, slab_sites, slab_sites)
        )
        target_col = jnp.where(
            earlier,
            lax.dynamic_update_slice_in_dim(target_col, target_in, source * slab_sites, 1),
            target_col,
        )
        feat_in = arrived[:, :slab_sites]
        donor_feat_all = jnp.where(
            earlier,
            lax.dynamic_update_slice_in_dim(donor_feat_all, feat_in, source * slab_sites, 1),
            donor_feat_all,
        )
        acceptor_feat_all = jnp.where(
            earlier,
            acceptor_feat_all,
            lax.dynamic_update_slice_in_dim(acceptor_feat_all, feat_in, source * slab_sites, 1),
        )
        donor_in = arrived[:, slab_sites, :slab_sites] > 0
        acceptor_in = arrived[:, slab_sites + 1, :slab_sites] > 0
        donor_ok_all = jnp.where(
            earlier,
            lax.dynamic_update_slice_in_dim(donor_ok_all, donor_in, source * slab_sites, 1),
            donor_ok_all,
        )
        acceptor_ok_all = jnp.where(
            earlier,
            acceptor_ok_all,
            lax.dynamic_update_slice_in_dim(acceptor_ok_all, acceptor_in, source * slab_sites, 1),
        )

    if n_seq == 2:
        out_early, arrived = lax.optimization_barrier((out_early, arrived))
        from_early = from_seq_partner(out_early)

    site_slab = jnp.arange(sites, dtype=jnp.int32) // slab_sites
    big = jnp.int32(1 << 30)
    acceptor_tiled = jnp.tile(acceptor_pos, (1, n_seq))
    acceptor_eff = jnp.where(
        site_slab[None, :] == slab,
        acceptor_tiled,
        jnp.where(
            (site_slab[None, :] > slab) & acceptor_ok_all, (slab + 1) * slab_rows, -1
        ),
    )
    donor_tiled = jnp.tile(donor_pos, (1, n_seq))
    donor_eff = jnp.where(
        site_slab[None, :] == slab,
        donor_tiled,
        jnp.where(
            site_slab[None, :] > slab,
            big,
            jnp.where(donor_ok_all, slab * slab_rows - 1, -1),
        ),
    )

    donor_feat = own_donor
    acceptor_feat = own_acceptor

    scores_row = (
        jnp.einsum("bip,bjp->bij", donor_feat, acceptor_feat_all, preferred_element_type=jnp.float32)
        * scale
    )
    allowed_row = (donor_pos[:, :, None] >= 0) & (acceptor_eff[:, None, :] > donor_pos[:, :, None])
    slope_row = pair_slope(scores_row, target, allowed_row)
    donor_grad = (
        jnp.einsum("bij,bjp->bip", slope_row, acceptor_feat_all, preferred_element_type=jnp.float32)
        * scale
    ).astype(jnp.bfloat16)

    scores_col = (
        jnp.einsum("bip,bjp->bij", donor_feat_all, acceptor_feat, preferred_element_type=jnp.float32)
        * scale
    )
    allowed_col = (donor_eff[:, :, None] >= 0) & (acceptor_pos[:, None, :] > donor_eff[:, :, None])
    slope_col = pair_slope(scores_col, target_col, allowed_col)
    acceptor_grad = (
        jnp.einsum("bij,bip->bjp", slope_col, donor_feat_all, preferred_element_type=jnp.float32)
        * scale
    ).astype(jnp.bfloat16)


    if n_seq == 2:
        first = slab == 0
        grad_early = jnp.where(first, early_acceptor, early_donor)
        rows_early = jnp.where(first, acceptor_rows, donor_rows)
        grad_late = jnp.where(first, donor_grad, acceptor_grad)
        rows_late = jnp.where(first, donor_rows, acceptor_rows)
        donor_grad = jnp.where(first, grad_late, grad_early)
        acceptor_grad = jnp.where(first, grad_early, grad_late)

        own_late, out_late = to_seq_partner(rows_late, grad_late)
        from_late = from_seq_partner(out_late)
        sum_early = own_early + from_late
        sum_late = own_late + from_early
        mine = jnp.stack(
            [jnp.where(first, sum_late, sum_early), jnp.where(first, sum_early, sum_late)]
        )
    else:
        local_dw = jnp.einsum(
            "bnc,bnp->pc", donor_rows, donor_grad, preferred_element_type=jnp.float32
        )
        local_aw = jnp.einsum(
            "bnc,bnp->pc", acceptor_rows, acceptor_grad, preferred_element_type=jnp.float32
        )
        blocks = jnp.stack([local_dw, local_aw]).astype(jnp.bfloat16)
        mine = lax.dynamic_slice_in_dim(blocks, pair * half, half, 2).astype(jnp.float32)
        outgoing = lax.dynamic_slice_in_dim(blocks, (1 - pair) * half, half, 2)
        mine = mine + lax.ppermute(outgoing, "dp", [(i, i ^ 1) for i in range(n_dp)]).astype(
            jnp.float32
        )
        held = mine.astype(jnp.bfloat16)
        mine = lax.dynamic_slice_in_dim(held, slab * part, part, 1).astype(jnp.float32)
        for k in range(1, n_seq):
            outgoing = lax.dynamic_slice_in_dim(held, ((slab + k) % n_seq) * part, part, 1)
            perm = [(i, (i + k) % n_seq) for i in range(n_seq)]
            mine = mine + lax.ppermute(outgoing, "seq", perm).astype(jnp.float32)
    donor_site = jnp.einsum("bnp,cp->bnc", donor_grad, donor_w, preferred_element_type=jnp.float32)
    acceptor_site = jnp.einsum(
        "bnp,cp->bnc", acceptor_grad, acceptor_w, preferred_element_type=jnp.float32
    )
    row_grad = place_rows(donor_match, donor_site) + place_rows(acceptor_match, acceptor_site)
    bit = 2
    while bit < n_dp:
        held = mine.astype(jnp.bfloat16)
        perm = [(i, i ^ bit) for i in range(n_dp)]
        received = lax.ppermute(held, "dp", perm)
        if bit == 2:
            received, row_grad = lax.optimization_barrier((received, row_grad))
        mine = held.astype(jnp.float32) + received.astype(jnp.float32)
        bit *= 2
    other = lax.ppermute(mine, "dp", [(i, i ^ 1) for i in range(n_dp)])
    mine = jnp.where(pair == 0, jnp.concatenate([mine, other], 2), jnp.concatenate([other, mine], 2))
    mine = jnp.swapaxes(mine, 1, 2)
    column_major = Layout(major_to_minor=(1, 0))
    grad_dw = with_layout_constraint(mine[0], column_major)
    grad_aw = with_layout_constraint(mine[1], column_major)
    return (row_grad.astype(jnp.bfloat16), grad_dw, grad_aw)


def solution(mesh):
    in_specs = (
        P("dp", "seq", "head"),
        P("dp", "seq"),
        P("dp", "seq"),
        P("dp", "seq", None),
        P("head", None),
        P("head", None),
    )
    out_specs = (P("dp", "seq", "head"), P("head", "seq"), P("head", "seq"))
    return jax.shard_map(shards, mesh=mesh, in_specs=in_specs, out_specs=out_specs, check_vma=False)
```

```python
import math

import jax
import jax.numpy as jnp
from jax import lax
from jax.experimental.layout import Layout, with_layout_constraint
from jax.sharding import PartitionSpec as P


def site_match(positions, slab_rows, slab_index):
    local_pos = positions - slab_index * slab_rows
    return local_pos[:, :, None] == jnp.arange(slab_rows, dtype=jnp.int32)[None, None, :]


def pair_slope(scores, target, allowed):
    rate = jax.nn.softplus(scores) + 1.0
    return jnp.where(
        allowed, (1.0 - target.astype(jnp.float32) / rate) * jax.nn.sigmoid(scores), 0.0
    ).astype(jnp.bfloat16)


def place_rows(match_bf, values):
    upper = values.astype(jnp.bfloat16)
    lower = (values - upper.astype(jnp.float32)).astype(jnp.bfloat16)
    placed = jnp.einsum("bnr,bnc->brc", match_bf, upper, preferred_element_type=jnp.float32)
    return placed + jnp.einsum("bnr,bnc->brc", match_bf, lower, preferred_element_type=jnp.float32)


def gather_by_permute(x, axes, count, me):
    pieces = [x]
    for k in range(1, count):
        perm = [(i, (i + k) % count) for i in range(count)]
        pieces.append(lax.ppermute(x, axes, perm))
    by_offset = jnp.stack(pieces)
    order = (me - jnp.arange(count, dtype=jnp.int32)) % count
    return jnp.take(by_offset, order, axis=0)


def shards(embed, donor_pos, acceptor_pos, target, donor_w, acceptor_w):
    batch, slab_rows, _ = embed.shape
    slab_sites = donor_pos.shape[1]
    width = donor_w.shape[1]
    scale = 1.0 / math.sqrt(width)
    n_seq = lax.axis_size("seq")
    n_head = lax.axis_size("head")
    slab = lax.axis_index("seq")
    sites = slab_sites * n_seq

    head = lax.axis_index("head")
    me = slab * n_head + head

    donor_match = site_match(donor_pos, slab_rows, slab).astype(jnp.bfloat16)
    acceptor_match = site_match(acceptor_pos, slab_rows, slab).astype(jnp.bfloat16)
    donor_rows = jnp.einsum(
        "bnr,brc->bnc", donor_match, embed, preferred_element_type=jnp.float32
    ).astype(jnp.bfloat16)
    acceptor_rows = jnp.einsum(
        "bnr,brc->bnc", acceptor_match, embed, preferred_element_type=jnp.float32
    ).astype(jnp.bfloat16)
    donor_part = jnp.einsum(
        "bnc,cp->bnp", donor_rows, donor_w, preferred_element_type=jnp.float32
    ).astype(jnp.bfloat16)
    acceptor_part = jnp.einsum(
        "bnc,cp->bnp", acceptor_rows, acceptor_w, preferred_element_type=jnp.float32
    ).astype(jnp.bfloat16)

    both = 2 * slab_sites
    assert both % n_head == 0
    quarter = both // n_head
    parts = jnp.concatenate([donor_part, acceptor_part], axis=1)
    assert n_head & (n_head - 1) == 0
    pieces = [lax.dynamic_slice_in_dim(parts, head * quarter, quarter, 1)]
    for k in range(1, n_head):
        outgoing = lax.dynamic_slice_in_dim(parts, (head ^ k) * quarter, quarter, 1)
        pieces.append(lax.ppermute(outgoing, "head", [(i, i ^ k) for i in range(n_head)]))
    by_partner = jnp.stack(pieces)
    by_head = jnp.take(by_partner, head ^ jnp.arange(n_head, dtype=jnp.int32), axis=0)
    total = jnp.zeros((batch, quarter, width), jnp.float32)
    for h in range(n_head):
        total = total + by_head[h].astype(jnp.float32)
    feat_quarter = total.astype(jnp.bfloat16)

    pieces = [feat_quarter]
    for k in range(1, n_head):
        pieces.append(lax.ppermute(feat_quarter, "head", [(i, i ^ k) for i in range(n_head)]))
    slab_feats = jnp.take(jnp.stack(pieces), head ^ jnp.arange(n_head, dtype=jnp.int32), axis=0)
    slab_feats = jnp.moveaxis(slab_feats, 0, 1).reshape(batch, both, width)
    own_donor = slab_feats[:, :slab_sites]
    own_acceptor = slab_feats[:, slab_sites:]

    n_dp = lax.axis_size("dp")
    assert n_dp & (n_dp - 1) == 0 and n_dp >= 2
    dp = lax.axis_index("dp")
    pair = dp % 2
    channels = embed.shape[2]
    half = channels // 2
    part = width // n_seq
    if n_seq == 2:
        target_own = lax.dynamic_slice_in_dim(target, slab * slab_sites, slab_sites, 2)
        scores_own = (
            jnp.einsum("bip,bjp->bij", own_donor, own_acceptor, preferred_element_type=jnp.float32)
            * scale
        )
        allowed_own = (donor_pos[:, :, None] >= 0) & (acceptor_pos[:, None, :] > donor_pos[:, :, None])
        slope_own = pair_slope(scores_own, target_own, allowed_own)
        early_acceptor = (
            jnp.einsum("bij,bip->bjp", slope_own, own_donor, preferred_element_type=jnp.float32) * scale
        ).astype(jnp.bfloat16)
        early_donor = (
            jnp.einsum("bij,bjp->bip", slope_own, own_acceptor, preferred_element_type=jnp.float32)
            * scale
        ).astype(jnp.bfloat16)
        first = slab == 0
        grad_early = jnp.where(first, early_acceptor, early_donor)
        rows_early = jnp.where(first, acceptor_rows, donor_rows)

        def to_seq_partner(rows, grad):
            local = jnp.einsum("bnc,bnp->pc", rows, grad, preferred_element_type=jnp.float32)
            local = local.astype(jnp.bfloat16)
            kept = lax.dynamic_slice_in_dim(local, pair * half, half, 1).astype(jnp.float32)
            outgoing = lax.dynamic_slice_in_dim(local, (1 - pair) * half, half, 1)
            kept = kept + lax.ppermute(outgoing, "dp", [(i, i ^ 1) for i in range(n_dp)]).astype(
                jnp.float32
            )
            held = kept.astype(jnp.bfloat16)
            own = lax.dynamic_slice_in_dim(held, slab * part, part, 0).astype(jnp.float32)
            return own, lax.dynamic_slice_in_dim(held, (1 - slab) * part, part, 0)

        def from_seq_partner(outgoing):
            return lax.ppermute(outgoing, "seq", [(0, 1), (1, 0)]).astype(jnp.float32)

        own_early, out_early = to_seq_partner(rows_early, grad_early)

    assert slab_sites <= width
    flags = jnp.zeros((batch, 8, width), jnp.bfloat16)
    flags = flags.at[:, 0, :slab_sites].set((donor_pos >= 0).astype(jnp.bfloat16))
    flags = flags.at[:, 1, :slab_sites].set((acceptor_pos >= 0).astype(jnp.bfloat16))
    donor_feat_all = jnp.zeros((batch, sites, width), jnp.bfloat16)
    acceptor_feat_all = jnp.zeros((batch, sites, width), jnp.bfloat16)
    donor_feat_all = lax.dynamic_update_slice_in_dim(donor_feat_all, own_donor, slab * slab_sites, 1)
    acceptor_feat_all = lax.dynamic_update_slice_in_dim(
        acceptor_feat_all, own_acceptor, slab * slab_sites, 1
    )
    donor_ok_all = jnp.zeros((batch, sites), jnp.bool_)
    acceptor_ok_all = jnp.zeros((batch, sites), jnp.bool_)
    target_col = jnp.zeros((batch, sites, slab_sites), target.dtype)
    own_cols = lax.dynamic_slice_in_dim(target, slab * slab_sites, slab_sites, 2)
    target_col = lax.dynamic_update_slice_in_dim(target_col, own_cols, slab * slab_sites, 1)
    for k in range(1, n_seq):
        sent = jnp.where(slab + k < n_seq, own_donor, own_acceptor)
        target_block = lax.dynamic_slice_in_dim(
            target, jnp.minimum(slab + k, n_seq - 1) * slab_sites, slab_sites, 2
        ).reshape(batch, slab_sites * slab_sites)
        target_rows = -(-(slab_sites * slab_sites) // width)
        target_block = jnp.pad(target_block, ((0, 0), (0, target_rows * width - slab_sites * slab_sites)))
        payload = jnp.concatenate(
            [sent, flags, target_block.reshape(batch, target_rows, width).astype(jnp.bfloat16)], axis=1
        )
        perm = [(i, (i + k) % n_seq) for i in range(n_seq)]
        arrived = lax.ppermute(payload, "seq", perm)
        source = (slab - k) % n_seq
        earlier = slab >= k
        target_in = (
            arrived[:, slab_sites + 8 :]
            .reshape(batch, target_rows * width)[:, : slab_sites * slab_sites]
            .reshape(batch, slab_sites, slab_sites)
        )
        target_col = jnp.where(
            earlier,
            lax.dynamic_update_slice_in_dim(target_col, target_in, source * slab_sites, 1),
            target_col,
        )
        feat_in = arrived[:, :slab_sites]
        donor_feat_all = jnp.where(
            earlier,
            lax.dynamic_update_slice_in_dim(donor_feat_all, feat_in, source * slab_sites, 1),
            donor_feat_all,
        )
        acceptor_feat_all = jnp.where(
            earlier,
            acceptor_feat_all,
            lax.dynamic_update_slice_in_dim(acceptor_feat_all, feat_in, source * slab_sites, 1),
        )
        donor_in = arrived[:, slab_sites, :slab_sites] > 0
        acceptor_in = arrived[:, slab_sites + 1, :slab_sites] > 0
        donor_ok_all = jnp.where(
            earlier,
            lax.dynamic_update_slice_in_dim(donor_ok_all, donor_in, source * slab_sites, 1),
            donor_ok_all,
        )
        acceptor_ok_all = jnp.where(
            earlier,
            acceptor_ok_all,
            lax.dynamic_update_slice_in_dim(acceptor_ok_all, acceptor_in, source * slab_sites, 1),
        )

    if n_seq == 2:
        out_early, arrived = lax.optimization_barrier((out_early, arrived))
        from_early = from_seq_partner(out_early)

    site_slab = jnp.arange(sites, dtype=jnp.int32) // slab_sites
    big = jnp.int32(1 << 30)
    acceptor_tiled = jnp.tile(acceptor_pos, (1, n_seq))
    acceptor_eff = jnp.where(
        site_slab[None, :] == slab,
        acceptor_tiled,
        jnp.where(
            (site_slab[None, :] > slab) & acceptor_ok_all, (slab + 1) * slab_rows, -1
        ),
    )
    donor_tiled = jnp.tile(donor_pos, (1, n_seq))
    donor_eff = jnp.where(
        site_slab[None, :] == slab,
        donor_tiled,
        jnp.where(
            site_slab[None, :] > slab,
            big,
            jnp.where(donor_ok_all, slab * slab_rows - 1, -1),
        ),
    )

    donor_feat = own_donor
    acceptor_feat = own_acceptor

    if n_seq == 2:
        first = slab == 0
        queries = jnp.where(first, own_donor, own_acceptor)
        keys = jnp.where(first, acceptor_feat_all, donor_feat_all)
        scores_late = (
            jnp.einsum("bip,bjp->bij", queries, keys, preferred_element_type=jnp.float32) * scale
        )
        allowed_row = (donor_pos[:, :, None] >= 0) & (acceptor_eff[:, None, :] > donor_pos[:, :, None])
        allowed_col = (donor_eff[:, None, :] >= 0) & (acceptor_pos[:, :, None] > donor_eff[:, None, :])
        allowed_late = jnp.where(first, allowed_row, allowed_col)
        target_late = jnp.where(first, target, jnp.swapaxes(target_col, 1, 2))
        slope_late = pair_slope(scores_late, target_late, allowed_late)
        grad_late = (
            jnp.einsum("bij,bjp->bip", slope_late, keys, preferred_element_type=jnp.float32) * scale
        ).astype(jnp.bfloat16)
    else:
        scores_row = (
            jnp.einsum("bip,bjp->bij", donor_feat, acceptor_feat_all, preferred_element_type=jnp.float32)
            * scale
        )
        allowed_row = (donor_pos[:, :, None] >= 0) & (acceptor_eff[:, None, :] > donor_pos[:, :, None])
        slope_row = pair_slope(scores_row, target, allowed_row)
        donor_grad = (
            jnp.einsum("bij,bjp->bip", slope_row, acceptor_feat_all, preferred_element_type=jnp.float32)
            * scale
        ).astype(jnp.bfloat16)

        scores_col = (
            jnp.einsum("bip,bjp->bij", donor_feat_all, acceptor_feat, preferred_element_type=jnp.float32)
            * scale
        )
        allowed_col = (donor_eff[:, :, None] >= 0) & (acceptor_pos[:, None, :] > donor_eff[:, :, None])
        slope_col = pair_slope(scores_col, target_col, allowed_col)
        acceptor_grad = (
            jnp.einsum("bij,bip->bjp", slope_col, donor_feat_all, preferred_element_type=jnp.float32)
            * scale
        ).astype(jnp.bfloat16)

    if n_seq == 2:
        grad_early = jnp.where(first, early_acceptor, early_donor)
        rows_early = jnp.where(first, acceptor_rows, donor_rows)
        rows_late = jnp.where(first, donor_rows, acceptor_rows)
        donor_grad = jnp.where(first, grad_late, grad_early)
        acceptor_grad = jnp.where(first, grad_early, grad_late)

        own_late, out_late = to_seq_partner(rows_late, grad_late)
        from_late = from_seq_partner(out_late)
        sum_early = own_early + from_late
        sum_late = own_late + from_early
        mine = jnp.stack(
            [jnp.where(first, sum_late, sum_early), jnp.where(first, sum_early, sum_late)]
        )
    else:
        local_dw = jnp.einsum(
            "bnc,bnp->pc", donor_rows, donor_grad, preferred_element_type=jnp.float32
        )
        local_aw = jnp.einsum(
            "bnc,bnp->pc", acceptor_rows, acceptor_grad, preferred_element_type=jnp.float32
        )
        blocks = jnp.stack([local_dw, local_aw]).astype(jnp.bfloat16)
        mine = lax.dynamic_slice_in_dim(blocks, pair * half, half, 2).astype(jnp.float32)
        outgoing = lax.dynamic_slice_in_dim(blocks, (1 - pair) * half, half, 2)
        mine = mine + lax.ppermute(outgoing, "dp", [(i, i ^ 1) for i in range(n_dp)]).astype(
            jnp.float32
        )
        held = mine.astype(jnp.bfloat16)
        mine = lax.dynamic_slice_in_dim(held, slab * part, part, 1).astype(jnp.float32)
        for k in range(1, n_seq):
            outgoing = lax.dynamic_slice_in_dim(held, ((slab + k) % n_seq) * part, part, 1)
            perm = [(i, (i + k) % n_seq) for i in range(n_seq)]
            mine = mine + lax.ppermute(outgoing, "seq", perm).astype(jnp.float32)
    donor_site = jnp.einsum("bnp,cp->bnc", donor_grad, donor_w, preferred_element_type=jnp.float32)
    acceptor_site = jnp.einsum(
        "bnp,cp->bnc", acceptor_grad, acceptor_w, preferred_element_type=jnp.float32
    )
    row_grad = place_rows(donor_match, donor_site) + place_rows(acceptor_match, acceptor_site)
    bit = 2
    while bit < n_dp:
        held = mine.astype(jnp.bfloat16)
        perm = [(i, i ^ bit) for i in range(n_dp)]
        mine = held.astype(jnp.float32) + lax.ppermute(held, "dp", perm).astype(jnp.float32)
        bit *= 2
    other = lax.ppermute(mine, "dp", [(i, i ^ 1) for i in range(n_dp)])
    mine = jnp.where(pair == 0, jnp.concatenate([mine, other], 2), jnp.concatenate([other, mine], 2))
    mine = jnp.swapaxes(mine, 1, 2)
    column_major = Layout(major_to_minor=(1, 0))
    grad_dw = with_layout_constraint(mine[0], column_major)
    grad_aw = with_layout_constraint(mine[1], column_major)
    return (row_grad.astype(jnp.bfloat16), grad_dw, grad_aw)


def solution(mesh):
    in_specs = (
        P("dp", "seq", "head"),
        P("dp", "seq"),
        P("dp", "seq"),
        P("dp", "seq", None),
        P("head", None),
        P("head", None),
    )
    out_specs = (P("dp", "seq", "head"), P("head", "seq"), P("head", "seq"))
    return jax.shard_map(shards, mesh=mesh, in_specs=in_specs, out_specs=out_specs, check_vma=False)
```

```python
import math

import jax
import jax.numpy as jnp
from jax import lax
from jax.experimental.layout import Layout, with_layout_constraint
from jax.sharding import PartitionSpec as P


def site_match(positions, slab_rows, slab_index):
    local_pos = positions - slab_index * slab_rows
    return local_pos[:, :, None] == jnp.arange(slab_rows, dtype=jnp.int32)[None, None, :]


def pair_slope(scores, target, allowed):
    rate = jax.nn.softplus(scores) + 1.0
    return jnp.where(
        allowed, (1.0 - target.astype(jnp.float32) / rate) * jax.nn.sigmoid(scores), 0.0
    ).astype(jnp.bfloat16)


def place_rows(match_bf, values):
    upper = values.astype(jnp.bfloat16)
    lower = (values - upper.astype(jnp.float32)).astype(jnp.bfloat16)
    placed = jnp.einsum("bnr,bnc->brc", match_bf, upper, preferred_element_type=jnp.float32)
    return placed + jnp.einsum("bnr,bnc->brc", match_bf, lower, preferred_element_type=jnp.float32)


def gather_by_permute(x, axes, count, me):
    pieces = [x]
    for k in range(1, count):
        perm = [(i, (i + k) % count) for i in range(count)]
        pieces.append(lax.ppermute(x, axes, perm))
    by_offset = jnp.stack(pieces)
    order = (me - jnp.arange(count, dtype=jnp.int32)) % count
    return jnp.take(by_offset, order, axis=0)


def shards(embed, donor_pos, acceptor_pos, target, donor_w, acceptor_w):
    batch, slab_rows, _ = embed.shape
    slab_sites = donor_pos.shape[1]
    width = donor_w.shape[1]
    scale = 1.0 / math.sqrt(width)
    n_seq = lax.axis_size("seq")
    n_head = lax.axis_size("head")
    slab = lax.axis_index("seq")
    sites = slab_sites * n_seq

    head = lax.axis_index("head")
    me = slab * n_head + head

    donor_match = site_match(donor_pos, slab_rows, slab).astype(jnp.bfloat16)
    acceptor_match = site_match(acceptor_pos, slab_rows, slab).astype(jnp.bfloat16)
    donor_rows = jnp.einsum(
        "bnr,brc->bnc", donor_match, embed, preferred_element_type=jnp.float32
    ).astype(jnp.bfloat16)
    acceptor_rows = jnp.einsum(
        "bnr,brc->bnc", acceptor_match, embed, preferred_element_type=jnp.float32
    ).astype(jnp.bfloat16)
    donor_part = jnp.einsum(
        "bnc,cp->bnp", donor_rows, donor_w, preferred_element_type=jnp.float32
    ).astype(jnp.bfloat16)
    acceptor_part = jnp.einsum(
        "bnc,cp->bnp", acceptor_rows, acceptor_w, preferred_element_type=jnp.float32
    ).astype(jnp.bfloat16)

    both = 2 * slab_sites
    assert both % n_head == 0
    quarter = both // n_head
    parts = jnp.concatenate([donor_part, acceptor_part], axis=1)
    assert n_head & (n_head - 1) == 0
    pieces = [lax.dynamic_slice_in_dim(parts, head * quarter, quarter, 1)]
    for k in range(1, n_head):
        outgoing = lax.dynamic_slice_in_dim(parts, (head ^ k) * quarter, quarter, 1)
        pieces.append(lax.ppermute(outgoing, "head", [(i, i ^ k) for i in range(n_head)]))
    by_partner = jnp.stack(pieces)
    by_head = jnp.take(by_partner, head ^ jnp.arange(n_head, dtype=jnp.int32), axis=0)
    total = jnp.zeros((batch, quarter, width), jnp.float32)
    for h in range(n_head):
        total = total + by_head[h].astype(jnp.float32)
    feat_quarter = total.astype(jnp.bfloat16)

    pieces = [feat_quarter]
    for k in range(1, n_head):
        pieces.append(lax.ppermute(feat_quarter, "head", [(i, i ^ k) for i in range(n_head)]))
    slab_feats = jnp.take(jnp.stack(pieces), head ^ jnp.arange(n_head, dtype=jnp.int32), axis=0)
    slab_feats = jnp.moveaxis(slab_feats, 0, 1).reshape(batch, both, width)
    own_donor = slab_feats[:, :slab_sites]
    own_acceptor = slab_feats[:, slab_sites:]

    n_dp = lax.axis_size("dp")
    assert n_dp & (n_dp - 1) == 0 and n_dp >= 2
    dp = lax.axis_index("dp")
    pair = dp % 2
    channels = embed.shape[2]
    half = channels // 2
    part = width // n_seq
    def over_dp_bits(value):
        bit = 2
        while bit < n_dp:
            held = value.astype(jnp.bfloat16)
            perm = [(i, i ^ bit) for i in range(n_dp)]
            value = held.astype(jnp.float32) + lax.ppermute(held, "dp", perm).astype(jnp.float32)
            bit *= 2
        return value

    if n_seq == 2:
        target_own = lax.dynamic_slice_in_dim(target, slab * slab_sites, slab_sites, 2)
        scores_own = (
            jnp.einsum("bip,bjp->bij", own_donor, own_acceptor, preferred_element_type=jnp.float32)
            * scale
        )
        allowed_own = (donor_pos[:, :, None] >= 0) & (acceptor_pos[:, None, :] > donor_pos[:, :, None])
        slope_own = pair_slope(scores_own, target_own, allowed_own)
        early_acceptor = (
            jnp.einsum("bij,bip->bjp", slope_own, own_donor, preferred_element_type=jnp.float32) * scale
        ).astype(jnp.bfloat16)
        early_donor = (
            jnp.einsum("bij,bjp->bip", slope_own, own_acceptor, preferred_element_type=jnp.float32)
            * scale
        ).astype(jnp.bfloat16)
        first = slab == 0
        grad_early = jnp.where(first, early_acceptor, early_donor)
        rows_early = jnp.where(first, acceptor_rows, donor_rows)

        def to_seq_partner(rows, grad):
            local = jnp.einsum("bnc,bnp->pc", rows, grad, preferred_element_type=jnp.float32)
            local = local.astype(jnp.bfloat16)
            kept = lax.dynamic_slice_in_dim(local, pair * half, half, 1).astype(jnp.float32)
            outgoing = lax.dynamic_slice_in_dim(local, (1 - pair) * half, half, 1)
            kept = kept + lax.ppermute(outgoing, "dp", [(i, i ^ 1) for i in range(n_dp)]).astype(
                jnp.float32
            )
            held = kept.astype(jnp.bfloat16)
            own = lax.dynamic_slice_in_dim(held, slab * part, part, 0).astype(jnp.float32)
            return own, lax.dynamic_slice_in_dim(held, (1 - slab) * part, part, 0)

        def from_seq_partner(outgoing):
            return lax.ppermute(outgoing, "seq", [(0, 1), (1, 0)]).astype(jnp.float32)

        own_early, out_early = to_seq_partner(rows_early, grad_early)

    assert slab_sites <= width
    flags = jnp.zeros((batch, 8, width), jnp.bfloat16)
    flags = flags.at[:, 0, :slab_sites].set((donor_pos >= 0).astype(jnp.bfloat16))
    flags = flags.at[:, 1, :slab_sites].set((acceptor_pos >= 0).astype(jnp.bfloat16))
    donor_feat_all = jnp.zeros((batch, sites, width), jnp.bfloat16)
    acceptor_feat_all = jnp.zeros((batch, sites, width), jnp.bfloat16)
    donor_feat_all = lax.dynamic_update_slice_in_dim(donor_feat_all, own_donor, slab * slab_sites, 1)
    acceptor_feat_all = lax.dynamic_update_slice_in_dim(
        acceptor_feat_all, own_acceptor, slab * slab_sites, 1
    )
    donor_ok_all = jnp.zeros((batch, sites), jnp.bool_)
    acceptor_ok_all = jnp.zeros((batch, sites), jnp.bool_)
    target_col = jnp.zeros((batch, sites, slab_sites), target.dtype)
    own_cols = lax.dynamic_slice_in_dim(target, slab * slab_sites, slab_sites, 2)
    target_col = lax.dynamic_update_slice_in_dim(target_col, own_cols, slab * slab_sites, 1)
    for k in range(1, n_seq):
        sent = jnp.where(slab + k < n_seq, own_donor, own_acceptor)
        target_block = lax.dynamic_slice_in_dim(
            target, jnp.minimum(slab + k, n_seq - 1) * slab_sites, slab_sites, 2
        ).reshape(batch, slab_sites * slab_sites)
        target_rows = -(-(slab_sites * slab_sites) // width)
        target_block = jnp.pad(target_block, ((0, 0), (0, target_rows * width - slab_sites * slab_sites)))
        payload = jnp.concatenate(
            [sent, flags, target_block.reshape(batch, target_rows, width).astype(jnp.bfloat16)], axis=1
        )
        perm = [(i, (i + k) % n_seq) for i in range(n_seq)]
        arrived = lax.ppermute(payload, "seq", perm)
        source = (slab - k) % n_seq
        earlier = slab >= k
        target_in = (
            arrived[:, slab_sites + 8 :]
            .reshape(batch, target_rows * width)[:, : slab_sites * slab_sites]
            .reshape(batch, slab_sites, slab_sites)
        )
        target_col = jnp.where(
            earlier,
            lax.dynamic_update_slice_in_dim(target_col, target_in, source * slab_sites, 1),
            target_col,
        )
        feat_in = arrived[:, :slab_sites]
        donor_feat_all = jnp.where(
            earlier,
            lax.dynamic_update_slice_in_dim(donor_feat_all, feat_in, source * slab_sites, 1),
            donor_feat_all,
        )
        acceptor_feat_all = jnp.where(
            earlier,
            acceptor_feat_all,
            lax.dynamic_update_slice_in_dim(acceptor_feat_all, feat_in, source * slab_sites, 1),
        )
        donor_in = arrived[:, slab_sites, :slab_sites] > 0
        acceptor_in = arrived[:, slab_sites + 1, :slab_sites] > 0
        donor_ok_all = jnp.where(
            earlier,
            lax.dynamic_update_slice_in_dim(donor_ok_all, donor_in, source * slab_sites, 1),
            donor_ok_all,
        )
        acceptor_ok_all = jnp.where(
            earlier,
            acceptor_ok_all,
            lax.dynamic_update_slice_in_dim(acceptor_ok_all, acceptor_in, source * slab_sites, 1),
        )

    if n_seq == 2:
        out_early, arrived = lax.optimization_barrier((out_early, arrived))
        from_early = from_seq_partner(out_early)

    site_slab = jnp.arange(sites, dtype=jnp.int32) // slab_sites
    big = jnp.int32(1 << 30)
    acceptor_tiled = jnp.tile(acceptor_pos, (1, n_seq))
    acceptor_eff = jnp.where(
        site_slab[None, :] == slab,
        acceptor_tiled,
        jnp.where(
            (site_slab[None, :] > slab) & acceptor_ok_all, (slab + 1) * slab_rows, -1
        ),
    )
    donor_tiled = jnp.tile(donor_pos, (1, n_seq))
    donor_eff = jnp.where(
        site_slab[None, :] == slab,
        donor_tiled,
        jnp.where(
            site_slab[None, :] > slab,
            big,
            jnp.where(donor_ok_all, slab * slab_rows - 1, -1),
        ),
    )

    donor_feat = own_donor
    acceptor_feat = own_acceptor

    if n_seq == 2:
        first = slab == 0
        queries = jnp.where(first, own_donor, own_acceptor)
        keys = jnp.where(first, acceptor_feat_all, donor_feat_all)
        scores_late = (
            jnp.einsum("bip,bjp->bij", queries, keys, preferred_element_type=jnp.float32) * scale
        )
        allowed_row = (donor_pos[:, :, None] >= 0) & (acceptor_eff[:, None, :] > donor_pos[:, :, None])
        allowed_col = (donor_eff[:, None, :] >= 0) & (acceptor_pos[:, :, None] > donor_eff[:, None, :])
        allowed_late = jnp.where(first, allowed_row, allowed_col)
        target_late = jnp.where(first, target, jnp.swapaxes(target_col, 1, 2))
        slope_late = pair_slope(scores_late, target_late, allowed_late)
        grad_late = (
            jnp.einsum("bij,bjp->bip", slope_late, keys, preferred_element_type=jnp.float32) * scale
        ).astype(jnp.bfloat16)
    else:
        scores_row = (
            jnp.einsum("bip,bjp->bij", donor_feat, acceptor_feat_all, preferred_element_type=jnp.float32)
            * scale
        )
        allowed_row = (donor_pos[:, :, None] >= 0) & (acceptor_eff[:, None, :] > donor_pos[:, :, None])
        slope_row = pair_slope(scores_row, target, allowed_row)
        donor_grad = (
            jnp.einsum("bij,bjp->bip", slope_row, acceptor_feat_all, preferred_element_type=jnp.float32)
            * scale
        ).astype(jnp.bfloat16)

        scores_col = (
            jnp.einsum("bip,bjp->bij", donor_feat_all, acceptor_feat, preferred_element_type=jnp.float32)
            * scale
        )
        allowed_col = (donor_eff[:, :, None] >= 0) & (acceptor_pos[:, None, :] > donor_eff[:, :, None])
        slope_col = pair_slope(scores_col, target_col, allowed_col)
        acceptor_grad = (
            jnp.einsum("bij,bip->bjp", slope_col, donor_feat_all, preferred_element_type=jnp.float32)
            * scale
        ).astype(jnp.bfloat16)

    if n_seq == 2:
        grad_early = jnp.where(first, early_acceptor, early_donor)
        rows_early = jnp.where(first, acceptor_rows, donor_rows)
        rows_late = jnp.where(first, donor_rows, acceptor_rows)
        donor_grad = jnp.where(first, grad_late, grad_early)
        acceptor_grad = jnp.where(first, grad_early, grad_late)

        own_late, out_late = to_seq_partner(rows_late, grad_late)
        from_late = from_seq_partner(out_late)
        sum_early = own_early + from_late
        sum_late = own_late + from_early
        sum_late = over_dp_bits(sum_late)
        sum_early = over_dp_bits(sum_early)
        mine = jnp.stack(
            [jnp.where(first, sum_late, sum_early), jnp.where(first, sum_early, sum_late)]
        )
    else:
        local_dw = jnp.einsum(
            "bnc,bnp->pc", donor_rows, donor_grad, preferred_element_type=jnp.float32
        )
        local_aw = jnp.einsum(
            "bnc,bnp->pc", acceptor_rows, acceptor_grad, preferred_element_type=jnp.float32
        )
        blocks = jnp.stack([local_dw, local_aw]).astype(jnp.bfloat16)
        mine = lax.dynamic_slice_in_dim(blocks, pair * half, half, 2).astype(jnp.float32)
        outgoing = lax.dynamic_slice_in_dim(blocks, (1 - pair) * half, half, 2)
        mine = mine + lax.ppermute(outgoing, "dp", [(i, i ^ 1) for i in range(n_dp)]).astype(
            jnp.float32
        )
        held = mine.astype(jnp.bfloat16)
        mine = lax.dynamic_slice_in_dim(held, slab * part, part, 1).astype(jnp.float32)
        for k in range(1, n_seq):
            outgoing = lax.dynamic_slice_in_dim(held, ((slab + k) % n_seq) * part, part, 1)
            perm = [(i, (i + k) % n_seq) for i in range(n_seq)]
            mine = mine + lax.ppermute(outgoing, "seq", perm).astype(jnp.float32)
    donor_site = jnp.einsum("bnp,cp->bnc", donor_grad, donor_w, preferred_element_type=jnp.float32)
    acceptor_site = jnp.einsum(
        "bnp,cp->bnc", acceptor_grad, acceptor_w, preferred_element_type=jnp.float32
    )
    row_grad = place_rows(donor_match, donor_site) + place_rows(acceptor_match, acceptor_site)
    if n_seq != 2:
        mine = over_dp_bits(mine)
    other = lax.ppermute(mine, "dp", [(i, i ^ 1) for i in range(n_dp)])
    mine = jnp.where(pair == 0, jnp.concatenate([mine, other], 2), jnp.concatenate([other, mine], 2))
    mine = jnp.swapaxes(mine, 1, 2)
    column_major = Layout(major_to_minor=(1, 0))
    grad_dw = with_layout_constraint(mine[0], column_major)
    grad_aw = with_layout_constraint(mine[1], column_major)
    return (row_grad.astype(jnp.bfloat16), grad_dw, grad_aw)


def solution(mesh):
    in_specs = (
        P("dp", "seq", "head"),
        P("dp", "seq"),
        P("dp", "seq"),
        P("dp", "seq", None),
        P("head", None),
        P("head", None),
    )
    out_specs = (P("dp", "seq", "head"), P("head", "seq"), P("head", "seq"))
    return jax.shard_map(shards, mesh=mesh, in_specs=in_specs, out_specs=out_specs, check_vma=False)
```

```python
import math

import jax
import jax.numpy as jnp
from jax import lax
from jax.experimental.layout import Layout, with_layout_constraint
from jax.sharding import PartitionSpec as P


def site_match(positions, slab_rows, slab_index):
    local_pos = positions - slab_index * slab_rows
    return local_pos[:, :, None] == jnp.arange(slab_rows, dtype=jnp.int32)[None, None, :]


def pair_slope(scores, target, allowed):
    rate = jax.nn.softplus(scores) + 1.0
    return jnp.where(
        allowed, (1.0 - target.astype(jnp.float32) / rate) * jax.nn.sigmoid(scores), 0.0
    ).astype(jnp.bfloat16)


def place_rows(match_bf, values):
    upper = values.astype(jnp.bfloat16)
    lower = (values - upper.astype(jnp.float32)).astype(jnp.bfloat16)
    placed = jnp.einsum("bnr,bnc->brc", match_bf, upper, preferred_element_type=jnp.float32)
    return placed + jnp.einsum("bnr,bnc->brc", match_bf, lower, preferred_element_type=jnp.float32)


def gather_by_permute(x, axes, count, me):
    pieces = [x]
    for k in range(1, count):
        perm = [(i, (i + k) % count) for i in range(count)]
        pieces.append(lax.ppermute(x, axes, perm))
    by_offset = jnp.stack(pieces)
    order = (me - jnp.arange(count, dtype=jnp.int32)) % count
    return jnp.take(by_offset, order, axis=0)


def shards(embed, donor_pos, acceptor_pos, target, donor_w, acceptor_w):
    batch, slab_rows, _ = embed.shape
    slab_sites = donor_pos.shape[1]
    width = donor_w.shape[1]
    scale = 1.0 / math.sqrt(width)
    n_seq = lax.axis_size("seq")
    n_head = lax.axis_size("head")
    slab = lax.axis_index("seq")
    sites = slab_sites * n_seq

    head = lax.axis_index("head")
    me = slab * n_head + head

    donor_match = site_match(donor_pos, slab_rows, slab).astype(jnp.bfloat16)
    acceptor_match = site_match(acceptor_pos, slab_rows, slab).astype(jnp.bfloat16)
    donor_rows = jnp.einsum(
        "bnr,brc->bnc", donor_match, embed, preferred_element_type=jnp.float32
    ).astype(jnp.bfloat16)
    acceptor_rows = jnp.einsum(
        "bnr,brc->bnc", acceptor_match, embed, preferred_element_type=jnp.float32
    ).astype(jnp.bfloat16)
    donor_part = jnp.einsum(
        "bnc,cp->bnp", donor_rows, donor_w, preferred_element_type=jnp.float32
    ).astype(jnp.bfloat16)
    acceptor_part = jnp.einsum(
        "bnc,cp->bnp", acceptor_rows, acceptor_w, preferred_element_type=jnp.float32
    ).astype(jnp.bfloat16)

    both = 2 * slab_sites
    assert both % n_head == 0
    quarter = both // n_head
    parts = jnp.concatenate([donor_part, acceptor_part], axis=1)
    assert n_head & (n_head - 1) == 0
    pieces = [lax.dynamic_slice_in_dim(parts, head * quarter, quarter, 1)]
    for k in range(1, n_head):
        outgoing = lax.dynamic_slice_in_dim(parts, (head ^ k) * quarter, quarter, 1)
        pieces.append(lax.ppermute(outgoing, "head", [(i, i ^ k) for i in range(n_head)]))
    by_partner = jnp.stack(pieces)
    by_head = jnp.take(by_partner, head ^ jnp.arange(n_head, dtype=jnp.int32), axis=0)
    total = jnp.zeros((batch, quarter, width), jnp.float32)
    for h in range(n_head):
        total = total + by_head[h].astype(jnp.float32)
    feat_quarter = total.astype(jnp.bfloat16)

    pieces = [feat_quarter]
    for k in range(1, n_head):
        pieces.append(lax.ppermute(feat_quarter, "head", [(i, i ^ k) for i in range(n_head)]))
    slab_feats = jnp.take(jnp.stack(pieces), head ^ jnp.arange(n_head, dtype=jnp.int32), axis=0)
    slab_feats = jnp.moveaxis(slab_feats, 0, 1).reshape(batch, both, width)
    own_donor = slab_feats[:, :slab_sites]
    own_acceptor = slab_feats[:, slab_sites:]

    n_dp = lax.axis_size("dp")
    assert n_dp & (n_dp - 1) == 0 and n_dp >= 2
    dp = lax.axis_index("dp")
    pair = dp % 2
    channels = embed.shape[2]
    half = channels // 2
    part = width // n_seq
    def over_dp_bits(value):
        bit = 2
        while bit < n_dp:
            held = value.astype(jnp.bfloat16)
            perm = [(i, i ^ bit) for i in range(n_dp)]
            value = held.astype(jnp.float32) + lax.ppermute(held, "dp", perm).astype(jnp.float32)
            bit *= 2
        return value

    if n_seq == 2:
        target_own = lax.dynamic_slice_in_dim(target, slab * slab_sites, slab_sites, 2)
        scores_own = (
            jnp.einsum("bip,bjp->bij", own_donor, own_acceptor, preferred_element_type=jnp.float32)
            * scale
        )
        allowed_own = (donor_pos[:, :, None] >= 0) & (acceptor_pos[:, None, :] > donor_pos[:, :, None])
        slope_own = pair_slope(scores_own, target_own, allowed_own)
        early_acceptor = (
            jnp.einsum("bij,bip->bjp", slope_own, own_donor, preferred_element_type=jnp.float32) * scale
        ).astype(jnp.bfloat16)
        early_donor = (
            jnp.einsum("bij,bjp->bip", slope_own, own_acceptor, preferred_element_type=jnp.float32)
            * scale
        ).astype(jnp.bfloat16)
        first = slab == 0
        grad_early = jnp.where(first, early_acceptor, early_donor)
        rows_early = jnp.where(first, acceptor_rows, donor_rows)

        def to_seq_partner(rows, grad):
            local = jnp.einsum("bnc,bnp->pc", rows, grad, preferred_element_type=jnp.float32)
            local = local.astype(jnp.bfloat16)
            kept = lax.dynamic_slice_in_dim(local, pair * half, half, 1).astype(jnp.float32)
            outgoing = lax.dynamic_slice_in_dim(local, (1 - pair) * half, half, 1)
            kept = kept + lax.ppermute(outgoing, "dp", [(i, i ^ 1) for i in range(n_dp)]).astype(
                jnp.float32
            )
            held = kept.astype(jnp.bfloat16)
            own = lax.dynamic_slice_in_dim(held, slab * part, part, 0).astype(jnp.float32)
            return own, lax.dynamic_slice_in_dim(held, (1 - slab) * part, part, 0)

        def from_seq_partner(outgoing):
            return lax.ppermute(outgoing, "seq", [(0, 1), (1, 0)]).astype(jnp.float32)

        own_early, out_early = to_seq_partner(rows_early, grad_early)

    assert slab_sites <= width
    flags = jnp.zeros((batch, 8, width), jnp.bfloat16)
    flags = flags.at[:, 0, :slab_sites].set((donor_pos >= 0).astype(jnp.bfloat16))
    flags = flags.at[:, 1, :slab_sites].set((acceptor_pos >= 0).astype(jnp.bfloat16))
    donor_feat_all = jnp.zeros((batch, sites, width), jnp.bfloat16)
    acceptor_feat_all = jnp.zeros((batch, sites, width), jnp.bfloat16)
    donor_feat_all = lax.dynamic_update_slice_in_dim(donor_feat_all, own_donor, slab * slab_sites, 1)
    acceptor_feat_all = lax.dynamic_update_slice_in_dim(
        acceptor_feat_all, own_acceptor, slab * slab_sites, 1
    )
    donor_ok_all = jnp.zeros((batch, sites), jnp.bool_)
    acceptor_ok_all = jnp.zeros((batch, sites), jnp.bool_)
    target_col = jnp.zeros((batch, sites, slab_sites), target.dtype)
    own_cols = lax.dynamic_slice_in_dim(target, slab * slab_sites, slab_sites, 2)
    target_col = lax.dynamic_update_slice_in_dim(target_col, own_cols, slab * slab_sites, 1)
    for k in range(1, n_seq):
        sent = jnp.where(slab + k < n_seq, own_donor, own_acceptor)
        target_block = lax.dynamic_slice_in_dim(
            target, jnp.minimum(slab + k, n_seq - 1) * slab_sites, slab_sites, 2
        ).reshape(batch, slab_sites * slab_sites)
        target_rows = -(-(slab_sites * slab_sites) // width)
        target_block = jnp.pad(target_block, ((0, 0), (0, target_rows * width - slab_sites * slab_sites)))
        payload = jnp.concatenate(
            [sent, flags, target_block.reshape(batch, target_rows, width).astype(jnp.bfloat16)], axis=1
        )
        perm = [(i, (i + k) % n_seq) for i in range(n_seq)]
        arrived = lax.ppermute(payload, "seq", perm)
        source = (slab - k) % n_seq
        earlier = slab >= k
        target_in = (
            arrived[:, slab_sites + 8 :]
            .reshape(batch, target_rows * width)[:, : slab_sites * slab_sites]
            .reshape(batch, slab_sites, slab_sites)
        )
        target_col = jnp.where(
            earlier,
            lax.dynamic_update_slice_in_dim(target_col, target_in, source * slab_sites, 1),
            target_col,
        )
        feat_in = arrived[:, :slab_sites]
        donor_feat_all = jnp.where(
            earlier,
            lax.dynamic_update_slice_in_dim(donor_feat_all, feat_in, source * slab_sites, 1),
            donor_feat_all,
        )
        acceptor_feat_all = jnp.where(
            earlier,
            acceptor_feat_all,
            lax.dynamic_update_slice_in_dim(acceptor_feat_all, feat_in, source * slab_sites, 1),
        )
        donor_in = arrived[:, slab_sites, :slab_sites] > 0
        acceptor_in = arrived[:, slab_sites + 1, :slab_sites] > 0
        donor_ok_all = jnp.where(
            earlier,
            lax.dynamic_update_slice_in_dim(donor_ok_all, donor_in, source * slab_sites, 1),
            donor_ok_all,
        )
        acceptor_ok_all = jnp.where(
            earlier,
            acceptor_ok_all,
            lax.dynamic_update_slice_in_dim(acceptor_ok_all, acceptor_in, source * slab_sites, 1),
        )

    if n_seq == 2:
        out_early, arrived = lax.optimization_barrier((out_early, arrived))
        from_early = from_seq_partner(out_early)

    site_slab = jnp.arange(sites, dtype=jnp.int32) // slab_sites
    big = jnp.int32(1 << 30)
    acceptor_tiled = jnp.tile(acceptor_pos, (1, n_seq))
    acceptor_eff = jnp.where(
        site_slab[None, :] == slab,
        acceptor_tiled,
        jnp.where(
            (site_slab[None, :] > slab) & acceptor_ok_all, (slab + 1) * slab_rows, -1
        ),
    )
    donor_tiled = jnp.tile(donor_pos, (1, n_seq))
    donor_eff = jnp.where(
        site_slab[None, :] == slab,
        donor_tiled,
        jnp.where(
            site_slab[None, :] > slab,
            big,
            jnp.where(donor_ok_all, slab * slab_rows - 1, -1),
        ),
    )

    donor_feat = own_donor
    acceptor_feat = own_acceptor

    if n_seq == 2:
        first = slab == 0
        queries = jnp.where(first, own_donor, own_acceptor)
        keys = jnp.where(first, acceptor_feat_all, donor_feat_all)
        scores_late = (
            jnp.einsum("bip,bjp->bij", queries, keys, preferred_element_type=jnp.float32) * scale
        )
        allowed_row = (donor_pos[:, :, None] >= 0) & (acceptor_eff[:, None, :] > donor_pos[:, :, None])
        allowed_col = (donor_eff[:, None, :] >= 0) & (acceptor_pos[:, :, None] > donor_eff[:, None, :])
        allowed_late = jnp.where(first, allowed_row, allowed_col)
        target_late = jnp.where(first, target, jnp.swapaxes(target_col, 1, 2))
        slope_late = pair_slope(scores_late, target_late, allowed_late)
        grad_late = (
            jnp.einsum("bij,bjp->bip", slope_late, keys, preferred_element_type=jnp.float32) * scale
        ).astype(jnp.bfloat16)
    else:
        scores_row = (
            jnp.einsum("bip,bjp->bij", donor_feat, acceptor_feat_all, preferred_element_type=jnp.float32)
            * scale
        )
        allowed_row = (donor_pos[:, :, None] >= 0) & (acceptor_eff[:, None, :] > donor_pos[:, :, None])
        slope_row = pair_slope(scores_row, target, allowed_row)
        donor_grad = (
            jnp.einsum("bij,bjp->bip", slope_row, acceptor_feat_all, preferred_element_type=jnp.float32)
            * scale
        ).astype(jnp.bfloat16)

        scores_col = (
            jnp.einsum("bip,bjp->bij", donor_feat_all, acceptor_feat, preferred_element_type=jnp.float32)
            * scale
        )
        allowed_col = (donor_eff[:, :, None] >= 0) & (acceptor_pos[:, None, :] > donor_eff[:, :, None])
        slope_col = pair_slope(scores_col, target_col, allowed_col)
        acceptor_grad = (
            jnp.einsum("bij,bip->bjp", slope_col, donor_feat_all, preferred_element_type=jnp.float32)
            * scale
        ).astype(jnp.bfloat16)

    if n_seq == 2:
        grad_early = jnp.where(first, early_acceptor, early_donor)
        rows_early = jnp.where(first, acceptor_rows, donor_rows)
        rows_late = jnp.where(first, donor_rows, acceptor_rows)
        donor_grad = jnp.where(first, grad_late, grad_early)
        acceptor_grad = jnp.where(first, grad_early, grad_late)

        own_late, out_late = to_seq_partner(rows_late, grad_late)
        from_late = from_seq_partner(out_late)
        sum_early = own_early + from_late
        sum_late = own_late + from_early
        sum_late = over_dp_bits(sum_late)
    else:
        local_dw = jnp.einsum(
            "bnc,bnp->pc", donor_rows, donor_grad, preferred_element_type=jnp.float32
        )
        local_aw = jnp.einsum(
            "bnc,bnp->pc", acceptor_rows, acceptor_grad, preferred_element_type=jnp.float32
        )
        blocks = jnp.stack([local_dw, local_aw]).astype(jnp.bfloat16)
        mine = lax.dynamic_slice_in_dim(blocks, pair * half, half, 2).astype(jnp.float32)
        outgoing = lax.dynamic_slice_in_dim(blocks, (1 - pair) * half, half, 2)
        mine = mine + lax.ppermute(outgoing, "dp", [(i, i ^ 1) for i in range(n_dp)]).astype(
            jnp.float32
        )
        held = mine.astype(jnp.bfloat16)
        mine = lax.dynamic_slice_in_dim(held, slab * part, part, 1).astype(jnp.float32)
        for k in range(1, n_seq):
            outgoing = lax.dynamic_slice_in_dim(held, ((slab + k) % n_seq) * part, part, 1)
            perm = [(i, (i + k) % n_seq) for i in range(n_seq)]
            mine = mine + lax.ppermute(outgoing, "seq", perm).astype(jnp.float32)
    donor_site = jnp.einsum("bnp,cp->bnc", donor_grad, donor_w, preferred_element_type=jnp.float32)
    acceptor_site = jnp.einsum(
        "bnp,cp->bnc", acceptor_grad, acceptor_w, preferred_element_type=jnp.float32
    )
    row_grad = place_rows(donor_match, donor_site) + place_rows(acceptor_match, acceptor_site)

    def with_partner_half(value):
        other = lax.ppermute(value, "dp", [(i, i ^ 1) for i in range(n_dp)])
        axis = value.ndim - 1
        return jnp.where(
            pair == 0, jnp.concatenate([value, other], axis), jnp.concatenate([other, value], axis)
        )

    if n_seq == 2:
        late_full = with_partner_half(sum_late)
        sum_early, row_grad = lax.optimization_barrier((sum_early, row_grad))
        early_full = with_partner_half(over_dp_bits(sum_early))
        mine = jnp.stack(
            [jnp.where(first, late_full, early_full), jnp.where(first, early_full, late_full)]
        )
    else:
        mine = with_partner_half(over_dp_bits(mine))
    mine = jnp.swapaxes(mine, 1, 2)
    column_major = Layout(major_to_minor=(1, 0))
    grad_dw = with_layout_constraint(mine[0], column_major)
    grad_aw = with_layout_constraint(mine[1], column_major)
    return (row_grad.astype(jnp.bfloat16), grad_dw, grad_aw)


def solution(mesh):
    in_specs = (
        P("dp", "seq", "head"),
        P("dp", "seq"),
        P("dp", "seq"),
        P("dp", "seq", None),
        P("head", None),
        P("head", None),
    )
    out_specs = (P("dp", "seq", "head"), P("head", "seq"), P("head", "seq"))
    return jax.shard_map(shards, mesh=mesh, in_specs=in_specs, out_specs=out_specs, check_vma=False)
```

```python
import math

import jax
import jax.numpy as jnp
from jax import lax
from jax.experimental.layout import Layout, with_layout_constraint
from jax.sharding import PartitionSpec as P


def site_match(positions, slab_rows, slab_index):
    local_pos = positions - slab_index * slab_rows
    return local_pos[:, :, None] == jnp.arange(slab_rows, dtype=jnp.int32)[None, None, :]


def pair_slope(scores, target, allowed):
    rate = jax.nn.softplus(scores) + 1.0
    return jnp.where(
        allowed, (1.0 - target.astype(jnp.float32) / rate) * jax.nn.sigmoid(scores), 0.0
    ).astype(jnp.bfloat16)


def place_rows(match_bf, values):
    upper = values.astype(jnp.bfloat16)
    lower = (values - upper.astype(jnp.float32)).astype(jnp.bfloat16)
    placed = jnp.einsum("bnr,bnc->brc", match_bf, upper, preferred_element_type=jnp.float32)
    return placed + jnp.einsum("bnr,bnc->brc", match_bf, lower, preferred_element_type=jnp.float32)


def gather_by_permute(x, axes, count, me):
    pieces = [x]
    for k in range(1, count):
        perm = [(i, (i + k) % count) for i in range(count)]
        pieces.append(lax.ppermute(x, axes, perm))
    by_offset = jnp.stack(pieces)
    order = (me - jnp.arange(count, dtype=jnp.int32)) % count
    return jnp.take(by_offset, order, axis=0)


def shards(embed, donor_pos, acceptor_pos, target, donor_w, acceptor_w):
    batch, slab_rows, _ = embed.shape
    slab_sites = donor_pos.shape[1]
    width = donor_w.shape[1]
    scale = 1.0 / math.sqrt(width)
    n_seq = lax.axis_size("seq")
    n_head = lax.axis_size("head")
    slab = lax.axis_index("seq")
    sites = slab_sites * n_seq

    head = lax.axis_index("head")
    me = slab * n_head + head

    donor_match = site_match(donor_pos, slab_rows, slab).astype(jnp.bfloat16)
    acceptor_match = site_match(acceptor_pos, slab_rows, slab).astype(jnp.bfloat16)
    donor_rows = jnp.einsum(
        "bnr,brc->bnc", donor_match, embed, preferred_element_type=jnp.float32
    ).astype(jnp.bfloat16)
    acceptor_rows = jnp.einsum(
        "bnr,brc->bnc", acceptor_match, embed, preferred_element_type=jnp.float32
    ).astype(jnp.bfloat16)
    donor_part = jnp.einsum(
        "bnc,cp->bnp", donor_rows, donor_w, preferred_element_type=jnp.float32
    ).astype(jnp.bfloat16)
    acceptor_part = jnp.einsum(
        "bnc,cp->bnp", acceptor_rows, acceptor_w, preferred_element_type=jnp.float32
    ).astype(jnp.bfloat16)

    both = 2 * slab_sites
    assert both % n_head == 0
    quarter = both // n_head
    parts = jnp.concatenate([donor_part, acceptor_part], axis=1)
    assert n_head & (n_head - 1) == 0
    pieces = [lax.dynamic_slice_in_dim(parts, head * quarter, quarter, 1)]
    for k in range(1, n_head):
        outgoing = lax.dynamic_slice_in_dim(parts, (head ^ k) * quarter, quarter, 1)
        pieces.append(lax.ppermute(outgoing, "head", [(i, i ^ k) for i in range(n_head)]))
    by_partner = jnp.stack(pieces)
    by_head = jnp.take(by_partner, head ^ jnp.arange(n_head, dtype=jnp.int32), axis=0)
    total = jnp.zeros((batch, quarter, width), jnp.float32)
    for h in range(n_head):
        total = total + by_head[h].astype(jnp.float32)
    feat_quarter = total.astype(jnp.bfloat16)

    pieces = [feat_quarter]
    for k in range(1, n_head):
        pieces.append(lax.ppermute(feat_quarter, "head", [(i, i ^ k) for i in range(n_head)]))
    slab_feats = jnp.take(jnp.stack(pieces), head ^ jnp.arange(n_head, dtype=jnp.int32), axis=0)
    slab_feats = jnp.moveaxis(slab_feats, 0, 1).reshape(batch, both, width)
    own_donor = slab_feats[:, :slab_sites]
    own_acceptor = slab_feats[:, slab_sites:]

    n_dp = lax.axis_size("dp")
    assert n_dp & (n_dp - 1) == 0 and n_dp >= 2
    dp = lax.axis_index("dp")
    pair = dp % 2
    channels = embed.shape[2]
    half = channels // 2
    part = width // n_seq
    def over_dp_bits(value):
        bit = 2
        while bit < n_dp:
            held = value.astype(jnp.bfloat16)
            perm = [(i, i ^ bit) for i in range(n_dp)]
            value = held.astype(jnp.float32) + lax.ppermute(held, "dp", perm).astype(jnp.float32)
            bit *= 2
        return value

    if n_seq == 2:
        target_own = lax.dynamic_slice_in_dim(target, slab * slab_sites, slab_sites, 2)
        scores_own = (
            jnp.einsum("bip,bjp->bij", own_donor, own_acceptor, preferred_element_type=jnp.float32)
            * scale
        )
        allowed_own = (donor_pos[:, :, None] >= 0) & (acceptor_pos[:, None, :] > donor_pos[:, :, None])
        slope_own = pair_slope(scores_own, target_own, allowed_own)
        early_acceptor = (
            jnp.einsum("bij,bip->bjp", slope_own, own_donor, preferred_element_type=jnp.float32) * scale
        ).astype(jnp.bfloat16)
        early_donor = (
            jnp.einsum("bij,bjp->bip", slope_own, own_acceptor, preferred_element_type=jnp.float32)
            * scale
        ).astype(jnp.bfloat16)
        first = slab == 0
        grad_early = jnp.where(first, early_acceptor, early_donor)
        rows_early = jnp.where(first, acceptor_rows, donor_rows)

        def to_seq_partner(rows, grad):
            local = jnp.einsum("bnc,bnp->pc", rows, grad, preferred_element_type=jnp.float32)
            local = local.astype(jnp.bfloat16)

            def chip_sum(width_part):
                block = lax.dynamic_slice_in_dim(local, width_part * part, part, 0)
                kept = lax.dynamic_slice_in_dim(block, pair * half, half, 1).astype(jnp.float32)
                outgoing = lax.dynamic_slice_in_dim(block, (1 - pair) * half, half, 1)
                received = lax.ppermute(outgoing, "dp", [(i, i ^ 1) for i in range(n_dp)])
                return (kept + received.astype(jnp.float32)).astype(jnp.bfloat16)

            for_partner = chip_sum(1 - slab)
            own = chip_sum(slab).astype(jnp.float32)
            return own, for_partner

        def from_seq_partner(outgoing):
            return lax.ppermute(outgoing, "seq", [(0, 1), (1, 0)]).astype(jnp.float32)

        own_early, out_early = to_seq_partner(rows_early, grad_early)

    assert slab_sites <= width
    flags = jnp.zeros((batch, 8, width), jnp.bfloat16)
    flags = flags.at[:, 0, :slab_sites].set((donor_pos >= 0).astype(jnp.bfloat16))
    flags = flags.at[:, 1, :slab_sites].set((acceptor_pos >= 0).astype(jnp.bfloat16))
    donor_feat_all = jnp.zeros((batch, sites, width), jnp.bfloat16)
    acceptor_feat_all = jnp.zeros((batch, sites, width), jnp.bfloat16)
    donor_feat_all = lax.dynamic_update_slice_in_dim(donor_feat_all, own_donor, slab * slab_sites, 1)
    acceptor_feat_all = lax.dynamic_update_slice_in_dim(
        acceptor_feat_all, own_acceptor, slab * slab_sites, 1
    )
    donor_ok_all = jnp.zeros((batch, sites), jnp.bool_)
    acceptor_ok_all = jnp.zeros((batch, sites), jnp.bool_)
    target_col = jnp.zeros((batch, sites, slab_sites), target.dtype)
    own_cols = lax.dynamic_slice_in_dim(target, slab * slab_sites, slab_sites, 2)
    target_col = lax.dynamic_update_slice_in_dim(target_col, own_cols, slab * slab_sites, 1)
    for k in range(1, n_seq):
        sent = jnp.where(slab + k < n_seq, own_donor, own_acceptor)
        target_block = lax.dynamic_slice_in_dim(
            target, jnp.minimum(slab + k, n_seq - 1) * slab_sites, slab_sites, 2
        ).reshape(batch, slab_sites * slab_sites)
        target_rows = -(-(slab_sites * slab_sites) // width)
        target_block = jnp.pad(target_block, ((0, 0), (0, target_rows * width - slab_sites * slab_sites)))
        payload = jnp.concatenate(
            [sent, flags, target_block.reshape(batch, target_rows, width).astype(jnp.bfloat16)], axis=1
        )
        perm = [(i, (i + k) % n_seq) for i in range(n_seq)]
        arrived = lax.ppermute(payload, "seq", perm)
        source = (slab - k) % n_seq
        earlier = slab >= k
        target_in = (
            arrived[:, slab_sites + 8 :]
            .reshape(batch, target_rows * width)[:, : slab_sites * slab_sites]
            .reshape(batch, slab_sites, slab_sites)
        )
        target_col = jnp.where(
            earlier,
            lax.dynamic_update_slice_in_dim(target_col, target_in, source * slab_sites, 1),
            target_col,
        )
        feat_in = arrived[:, :slab_sites]
        donor_feat_all = jnp.where(
            earlier,
            lax.dynamic_update_slice_in_dim(donor_feat_all, feat_in, source * slab_sites, 1),
            donor_feat_all,
        )
        acceptor_feat_all = jnp.where(
            earlier,
            acceptor_feat_all,
            lax.dynamic_update_slice_in_dim(acceptor_feat_all, feat_in, source * slab_sites, 1),
        )
        donor_in = arrived[:, slab_sites, :slab_sites] > 0
        acceptor_in = arrived[:, slab_sites + 1, :slab_sites] > 0
        donor_ok_all = jnp.where(
            earlier,
            lax.dynamic_update_slice_in_dim(donor_ok_all, donor_in, source * slab_sites, 1),
            donor_ok_all,
        )
        acceptor_ok_all = jnp.where(
            earlier,
            acceptor_ok_all,
            lax.dynamic_update_slice_in_dim(acceptor_ok_all, acceptor_in, source * slab_sites, 1),
        )

    if n_seq == 2:
        out_early, arrived = lax.optimization_barrier((out_early, arrived))
        from_early = from_seq_partner(out_early)

    site_slab = jnp.arange(sites, dtype=jnp.int32) // slab_sites
    big = jnp.int32(1 << 30)
    acceptor_tiled = jnp.tile(acceptor_pos, (1, n_seq))
    acceptor_eff = jnp.where(
        site_slab[None, :] == slab,
        acceptor_tiled,
        jnp.where(
            (site_slab[None, :] > slab) & acceptor_ok_all, (slab + 1) * slab_rows, -1
        ),
    )
    donor_tiled = jnp.tile(donor_pos, (1, n_seq))
    donor_eff = jnp.where(
        site_slab[None, :] == slab,
        donor_tiled,
        jnp.where(
            site_slab[None, :] > slab,
            big,
            jnp.where(donor_ok_all, slab * slab_rows - 1, -1),
        ),
    )

    donor_feat = own_donor
    acceptor_feat = own_acceptor

    if n_seq == 2:
        first = slab == 0
        queries = jnp.where(first, own_donor, own_acceptor)
        keys = jnp.where(first, acceptor_feat_all, donor_feat_all)
        scores_late = (
            jnp.einsum("bip,bjp->bij", queries, keys, preferred_element_type=jnp.float32) * scale
        )
        allowed_row = (donor_pos[:, :, None] >= 0) & (acceptor_eff[:, None, :] > donor_pos[:, :, None])
        allowed_col = (donor_eff[:, None, :] >= 0) & (acceptor_pos[:, :, None] > donor_eff[:, None, :])
        allowed_late = jnp.where(first, allowed_row, allowed_col)
        target_late = jnp.where(first, target, jnp.swapaxes(target_col, 1, 2))
        slope_late = pair_slope(scores_late, target_late, allowed_late)
        grad_late = (
            jnp.einsum("bij,bjp->bip", slope_late, keys, preferred_element_type=jnp.float32) * scale
        ).astype(jnp.bfloat16)
    else:
        scores_row = (
            jnp.einsum("bip,bjp->bij", donor_feat, acceptor_feat_all, preferred_element_type=jnp.float32)
            * scale
        )
        allowed_row = (donor_pos[:, :, None] >= 0) & (acceptor_eff[:, None, :] > donor_pos[:, :, None])
        slope_row = pair_slope(scores_row, target, allowed_row)
        donor_grad = (
            jnp.einsum("bij,bjp->bip", slope_row, acceptor_feat_all, preferred_element_type=jnp.float32)
            * scale
        ).astype(jnp.bfloat16)

        scores_col = (
            jnp.einsum("bip,bjp->bij", donor_feat_all, acceptor_feat, preferred_element_type=jnp.float32)
            * scale
        )
        allowed_col = (donor_eff[:, :, None] >= 0) & (acceptor_pos[:, None, :] > donor_eff[:, :, None])
        slope_col = pair_slope(scores_col, target_col, allowed_col)
        acceptor_grad = (
            jnp.einsum("bij,bip->bjp", slope_col, donor_feat_all, preferred_element_type=jnp.float32)
            * scale
        ).astype(jnp.bfloat16)

    if n_seq == 2:
        grad_early = jnp.where(first, early_acceptor, early_donor)
        rows_early = jnp.where(first, acceptor_rows, donor_rows)
        rows_late = jnp.where(first, donor_rows, acceptor_rows)
        donor_grad = jnp.where(first, grad_late, grad_early)
        acceptor_grad = jnp.where(first, grad_early, grad_late)

        own_late, out_late = to_seq_partner(rows_late, grad_late)
        from_late = from_seq_partner(out_late)
        sum_early = own_early + from_late
        sum_late = own_late + from_early
        sum_late = over_dp_bits(sum_late)
        sum_early = over_dp_bits(sum_early)
        mine = jnp.stack(
            [jnp.where(first, sum_late, sum_early), jnp.where(first, sum_early, sum_late)]
        )
    else:
        local_dw = jnp.einsum(
            "bnc,bnp->pc", donor_rows, donor_grad, preferred_element_type=jnp.float32
        )
        local_aw = jnp.einsum(
            "bnc,bnp->pc", acceptor_rows, acceptor_grad, preferred_element_type=jnp.float32
        )
        blocks = jnp.stack([local_dw, local_aw]).astype(jnp.bfloat16)
        mine = lax.dynamic_slice_in_dim(blocks, pair * half, half, 2).astype(jnp.float32)
        outgoing = lax.dynamic_slice_in_dim(blocks, (1 - pair) * half, half, 2)
        mine = mine + lax.ppermute(outgoing, "dp", [(i, i ^ 1) for i in range(n_dp)]).astype(
            jnp.float32
        )
        held = mine.astype(jnp.bfloat16)
        mine = lax.dynamic_slice_in_dim(held, slab * part, part, 1).astype(jnp.float32)
        for k in range(1, n_seq):
            outgoing = lax.dynamic_slice_in_dim(held, ((slab + k) % n_seq) * part, part, 1)
            perm = [(i, (i + k) % n_seq) for i in range(n_seq)]
            mine = mine + lax.ppermute(outgoing, "seq", perm).astype(jnp.float32)
    donor_site = jnp.einsum("bnp,cp->bnc", donor_grad, donor_w, preferred_element_type=jnp.float32)
    acceptor_site = jnp.einsum(
        "bnp,cp->bnc", acceptor_grad, acceptor_w, preferred_element_type=jnp.float32
    )
    row_grad = place_rows(donor_match, donor_site) + place_rows(acceptor_match, acceptor_site)
    if n_seq != 2:
        mine = over_dp_bits(mine)
    other = lax.ppermute(mine, "dp", [(i, i ^ 1) for i in range(n_dp)])
    mine = jnp.where(pair == 0, jnp.concatenate([mine, other], 2), jnp.concatenate([other, mine], 2))
    mine = jnp.swapaxes(mine, 1, 2)
    column_major = Layout(major_to_minor=(1, 0))
    grad_dw = with_layout_constraint(mine[0], column_major)
    grad_aw = with_layout_constraint(mine[1], column_major)
    return (row_grad.astype(jnp.bfloat16), grad_dw, grad_aw)


def solution(mesh):
    in_specs = (
        P("dp", "seq", "head"),
        P("dp", "seq"),
        P("dp", "seq"),
        P("dp", "seq", None),
        P("head", None),
        P("head", None),
    )
    out_specs = (P("dp", "seq", "head"), P("head", "seq"), P("head", "seq"))
    return jax.shard_map(shards, mesh=mesh, in_specs=in_specs, out_specs=out_specs, check_vma=False)
```

```python
import math

import jax
import jax.numpy as jnp
from jax import lax
from jax.experimental.layout import Layout, with_layout_constraint
from jax.sharding import PartitionSpec as P


def site_match(positions, slab_rows, slab_index):
    local_pos = positions - slab_index * slab_rows
    return local_pos[:, :, None] == jnp.arange(slab_rows, dtype=jnp.int32)[None, None, :]


def pair_slope(scores, target, allowed):
    rate = jax.nn.softplus(scores) + 1.0
    return jnp.where(
        allowed, (1.0 - target.astype(jnp.float32) / rate) * jax.nn.sigmoid(scores), 0.0
    ).astype(jnp.bfloat16)


def place_rows(match_bf, values):
    upper = values.astype(jnp.bfloat16)
    lower = (values - upper.astype(jnp.float32)).astype(jnp.bfloat16)
    placed = jnp.einsum("bnr,bnc->brc", match_bf, upper, preferred_element_type=jnp.float32)
    return placed + jnp.einsum("bnr,bnc->brc", match_bf, lower, preferred_element_type=jnp.float32)


def gather_by_permute(x, axes, count, me):
    pieces = [x]
    for k in range(1, count):
        perm = [(i, (i + k) % count) for i in range(count)]
        pieces.append(lax.ppermute(x, axes, perm))
    by_offset = jnp.stack(pieces)
    order = (me - jnp.arange(count, dtype=jnp.int32)) % count
    return jnp.take(by_offset, order, axis=0)


def from_head(pieces, head, source):
    chosen = pieces[0]
    for k in range(1, len(pieces)):
        chosen = jnp.where((head ^ k) == source, pieces[k], chosen)
    return chosen


def shards(embed, donor_pos, acceptor_pos, target, donor_w, acceptor_w):
    batch, slab_rows, _ = embed.shape
    slab_sites = donor_pos.shape[1]
    width = donor_w.shape[1]
    scale = 1.0 / math.sqrt(width)
    n_seq = lax.axis_size("seq")
    n_head = lax.axis_size("head")
    slab = lax.axis_index("seq")
    sites = slab_sites * n_seq

    head = lax.axis_index("head")
    me = slab * n_head + head

    donor_match = site_match(donor_pos, slab_rows, slab).astype(jnp.bfloat16)
    acceptor_match = site_match(acceptor_pos, slab_rows, slab).astype(jnp.bfloat16)
    donor_rows = jnp.einsum(
        "bnr,brc->bnc", donor_match, embed, preferred_element_type=jnp.float32
    ).astype(jnp.bfloat16)
    acceptor_rows = jnp.einsum(
        "bnr,brc->bnc", acceptor_match, embed, preferred_element_type=jnp.float32
    ).astype(jnp.bfloat16)
    donor_part = jnp.einsum(
        "bnc,cp->bnp", donor_rows, donor_w, preferred_element_type=jnp.float32
    ).astype(jnp.bfloat16)
    acceptor_part = jnp.einsum(
        "bnc,cp->bnp", acceptor_rows, acceptor_w, preferred_element_type=jnp.float32
    ).astype(jnp.bfloat16)

    both = 2 * slab_sites
    assert both % n_head == 0
    quarter = both // n_head
    parts = jnp.concatenate([donor_part, acceptor_part], axis=1)
    assert n_head & (n_head - 1) == 0
    pieces = [lax.dynamic_slice_in_dim(parts, head * quarter, quarter, 1)]
    for k in range(1, n_head):
        outgoing = lax.dynamic_slice_in_dim(parts, (head ^ k) * quarter, quarter, 1)
        pieces.append(lax.ppermute(outgoing, "head", [(i, i ^ k) for i in range(n_head)]))
    total = jnp.zeros((batch, quarter, width), jnp.float32)
    for h in range(n_head):
        total = total + from_head(pieces, head, h).astype(jnp.float32)
    feat_quarter = total.astype(jnp.bfloat16)

    pieces = [feat_quarter]
    for k in range(1, n_head):
        pieces.append(lax.ppermute(feat_quarter, "head", [(i, i ^ k) for i in range(n_head)]))
    slab_feats = jnp.concatenate([from_head(pieces, head, h) for h in range(n_head)], axis=1)
    own_donor = slab_feats[:, :slab_sites]
    own_acceptor = slab_feats[:, slab_sites:]

    n_dp = lax.axis_size("dp")
    assert n_dp & (n_dp - 1) == 0 and n_dp >= 2
    dp = lax.axis_index("dp")
    pair = dp % 2
    channels = embed.shape[2]
    half = channels // 2
    part = width // n_seq
    def over_dp_bits(value):
        bit = 2
        while bit < n_dp:
            held = value.astype(jnp.bfloat16)
            perm = [(i, i ^ bit) for i in range(n_dp)]
            value = held.astype(jnp.float32) + lax.ppermute(held, "dp", perm).astype(jnp.float32)
            bit *= 2
        return value

    if n_seq == 2:
        target_own = lax.dynamic_slice_in_dim(target, slab * slab_sites, slab_sites, 2)
        scores_own = (
            jnp.einsum("bip,bjp->bij", own_donor, own_acceptor, preferred_element_type=jnp.float32)
            * scale
        )
        allowed_own = (donor_pos[:, :, None] >= 0) & (acceptor_pos[:, None, :] > donor_pos[:, :, None])
        slope_own = pair_slope(scores_own, target_own, allowed_own)
        early_acceptor = (
            jnp.einsum("bij,bip->bjp", slope_own, own_donor, preferred_element_type=jnp.float32) * scale
        ).astype(jnp.bfloat16)
        early_donor = (
            jnp.einsum("bij,bjp->bip", slope_own, own_acceptor, preferred_element_type=jnp.float32)
            * scale
        ).astype(jnp.bfloat16)
        first = slab == 0
        grad_early = jnp.where(first, early_acceptor, early_donor)
        rows_early = jnp.where(first, acceptor_rows, donor_rows)

        def to_seq_partner(rows, grad):
            local = jnp.einsum("bnc,bnp->pc", rows, grad, preferred_element_type=jnp.float32)
            local = local.astype(jnp.bfloat16)
            kept = lax.dynamic_slice_in_dim(local, pair * half, half, 1).astype(jnp.float32)
            outgoing = lax.dynamic_slice_in_dim(local, (1 - pair) * half, half, 1)
            kept = kept + lax.ppermute(outgoing, "dp", [(i, i ^ 1) for i in range(n_dp)]).astype(
                jnp.float32
            )
            held = kept.astype(jnp.bfloat16)
            own = lax.dynamic_slice_in_dim(held, slab * part, part, 0).astype(jnp.float32)
            return own, lax.dynamic_slice_in_dim(held, (1 - slab) * part, part, 0)

        def from_seq_partner(outgoing):
            return lax.ppermute(outgoing, "seq", [(0, 1), (1, 0)]).astype(jnp.float32)

        own_early, out_early = to_seq_partner(rows_early, grad_early)

    assert slab_sites <= width
    flags = jnp.zeros((batch, 8, width), jnp.bfloat16)
    flags = flags.at[:, 0, :slab_sites].set((donor_pos >= 0).astype(jnp.bfloat16))
    flags = flags.at[:, 1, :slab_sites].set((acceptor_pos >= 0).astype(jnp.bfloat16))
    donor_feat_all = jnp.zeros((batch, sites, width), jnp.bfloat16)
    acceptor_feat_all = jnp.zeros((batch, sites, width), jnp.bfloat16)
    donor_feat_all = lax.dynamic_update_slice_in_dim(donor_feat_all, own_donor, slab * slab_sites, 1)
    acceptor_feat_all = lax.dynamic_update_slice_in_dim(
        acceptor_feat_all, own_acceptor, slab * slab_sites, 1
    )
    donor_ok_all = jnp.zeros((batch, sites), jnp.bool_)
    acceptor_ok_all = jnp.zeros((batch, sites), jnp.bool_)
    target_col = jnp.zeros((batch, sites, slab_sites), target.dtype)
    own_cols = lax.dynamic_slice_in_dim(target, slab * slab_sites, slab_sites, 2)
    target_col = lax.dynamic_update_slice_in_dim(target_col, own_cols, slab * slab_sites, 1)
    for k in range(1, n_seq):
        sent = jnp.where(slab + k < n_seq, own_donor, own_acceptor)
        target_block = lax.dynamic_slice_in_dim(
            target, jnp.minimum(slab + k, n_seq - 1) * slab_sites, slab_sites, 2
        ).reshape(batch, slab_sites * slab_sites)
        target_rows = -(-(slab_sites * slab_sites) // width)
        target_block = jnp.pad(target_block, ((0, 0), (0, target_rows * width - slab_sites * slab_sites)))
        payload = jnp.concatenate(
            [sent, flags, target_block.reshape(batch, target_rows, width).astype(jnp.bfloat16)], axis=1
        )
        perm = [(i, (i + k) % n_seq) for i in range(n_seq)]
        arrived = lax.ppermute(payload, "seq", perm)
        source = (slab - k) % n_seq
        earlier = slab >= k
        target_in = (
            arrived[:, slab_sites + 8 :]
            .reshape(batch, target_rows * width)[:, : slab_sites * slab_sites]
            .reshape(batch, slab_sites, slab_sites)
        )
        target_col = jnp.where(
            earlier,
            lax.dynamic_update_slice_in_dim(target_col, target_in, source * slab_sites, 1),
            target_col,
        )
        feat_in = arrived[:, :slab_sites]
        donor_feat_all = jnp.where(
            earlier,
            lax.dynamic_update_slice_in_dim(donor_feat_all, feat_in, source * slab_sites, 1),
            donor_feat_all,
        )
        acceptor_feat_all = jnp.where(
            earlier,
            acceptor_feat_all,
            lax.dynamic_update_slice_in_dim(acceptor_feat_all, feat_in, source * slab_sites, 1),
        )
        donor_in = arrived[:, slab_sites, :slab_sites] > 0
        acceptor_in = arrived[:, slab_sites + 1, :slab_sites] > 0
        donor_ok_all = jnp.where(
            earlier,
            lax.dynamic_update_slice_in_dim(donor_ok_all, donor_in, source * slab_sites, 1),
            donor_ok_all,
        )
        acceptor_ok_all = jnp.where(
            earlier,
            acceptor_ok_all,
            lax.dynamic_update_slice_in_dim(acceptor_ok_all, acceptor_in, source * slab_sites, 1),
        )

    if n_seq == 2:
        out_early, arrived = lax.optimization_barrier((out_early, arrived))
        from_early = from_seq_partner(out_early)

    site_slab = jnp.arange(sites, dtype=jnp.int32) // slab_sites
    big = jnp.int32(1 << 30)
    acceptor_tiled = jnp.tile(acceptor_pos, (1, n_seq))
    acceptor_eff = jnp.where(
        site_slab[None, :] == slab,
        acceptor_tiled,
        jnp.where(
            (site_slab[None, :] > slab) & acceptor_ok_all, (slab + 1) * slab_rows, -1
        ),
    )
    donor_tiled = jnp.tile(donor_pos, (1, n_seq))
    donor_eff = jnp.where(
        site_slab[None, :] == slab,
        donor_tiled,
        jnp.where(
            site_slab[None, :] > slab,
            big,
            jnp.where(donor_ok_all, slab * slab_rows - 1, -1),
        ),
    )

    donor_feat = own_donor
    acceptor_feat = own_acceptor

    if n_seq == 2:
        first = slab == 0
        queries = jnp.where(first, own_donor, own_acceptor)
        keys = jnp.where(first, acceptor_feat_all, donor_feat_all)
        scores_late = (
            jnp.einsum("bip,bjp->bij", queries, keys, preferred_element_type=jnp.float32) * scale
        )
        allowed_row = (donor_pos[:, :, None] >= 0) & (acceptor_eff[:, None, :] > donor_pos[:, :, None])
        allowed_col = (donor_eff[:, None, :] >= 0) & (acceptor_pos[:, :, None] > donor_eff[:, None, :])
        allowed_late = jnp.where(first, allowed_row, allowed_col)
        target_late = jnp.where(first, target, jnp.swapaxes(target_col, 1, 2))
        slope_late = pair_slope(scores_late, target_late, allowed_late)
        grad_late = (
            jnp.einsum("bij,bjp->bip", slope_late, keys, preferred_element_type=jnp.float32) * scale
        ).astype(jnp.bfloat16)
    else:
        scores_row = (
            jnp.einsum("bip,bjp->bij", donor_feat, acceptor_feat_all, preferred_element_type=jnp.float32)
            * scale
        )
        allowed_row = (donor_pos[:, :, None] >= 0) & (acceptor_eff[:, None, :] > donor_pos[:, :, None])
        slope_row = pair_slope(scores_row, target, allowed_row)
        donor_grad = (
            jnp.einsum("bij,bjp->bip", slope_row, acceptor_feat_all, preferred_element_type=jnp.float32)
            * scale
        ).astype(jnp.bfloat16)

        scores_col = (
            jnp.einsum("bip,bjp->bij", donor_feat_all, acceptor_feat, preferred_element_type=jnp.float32)
            * scale
        )
        allowed_col = (donor_eff[:, :, None] >= 0) & (acceptor_pos[:, None, :] > donor_eff[:, :, None])
        slope_col = pair_slope(scores_col, target_col, allowed_col)
        acceptor_grad = (
            jnp.einsum("bij,bip->bjp", slope_col, donor_feat_all, preferred_element_type=jnp.float32)
            * scale
        ).astype(jnp.bfloat16)

    if n_seq == 2:
        grad_early = jnp.where(first, early_acceptor, early_donor)
        rows_early = jnp.where(first, acceptor_rows, donor_rows)
        rows_late = jnp.where(first, donor_rows, acceptor_rows)
        donor_grad = jnp.where(first, grad_late, grad_early)
        acceptor_grad = jnp.where(first, grad_early, grad_late)

        own_late, out_late = to_seq_partner(rows_late, grad_late)
        from_late = from_seq_partner(out_late)
        sum_early = own_early + from_late
        sum_late = own_late + from_early
        sum_late = over_dp_bits(sum_late)
        sum_early = over_dp_bits(sum_early)
        mine = jnp.stack(
            [jnp.where(first, sum_late, sum_early), jnp.where(first, sum_early, sum_late)]
        )
    else:
        local_dw = jnp.einsum(
            "bnc,bnp->pc", donor_rows, donor_grad, preferred_element_type=jnp.float32
        )
        local_aw = jnp.einsum(
            "bnc,bnp->pc", acceptor_rows, acceptor_grad, preferred_element_type=jnp.float32
        )
        blocks = jnp.stack([local_dw, local_aw]).astype(jnp.bfloat16)
        mine = lax.dynamic_slice_in_dim(blocks, pair * half, half, 2).astype(jnp.float32)
        outgoing = lax.dynamic_slice_in_dim(blocks, (1 - pair) * half, half, 2)
        mine = mine + lax.ppermute(outgoing, "dp", [(i, i ^ 1) for i in range(n_dp)]).astype(
            jnp.float32
        )
        held = mine.astype(jnp.bfloat16)
        mine = lax.dynamic_slice_in_dim(held, slab * part, part, 1).astype(jnp.float32)
        for k in range(1, n_seq):
            outgoing = lax.dynamic_slice_in_dim(held, ((slab + k) % n_seq) * part, part, 1)
            perm = [(i, (i + k) % n_seq) for i in range(n_seq)]
            mine = mine + lax.ppermute(outgoing, "seq", perm).astype(jnp.float32)
    donor_site = jnp.einsum("bnp,cp->bnc", donor_grad, donor_w, preferred_element_type=jnp.float32)
    acceptor_site = jnp.einsum(
        "bnp,cp->bnc", acceptor_grad, acceptor_w, preferred_element_type=jnp.float32
    )
    row_grad = place_rows(donor_match, donor_site) + place_rows(acceptor_match, acceptor_site)
    if n_seq != 2:
        mine = over_dp_bits(mine)
    other = lax.ppermute(mine, "dp", [(i, i ^ 1) for i in range(n_dp)])
    mine = jnp.where(pair == 0, jnp.concatenate([mine, other], 2), jnp.concatenate([other, mine], 2))
    mine = jnp.swapaxes(mine, 1, 2)
    column_major = Layout(major_to_minor=(1, 0))
    grad_dw = with_layout_constraint(mine[0], column_major)
    grad_aw = with_layout_constraint(mine[1], column_major)
    return (row_grad.astype(jnp.bfloat16), grad_dw, grad_aw)


def solution(mesh):
    in_specs = (
        P("dp", "seq", "head"),
        P("dp", "seq"),
        P("dp", "seq"),
        P("dp", "seq", None),
        P("head", None),
        P("head", None),
    )
    out_specs = (P("dp", "seq", "head"), P("head", "seq"), P("head", "seq"))
    return jax.shard_map(shards, mesh=mesh, in_specs=in_specs, out_specs=out_specs, check_vma=False)
```

```python
import math

import jax
import jax.numpy as jnp
from jax import lax
from jax.experimental.layout import Layout, with_layout_constraint
from jax.sharding import PartitionSpec as P


def site_match(positions, slab_rows, slab_index):
    local_pos = positions - slab_index * slab_rows
    return local_pos[:, :, None] == jnp.arange(slab_rows, dtype=jnp.int32)[None, None, :]


def pair_slope(scores, target, allowed):
    rate = jax.nn.softplus(scores) + 1.0
    return jnp.where(
        allowed, (1.0 - target.astype(jnp.float32) / rate) * jax.nn.sigmoid(scores), 0.0
    ).astype(jnp.bfloat16)


def place_rows(match_bf, values):
    upper = values.astype(jnp.bfloat16)
    lower = (values - upper.astype(jnp.float32)).astype(jnp.bfloat16)
    placed = jnp.einsum("bnr,bnc->brc", match_bf, upper, preferred_element_type=jnp.float32)
    return placed + jnp.einsum("bnr,bnc->brc", match_bf, lower, preferred_element_type=jnp.float32)


def gather_by_permute(x, axes, count, me):
    pieces = [x]
    for k in range(1, count):
        perm = [(i, (i + k) % count) for i in range(count)]
        pieces.append(lax.ppermute(x, axes, perm))
    by_offset = jnp.stack(pieces)
    order = (me - jnp.arange(count, dtype=jnp.int32)) % count
    return jnp.take(by_offset, order, axis=0)


def from_head(pieces, head, source):
    chosen = pieces[0]
    for k in range(1, len(pieces)):
        chosen = jnp.where((head ^ k) == source, pieces[k], chosen)
    return chosen


def shards(embed, donor_pos, acceptor_pos, target, donor_w, acceptor_w):
    batch, slab_rows, _ = embed.shape
    slab_sites = donor_pos.shape[1]
    width = donor_w.shape[1]
    scale = 1.0 / math.sqrt(width)
    n_seq = lax.axis_size("seq")
    n_head = lax.axis_size("head")
    slab = lax.axis_index("seq")
    sites = slab_sites * n_seq

    head = lax.axis_index("head")
    me = slab * n_head + head

    donor_match = site_match(donor_pos, slab_rows, slab).astype(jnp.bfloat16)
    acceptor_match = site_match(acceptor_pos, slab_rows, slab).astype(jnp.bfloat16)
    donor_rows = jnp.einsum(
        "bnr,brc->bnc", donor_match, embed, preferred_element_type=jnp.float32
    ).astype(jnp.bfloat16)
    acceptor_rows = jnp.einsum(
        "bnr,brc->bnc", acceptor_match, embed, preferred_element_type=jnp.float32
    ).astype(jnp.bfloat16)
    donor_part = jnp.einsum(
        "bnc,cp->bnp", donor_rows, donor_w, preferred_element_type=jnp.float32
    ).astype(jnp.bfloat16)
    acceptor_part = jnp.einsum(
        "bnc,cp->bnp", acceptor_rows, acceptor_w, preferred_element_type=jnp.float32
    ).astype(jnp.bfloat16)

    both = 2 * slab_sites
    assert both % n_head == 0
    quarter = both // n_head
    parts = jnp.concatenate([donor_part, acceptor_part], axis=1)
    assert n_head & (n_head - 1) == 0
    pieces = [lax.dynamic_slice_in_dim(parts, head * quarter, quarter, 1)]
    for k in range(1, n_head):
        outgoing = lax.dynamic_slice_in_dim(parts, (head ^ k) * quarter, quarter, 1)
        pieces.append(lax.ppermute(outgoing, "head", [(i, i ^ k) for i in range(n_head)]))
    total = jnp.zeros((batch, quarter, width), jnp.float32)
    for h in range(n_head):
        total = total + from_head(pieces, head, h).astype(jnp.float32)
    feat_quarter = total.astype(jnp.bfloat16)

    pieces = [feat_quarter]
    for k in range(1, n_head):
        pieces.append(lax.ppermute(feat_quarter, "head", [(i, i ^ k) for i in range(n_head)]))
    slab_feats = jnp.concatenate([from_head(pieces, head, h) for h in range(n_head)], axis=1)
    own_donor = slab_feats[:, :slab_sites]
    own_acceptor = slab_feats[:, slab_sites:]

    n_dp = lax.axis_size("dp")
    assert n_dp & (n_dp - 1) == 0 and n_dp >= 2
    dp = lax.axis_index("dp")
    pair = dp % 2
    channels = embed.shape[2]
    half = channels // 2
    part = width // n_seq
    def over_dp_bits(value):
        bit = 2
        while bit < n_dp:
            held = value.astype(jnp.bfloat16)
            perm = [(i, i ^ bit) for i in range(n_dp)]
            value = held.astype(jnp.float32) + lax.ppermute(held, "dp", perm).astype(jnp.float32)
            bit *= 2
        return value

    if n_seq == 2:
        target_own = lax.dynamic_slice_in_dim(target, slab * slab_sites, slab_sites, 2)
        scores_own = (
            jnp.einsum("bip,bjp->bij", own_donor, own_acceptor, preferred_element_type=jnp.float32)
            * scale
        )
        allowed_own = (donor_pos[:, :, None] >= 0) & (acceptor_pos[:, None, :] > donor_pos[:, :, None])
        slope_own = pair_slope(scores_own, target_own, allowed_own)
        early_acceptor = (
            jnp.einsum("bij,bip->bjp", slope_own, own_donor, preferred_element_type=jnp.float32) * scale
        ).astype(jnp.bfloat16)
        early_donor = (
            jnp.einsum("bij,bjp->bip", slope_own, own_acceptor, preferred_element_type=jnp.float32)
            * scale
        ).astype(jnp.bfloat16)
        first = slab == 0
        grad_early = jnp.where(first, early_acceptor, early_donor)
        rows_early = jnp.where(first, acceptor_rows, donor_rows)

        def to_seq_partner(rows, grad):
            local = jnp.einsum("bnc,bnp->pc", rows, grad, preferred_element_type=jnp.float32)
            local = local.astype(jnp.bfloat16)
            kept = lax.dynamic_slice_in_dim(local, pair * half, half, 1).astype(jnp.float32)
            outgoing = lax.dynamic_slice_in_dim(local, (1 - pair) * half, half, 1)
            kept = kept + lax.ppermute(outgoing, "dp", [(i, i ^ 1) for i in range(n_dp)]).astype(
                jnp.float32
            )
            held = kept.astype(jnp.bfloat16)
            own = lax.dynamic_slice_in_dim(held, slab * part, part, 0).astype(jnp.float32)
            return own, lax.dynamic_slice_in_dim(held, (1 - slab) * part, part, 0)

        def from_seq_partner(outgoing):
            return lax.ppermute(outgoing, "seq", [(0, 1), (1, 0)]).astype(jnp.float32)

        own_early, out_early = to_seq_partner(rows_early, grad_early)

    assert slab_sites <= width
    flags = jnp.zeros((batch, 8, width), jnp.bfloat16)
    flags = flags.at[:, 0, :slab_sites].set((donor_pos >= 0).astype(jnp.bfloat16))
    flags = flags.at[:, 1, :slab_sites].set((acceptor_pos >= 0).astype(jnp.bfloat16))
    donor_feat_all = jnp.zeros((batch, sites, width), jnp.bfloat16)
    acceptor_feat_all = jnp.zeros((batch, sites, width), jnp.bfloat16)
    donor_feat_all = lax.dynamic_update_slice_in_dim(donor_feat_all, own_donor, slab * slab_sites, 1)
    acceptor_feat_all = lax.dynamic_update_slice_in_dim(
        acceptor_feat_all, own_acceptor, slab * slab_sites, 1
    )
    donor_ok_all = jnp.zeros((batch, sites), jnp.bool_)
    acceptor_ok_all = jnp.zeros((batch, sites), jnp.bool_)
    target_col = jnp.zeros((batch, sites, slab_sites), target.dtype)
    own_cols = lax.dynamic_slice_in_dim(target, slab * slab_sites, slab_sites, 2)
    target_col = lax.dynamic_update_slice_in_dim(target_col, own_cols, slab * slab_sites, 1)
    for k in range(1, n_seq):
        sent = jnp.where(slab + k < n_seq, own_donor, own_acceptor)
        target_block = lax.dynamic_slice_in_dim(
            target, jnp.minimum(slab + k, n_seq - 1) * slab_sites, slab_sites, 2
        ).reshape(batch, slab_sites * slab_sites)
        target_rows = -(-(slab_sites * slab_sites) // width)
        target_block = jnp.pad(target_block, ((0, 0), (0, target_rows * width - slab_sites * slab_sites)))
        payload = jnp.concatenate(
            [sent, flags, target_block.reshape(batch, target_rows, width).astype(jnp.bfloat16)], axis=1
        )
        perm = [(i, (i + k) % n_seq) for i in range(n_seq)]
        arrived = lax.ppermute(payload, "seq", perm)
        source = (slab - k) % n_seq
        earlier = slab >= k
        target_in = (
            arrived[:, slab_sites + 8 :]
            .reshape(batch, target_rows * width)[:, : slab_sites * slab_sites]
            .reshape(batch, slab_sites, slab_sites)
        )
        target_col = jnp.where(
            earlier,
            lax.dynamic_update_slice_in_dim(target_col, target_in, source * slab_sites, 1),
            target_col,
        )
        feat_in = arrived[:, :slab_sites]
        donor_feat_all = jnp.where(
            earlier,
            lax.dynamic_update_slice_in_dim(donor_feat_all, feat_in, source * slab_sites, 1),
            donor_feat_all,
        )
        acceptor_feat_all = jnp.where(
            earlier,
            acceptor_feat_all,
            lax.dynamic_update_slice_in_dim(acceptor_feat_all, feat_in, source * slab_sites, 1),
        )
        donor_in = arrived[:, slab_sites, :slab_sites] > 0
        acceptor_in = arrived[:, slab_sites + 1, :slab_sites] > 0
        donor_ok_all = jnp.where(
            earlier,
            lax.dynamic_update_slice_in_dim(donor_ok_all, donor_in, source * slab_sites, 1),
            donor_ok_all,
        )
        acceptor_ok_all = jnp.where(
            earlier,
            acceptor_ok_all,
            lax.dynamic_update_slice_in_dim(acceptor_ok_all, acceptor_in, source * slab_sites, 1),
        )

    if n_seq == 2:
        out_early, arrived = lax.optimization_barrier((out_early, arrived))
        from_early = from_seq_partner(out_early)

    site_slab = jnp.arange(sites, dtype=jnp.int32) // slab_sites
    big = jnp.int32(1 << 30)
    acceptor_tiled = jnp.tile(acceptor_pos, (1, n_seq))
    acceptor_eff = jnp.where(
        site_slab[None, :] == slab,
        acceptor_tiled,
        jnp.where(
            (site_slab[None, :] > slab) & acceptor_ok_all, (slab + 1) * slab_rows, -1
        ),
    )
    donor_tiled = jnp.tile(donor_pos, (1, n_seq))
    donor_eff = jnp.where(
        site_slab[None, :] == slab,
        donor_tiled,
        jnp.where(
            site_slab[None, :] > slab,
            big,
            jnp.where(donor_ok_all, slab * slab_rows - 1, -1),
        ),
    )

    donor_feat = own_donor
    acceptor_feat = own_acceptor

    if n_seq == 2:
        first = slab == 0
        queries = jnp.where(first, own_donor, own_acceptor)
        keys = jnp.where(first, acceptor_feat_all, donor_feat_all)
        scores_late = (
            jnp.einsum("bip,bjp->bij", queries, keys, preferred_element_type=jnp.float32) * scale
        )
        allowed_row = (donor_pos[:, :, None] >= 0) & (acceptor_eff[:, None, :] > donor_pos[:, :, None])
        allowed_col = (donor_eff[:, None, :] >= 0) & (acceptor_pos[:, :, None] > donor_eff[:, None, :])
        allowed_late = jnp.where(first, allowed_row, allowed_col)
        target_late = jnp.where(first, target, jnp.swapaxes(target_col, 1, 2))
        slope_late = pair_slope(scores_late, target_late, allowed_late)
        grad_late = (
            jnp.einsum("bij,bjp->bip", slope_late, keys, preferred_element_type=jnp.float32) * scale
        ).astype(jnp.bfloat16)
    else:
        scores_row = (
            jnp.einsum("bip,bjp->bij", donor_feat, acceptor_feat_all, preferred_element_type=jnp.float32)
            * scale
        )
        allowed_row = (donor_pos[:, :, None] >= 0) & (acceptor_eff[:, None, :] > donor_pos[:, :, None])
        slope_row = pair_slope(scores_row, target, allowed_row)
        donor_grad = (
            jnp.einsum("bij,bjp->bip", slope_row, acceptor_feat_all, preferred_element_type=jnp.float32)
            * scale
        ).astype(jnp.bfloat16)

        scores_col = (
            jnp.einsum("bip,bjp->bij", donor_feat_all, acceptor_feat, preferred_element_type=jnp.float32)
            * scale
        )
        allowed_col = (donor_eff[:, :, None] >= 0) & (acceptor_pos[:, None, :] > donor_eff[:, :, None])
        slope_col = pair_slope(scores_col, target_col, allowed_col)
        acceptor_grad = (
            jnp.einsum("bij,bip->bjp", slope_col, donor_feat_all, preferred_element_type=jnp.float32)
            * scale
        ).astype(jnp.bfloat16)

    if n_seq == 2:
        grad_early = jnp.where(first, early_acceptor, early_donor)
        rows_early = jnp.where(first, acceptor_rows, donor_rows)
        rows_late = jnp.where(first, donor_rows, acceptor_rows)
        donor_grad = jnp.where(first, grad_late, grad_early)
        acceptor_grad = jnp.where(first, grad_early, grad_late)

        own_late, out_late = to_seq_partner(rows_late, grad_late)
        from_late = from_seq_partner(out_late)
        sum_early = own_early + from_late
        sum_late = own_late + from_early
        sum_late = over_dp_bits(sum_late)
        sum_early = over_dp_bits(sum_early)
        mine = jnp.stack(
            [jnp.where(first, sum_late, sum_early), jnp.where(first, sum_early, sum_late)]
        )
    else:
        local_dw = jnp.einsum(
            "bnc,bnp->pc", donor_rows, donor_grad, preferred_element_type=jnp.float32
        )
        local_aw = jnp.einsum(
            "bnc,bnp->pc", acceptor_rows, acceptor_grad, preferred_element_type=jnp.float32
        )
        blocks = jnp.stack([local_dw, local_aw]).astype(jnp.bfloat16)
        mine = lax.dynamic_slice_in_dim(blocks, pair * half, half, 2).astype(jnp.float32)
        outgoing = lax.dynamic_slice_in_dim(blocks, (1 - pair) * half, half, 2)
        mine = mine + lax.ppermute(outgoing, "dp", [(i, i ^ 1) for i in range(n_dp)]).astype(
            jnp.float32
        )
        held = mine.astype(jnp.bfloat16)
        mine = lax.dynamic_slice_in_dim(held, slab * part, part, 1).astype(jnp.float32)
        for k in range(1, n_seq):
            outgoing = lax.dynamic_slice_in_dim(held, ((slab + k) % n_seq) * part, part, 1)
            perm = [(i, (i + k) % n_seq) for i in range(n_seq)]
            mine = mine + lax.ppermute(outgoing, "seq", perm).astype(jnp.float32)
    donor_site = jnp.einsum("bnp,cp->bnc", donor_grad, donor_w, preferred_element_type=jnp.float32)
    acceptor_site = jnp.einsum(
        "bnp,cp->bnc", acceptor_grad, acceptor_w, preferred_element_type=jnp.float32
    )
    row_grad = place_rows(donor_match, donor_site) + place_rows(acceptor_match, acceptor_site)
    if n_seq != 2:
        mine = over_dp_bits(mine)
    other = lax.ppermute(mine, "dp", [(i, i ^ 1) for i in range(n_dp)])
    full = jnp.zeros(mine.shape[:2] + (2 * half,), jnp.float32)
    full = lax.dynamic_update_slice_in_dim(full, mine, pair * half, 2)
    mine = lax.dynamic_update_slice_in_dim(full, other, (1 - pair) * half, 2)
    mine = jnp.swapaxes(mine, 1, 2)
    column_major = Layout(major_to_minor=(1, 0))
    grad_dw = with_layout_constraint(mine[0], column_major)
    grad_aw = with_layout_constraint(mine[1], column_major)
    return (row_grad.astype(jnp.bfloat16), grad_dw, grad_aw)


def solution(mesh):
    in_specs = (
        P("dp", "seq", "head"),
        P("dp", "seq"),
        P("dp", "seq"),
        P("dp", "seq", None),
        P("head", None),
        P("head", None),
    )
    out_specs = (P("dp", "seq", "head"), P("head", "seq"), P("head", "seq"))
    return jax.shard_map(shards, mesh=mesh, in_specs=in_specs, out_specs=out_specs, check_vma=False)
```

```python
import math

import jax
import jax.numpy as jnp
from jax import lax
from jax.experimental.layout import Layout, with_layout_constraint
from jax.sharding import PartitionSpec as P


def site_match(positions, slab_rows, slab_index):
    local_pos = positions - slab_index * slab_rows
    return local_pos[:, :, None] == jnp.arange(slab_rows, dtype=jnp.int32)[None, None, :]


def pair_slope(scores, target, allowed):
    rate = jax.nn.softplus(scores) + 1.0
    return jnp.where(
        allowed, (1.0 - target.astype(jnp.float32) / rate) * jax.nn.sigmoid(scores), 0.0
    ).astype(jnp.bfloat16)


def place_rows(match_bf, values):
    upper = values.astype(jnp.bfloat16)
    lower = (values - upper.astype(jnp.float32)).astype(jnp.bfloat16)
    placed = jnp.einsum("bnr,bnc->brc", match_bf, upper, preferred_element_type=jnp.float32)
    return placed + jnp.einsum("bnr,bnc->brc", match_bf, lower, preferred_element_type=jnp.float32)


def gather_by_permute(x, axes, count, me):
    pieces = [x]
    for k in range(1, count):
        perm = [(i, (i + k) % count) for i in range(count)]
        pieces.append(lax.ppermute(x, axes, perm))
    by_offset = jnp.stack(pieces)
    order = (me - jnp.arange(count, dtype=jnp.int32)) % count
    return jnp.take(by_offset, order, axis=0)


def from_head(pieces, head, source):
    chosen = pieces[0]
    for k in range(1, len(pieces)):
        chosen = jnp.where((head ^ k) == source, pieces[k], chosen)
    return chosen


def shards(embed, donor_pos, acceptor_pos, target, donor_w, acceptor_w):
    batch, slab_rows, _ = embed.shape
    slab_sites = donor_pos.shape[1]
    width = donor_w.shape[1]
    scale = 1.0 / math.sqrt(width)
    n_seq = lax.axis_size("seq")
    n_head = lax.axis_size("head")
    slab = lax.axis_index("seq")
    sites = slab_sites * n_seq

    head = lax.axis_index("head")
    me = slab * n_head + head

    donor_match = site_match(donor_pos, slab_rows, slab).astype(jnp.bfloat16)
    acceptor_match = site_match(acceptor_pos, slab_rows, slab).astype(jnp.bfloat16)
    donor_rows = jnp.einsum(
        "bnr,brc->bnc", donor_match, embed, preferred_element_type=jnp.float32
    ).astype(jnp.bfloat16)
    acceptor_rows = jnp.einsum(
        "bnr,brc->bnc", acceptor_match, embed, preferred_element_type=jnp.float32
    ).astype(jnp.bfloat16)
    donor_part = jnp.einsum(
        "bnc,cp->bnp", donor_rows, donor_w, preferred_element_type=jnp.float32
    ).astype(jnp.bfloat16)
    acceptor_part = jnp.einsum(
        "bnc,cp->bnp", acceptor_rows, acceptor_w, preferred_element_type=jnp.float32
    ).astype(jnp.bfloat16)

    both = 2 * slab_sites
    assert both % n_head == 0
    quarter = both // n_head
    parts = jnp.concatenate([donor_part, acceptor_part], axis=1)
    assert n_head & (n_head - 1) == 0
    pieces = [lax.dynamic_slice_in_dim(parts, head * quarter, quarter, 1)]
    for k in range(1, n_head):
        outgoing = lax.dynamic_slice_in_dim(parts, (head ^ k) * quarter, quarter, 1)
        pieces.append(lax.ppermute(outgoing, "head", [(i, i ^ k) for i in range(n_head)]))
    total = jnp.zeros((batch, quarter, width), jnp.float32)
    for h in range(n_head):
        total = total + from_head(pieces, head, h).astype(jnp.float32)
    feat_quarter = total.astype(jnp.bfloat16)

    pieces = [feat_quarter]
    for k in range(1, n_head):
        pieces.append(lax.ppermute(feat_quarter, "head", [(i, i ^ k) for i in range(n_head)]))
    slab_feats = jnp.concatenate([from_head(pieces, head, h) for h in range(n_head)], axis=1)
    own_donor = slab_feats[:, :slab_sites]
    own_acceptor = slab_feats[:, slab_sites:]

    n_dp = lax.axis_size("dp")
    assert n_dp & (n_dp - 1) == 0 and n_dp >= 2
    dp = lax.axis_index("dp")
    pair = dp % 2
    channels = embed.shape[2]
    half = channels // 2
    part = width // n_seq
    def over_dp_bits(value):
        bit = 2
        while bit < n_dp:
            held = value.astype(jnp.bfloat16)
            perm = [(i, i ^ bit) for i in range(n_dp)]
            value = held.astype(jnp.float32) + lax.ppermute(held, "dp", perm).astype(jnp.float32)
            bit *= 2
        return value

    if n_seq == 2:
        target_own = lax.dynamic_slice_in_dim(target, slab * slab_sites, slab_sites, 2)
        scores_own = (
            jnp.einsum("bip,bjp->bij", own_donor, own_acceptor, preferred_element_type=jnp.float32)
            * scale
        )
        allowed_own = (donor_pos[:, :, None] >= 0) & (acceptor_pos[:, None, :] > donor_pos[:, :, None])
        slope_own = pair_slope(scores_own, target_own, allowed_own)
        own_part_acceptor = jnp.einsum(
            "bij,bip->bjp", slope_own, own_donor, preferred_element_type=jnp.float32
        )
        own_part_donor = jnp.einsum(
            "bij,bjp->bip", slope_own, own_acceptor, preferred_element_type=jnp.float32
        )
        early_acceptor = (own_part_acceptor * scale).astype(jnp.bfloat16)
        early_donor = (own_part_donor * scale).astype(jnp.bfloat16)
        first = slab == 0
        own_part_late = jnp.where(first, own_part_donor, own_part_acceptor)
        grad_early = jnp.where(first, early_acceptor, early_donor)
        rows_early = jnp.where(first, acceptor_rows, donor_rows)

        def to_seq_partner(rows, grad):
            local = jnp.einsum("bnc,bnp->pc", rows, grad, preferred_element_type=jnp.float32)
            local = local.astype(jnp.bfloat16)
            kept = lax.dynamic_slice_in_dim(local, pair * half, half, 1).astype(jnp.float32)
            outgoing = lax.dynamic_slice_in_dim(local, (1 - pair) * half, half, 1)
            kept = kept + lax.ppermute(outgoing, "dp", [(i, i ^ 1) for i in range(n_dp)]).astype(
                jnp.float32
            )
            held = kept.astype(jnp.bfloat16)
            own = lax.dynamic_slice_in_dim(held, slab * part, part, 0).astype(jnp.float32)
            return own, lax.dynamic_slice_in_dim(held, (1 - slab) * part, part, 0)

        def from_seq_partner(outgoing):
            return lax.ppermute(outgoing, "seq", [(0, 1), (1, 0)]).astype(jnp.float32)

        own_early, out_early = to_seq_partner(rows_early, grad_early)

    assert slab_sites <= width
    flags = jnp.zeros((batch, 8, width), jnp.bfloat16)
    flags = flags.at[:, 0, :slab_sites].set((donor_pos >= 0).astype(jnp.bfloat16))
    flags = flags.at[:, 1, :slab_sites].set((acceptor_pos >= 0).astype(jnp.bfloat16))
    donor_feat_all = jnp.zeros((batch, sites, width), jnp.bfloat16)
    acceptor_feat_all = jnp.zeros((batch, sites, width), jnp.bfloat16)
    donor_feat_all = lax.dynamic_update_slice_in_dim(donor_feat_all, own_donor, slab * slab_sites, 1)
    acceptor_feat_all = lax.dynamic_update_slice_in_dim(
        acceptor_feat_all, own_acceptor, slab * slab_sites, 1
    )
    donor_ok_all = jnp.zeros((batch, sites), jnp.bool_)
    acceptor_ok_all = jnp.zeros((batch, sites), jnp.bool_)
    target_col = jnp.zeros((batch, sites, slab_sites), target.dtype)
    own_cols = lax.dynamic_slice_in_dim(target, slab * slab_sites, slab_sites, 2)
    target_col = lax.dynamic_update_slice_in_dim(target_col, own_cols, slab * slab_sites, 1)
    for k in range(1, n_seq):
        sent = jnp.where(slab + k < n_seq, own_donor, own_acceptor)
        target_block = lax.dynamic_slice_in_dim(
            target, jnp.minimum(slab + k, n_seq - 1) * slab_sites, slab_sites, 2
        ).reshape(batch, slab_sites * slab_sites)
        target_rows = -(-(slab_sites * slab_sites) // width)
        target_block = jnp.pad(target_block, ((0, 0), (0, target_rows * width - slab_sites * slab_sites)))
        payload = jnp.concatenate(
            [sent, flags, target_block.reshape(batch, target_rows, width).astype(jnp.bfloat16)], axis=1
        )
        perm = [(i, (i + k) % n_seq) for i in range(n_seq)]
        arrived = lax.ppermute(payload, "seq", perm)
        source = (slab - k) % n_seq
        earlier = slab >= k
        target_in = (
            arrived[:, slab_sites + 8 :]
            .reshape(batch, target_rows * width)[:, : slab_sites * slab_sites]
            .reshape(batch, slab_sites, slab_sites)
        )
        target_col = jnp.where(
            earlier,
            lax.dynamic_update_slice_in_dim(target_col, target_in, source * slab_sites, 1),
            target_col,
        )
        feat_in = arrived[:, :slab_sites]
        donor_feat_all = jnp.where(
            earlier,
            lax.dynamic_update_slice_in_dim(donor_feat_all, feat_in, source * slab_sites, 1),
            donor_feat_all,
        )
        acceptor_feat_all = jnp.where(
            earlier,
            acceptor_feat_all,
            lax.dynamic_update_slice_in_dim(acceptor_feat_all, feat_in, source * slab_sites, 1),
        )
        donor_in = arrived[:, slab_sites, :slab_sites] > 0
        acceptor_in = arrived[:, slab_sites + 1, :slab_sites] > 0
        donor_ok_all = jnp.where(
            earlier,
            lax.dynamic_update_slice_in_dim(donor_ok_all, donor_in, source * slab_sites, 1),
            donor_ok_all,
        )
        acceptor_ok_all = jnp.where(
            earlier,
            acceptor_ok_all,
            lax.dynamic_update_slice_in_dim(acceptor_ok_all, acceptor_in, source * slab_sites, 1),
        )

    if n_seq == 2:
        out_early, arrived = lax.optimization_barrier((out_early, arrived))
        from_early = from_seq_partner(out_early)

    site_slab = jnp.arange(sites, dtype=jnp.int32) // slab_sites
    big = jnp.int32(1 << 30)
    acceptor_tiled = jnp.tile(acceptor_pos, (1, n_seq))
    acceptor_eff = jnp.where(
        site_slab[None, :] == slab,
        acceptor_tiled,
        jnp.where(
            (site_slab[None, :] > slab) & acceptor_ok_all, (slab + 1) * slab_rows, -1
        ),
    )
    donor_tiled = jnp.tile(donor_pos, (1, n_seq))
    donor_eff = jnp.where(
        site_slab[None, :] == slab,
        donor_tiled,
        jnp.where(
            site_slab[None, :] > slab,
            big,
            jnp.where(donor_ok_all, slab * slab_rows - 1, -1),
        ),
    )

    donor_feat = own_donor
    acceptor_feat = own_acceptor

    if n_seq == 2:
        first = slab == 0
        queries = jnp.where(first, own_donor, own_acceptor)
        scores_cross = (
            jnp.einsum("bip,bjp->bij", queries, feat_in, preferred_element_type=jnp.float32) * scale
        )
        own_ok = jnp.where(first, donor_pos >= 0, acceptor_pos >= 0)
        other_ok = jnp.where(first, acceptor_in, donor_in)
        allowed_cross = own_ok[:, :, None] & other_ok[:, None, :]
        target_cross = jnp.where(
            first,
            lax.dynamic_slice_in_dim(target, (1 - slab) * slab_sites, slab_sites, 2),
            jnp.swapaxes(target_in, 1, 2),
        )
        slope_cross = pair_slope(scores_cross, target_cross, allowed_cross)
        cross = jnp.einsum("bij,bjp->bip", slope_cross, feat_in, preferred_element_type=jnp.float32)
        grad_late = ((own_part_late + cross) * scale).astype(jnp.bfloat16)
    else:
        scores_row = (
            jnp.einsum("bip,bjp->bij", donor_feat, acceptor_feat_all, preferred_element_type=jnp.float32)
            * scale
        )
        allowed_row = (donor_pos[:, :, None] >= 0) & (acceptor_eff[:, None, :] > donor_pos[:, :, None])
        slope_row = pair_slope(scores_row, target, allowed_row)
        donor_grad = (
            jnp.einsum("bij,bjp->bip", slope_row, acceptor_feat_all, preferred_element_type=jnp.float32)
            * scale
        ).astype(jnp.bfloat16)

        scores_col = (
            jnp.einsum("bip,bjp->bij", donor_feat_all, acceptor_feat, preferred_element_type=jnp.float32)
            * scale
        )
        allowed_col = (donor_eff[:, :, None] >= 0) & (acceptor_pos[:, None, :] > donor_eff[:, :, None])
        slope_col = pair_slope(scores_col, target_col, allowed_col)
        acceptor_grad = (
            jnp.einsum("bij,bip->bjp", slope_col, donor_feat_all, preferred_element_type=jnp.float32)
            * scale
        ).astype(jnp.bfloat16)

    if n_seq == 2:
        grad_early = jnp.where(first, early_acceptor, early_donor)
        rows_early = jnp.where(first, acceptor_rows, donor_rows)
        rows_late = jnp.where(first, donor_rows, acceptor_rows)
        donor_grad = jnp.where(first, grad_late, grad_early)
        acceptor_grad = jnp.where(first, grad_early, grad_late)

        own_late, out_late = to_seq_partner(rows_late, grad_late)
        from_late = from_seq_partner(out_late)
        sum_early = own_early + from_late
        sum_late = own_late + from_early
        sum_late = over_dp_bits(sum_late)
        sum_early = over_dp_bits(sum_early)
        mine = jnp.stack(
            [jnp.where(first, sum_late, sum_early), jnp.where(first, sum_early, sum_late)]
        )
    else:
        local_dw = jnp.einsum(
            "bnc,bnp->pc", donor_rows, donor_grad, preferred_element_type=jnp.float32
        )
        local_aw = jnp.einsum(
            "bnc,bnp->pc", acceptor_rows, acceptor_grad, preferred_element_type=jnp.float32
        )
        blocks = jnp.stack([local_dw, local_aw]).astype(jnp.bfloat16)
        mine = lax.dynamic_slice_in_dim(blocks, pair * half, half, 2).astype(jnp.float32)
        outgoing = lax.dynamic_slice_in_dim(blocks, (1 - pair) * half, half, 2)
        mine = mine + lax.ppermute(outgoing, "dp", [(i, i ^ 1) for i in range(n_dp)]).astype(
            jnp.float32
        )
        held = mine.astype(jnp.bfloat16)
        mine = lax.dynamic_slice_in_dim(held, slab * part, part, 1).astype(jnp.float32)
        for k in range(1, n_seq):
            outgoing = lax.dynamic_slice_in_dim(held, ((slab + k) % n_seq) * part, part, 1)
            perm = [(i, (i + k) % n_seq) for i in range(n_seq)]
            mine = mine + lax.ppermute(outgoing, "seq", perm).astype(jnp.float32)
    donor_site = jnp.einsum("bnp,cp->bnc", donor_grad, donor_w, preferred_element_type=jnp.float32)
    acceptor_site = jnp.einsum(
        "bnp,cp->bnc", acceptor_grad, acceptor_w, preferred_element_type=jnp.float32
    )
    row_grad = place_rows(donor_match, donor_site) + place_rows(acceptor_match, acceptor_site)
    if n_seq != 2:
        mine = over_dp_bits(mine)
    other = lax.ppermute(mine, "dp", [(i, i ^ 1) for i in range(n_dp)])
    mine = jnp.where(pair == 0, jnp.concatenate([mine, other], 2), jnp.concatenate([other, mine], 2))
    mine = jnp.swapaxes(mine, 1, 2)
    column_major = Layout(major_to_minor=(1, 0))
    grad_dw = with_layout_constraint(mine[0], column_major)
    grad_aw = with_layout_constraint(mine[1], column_major)
    return (row_grad.astype(jnp.bfloat16), grad_dw, grad_aw)


def solution(mesh):
    in_specs = (
        P("dp", "seq", "head"),
        P("dp", "seq"),
        P("dp", "seq"),
        P("dp", "seq", None),
        P("head", None),
        P("head", None),
    )
    out_specs = (P("dp", "seq", "head"), P("head", "seq"), P("head", "seq"))
    return jax.shard_map(shards, mesh=mesh, in_specs=in_specs, out_specs=out_specs, check_vma=False)
```

```python
import math

import jax
import jax.numpy as jnp
from jax import lax
from jax.experimental.layout import Layout, with_layout_constraint
from jax.sharding import PartitionSpec as P


def site_match(positions, slab_rows, slab_index):
    local_pos = positions - slab_index * slab_rows
    return local_pos[:, :, None] == jnp.arange(slab_rows, dtype=jnp.int32)[None, None, :]


def pair_slope(scores, target, allowed):
    rate = jax.nn.softplus(scores) + 1.0
    return jnp.where(
        allowed, (1.0 - target.astype(jnp.float32) / rate) * jax.nn.sigmoid(scores), 0.0
    ).astype(jnp.bfloat16)


def place_rows(match_bf, values):
    upper = values.astype(jnp.bfloat16)
    lower = (values - upper.astype(jnp.float32)).astype(jnp.bfloat16)
    placed = jnp.einsum("bnr,bnc->brc", match_bf, upper, preferred_element_type=jnp.float32)
    return placed + jnp.einsum("bnr,bnc->brc", match_bf, lower, preferred_element_type=jnp.float32)


def gather_by_permute(x, axes, count, me):
    pieces = [x]
    for k in range(1, count):
        perm = [(i, (i + k) % count) for i in range(count)]
        pieces.append(lax.ppermute(x, axes, perm))
    by_offset = jnp.stack(pieces)
    order = (me - jnp.arange(count, dtype=jnp.int32)) % count
    return jnp.take(by_offset, order, axis=0)


def from_head(pieces, head, source):
    chosen = pieces[0]
    for k in range(1, len(pieces)):
        chosen = jnp.where((head ^ k) == source, pieces[k], chosen)
    return chosen


def shards(embed, donor_pos, acceptor_pos, target, donor_w, acceptor_w):
    batch, slab_rows, _ = embed.shape
    slab_sites = donor_pos.shape[1]
    width = donor_w.shape[1]
    scale = 1.0 / math.sqrt(width)
    n_seq = lax.axis_size("seq")
    n_head = lax.axis_size("head")
    slab = lax.axis_index("seq")
    sites = slab_sites * n_seq

    head = lax.axis_index("head")
    me = slab * n_head + head

    donor_match = site_match(donor_pos, slab_rows, slab).astype(jnp.bfloat16)
    acceptor_match = site_match(acceptor_pos, slab_rows, slab).astype(jnp.bfloat16)
    donor_rows = jnp.einsum(
        "bnr,brc->bnc", donor_match, embed, preferred_element_type=jnp.float32
    ).astype(jnp.bfloat16)
    acceptor_rows = jnp.einsum(
        "bnr,brc->bnc", acceptor_match, embed, preferred_element_type=jnp.float32
    ).astype(jnp.bfloat16)
    donor_part = jnp.einsum(
        "bnc,cp->bnp", donor_rows, donor_w, preferred_element_type=jnp.float32
    ).astype(jnp.bfloat16)
    acceptor_part = jnp.einsum(
        "bnc,cp->bnp", acceptor_rows, acceptor_w, preferred_element_type=jnp.float32
    ).astype(jnp.bfloat16)

    both = 2 * slab_sites
    assert both % n_head == 0
    quarter = both // n_head
    parts = jnp.concatenate([donor_part, acceptor_part], axis=1)
    assert n_head & (n_head - 1) == 0
    pieces = [lax.dynamic_slice_in_dim(parts, head * quarter, quarter, 1)]
    for k in range(1, n_head):
        outgoing = lax.dynamic_slice_in_dim(parts, (head ^ k) * quarter, quarter, 1)
        pieces.append(lax.ppermute(outgoing, "head", [(i, i ^ k) for i in range(n_head)]))
    total = jnp.zeros((batch, quarter, width), jnp.float32)
    for h in range(n_head):
        total = total + from_head(pieces, head, h).astype(jnp.float32)
    feat_quarter = total.astype(jnp.bfloat16)

    target_col = jnp.zeros((batch, sites, slab_sites), target.dtype)
    own_cols = lax.dynamic_slice_in_dim(target, slab * slab_sites, slab_sites, 2)
    target_col = lax.dynamic_update_slice_in_dim(target_col, own_cols, slab * slab_sites, 1)
    for k in range(1, n_seq):
        outgoing = lax.dynamic_slice_in_dim(
            target, jnp.minimum(slab + k, n_seq - 1) * slab_sites, slab_sites, 2
        )
        target_in = lax.ppermute(outgoing, "seq", [(i, i + k) for i in range(n_seq - k)])
        placed = lax.dynamic_update_slice_in_dim(
            target_col, target_in, jnp.maximum(slab - k, 0) * slab_sites, 1
        )
        target_col = jnp.where(slab >= k, placed, target_col)

    pieces = [feat_quarter]
    for k in range(1, n_head):
        pieces.append(lax.ppermute(feat_quarter, "head", [(i, i ^ k) for i in range(n_head)]))
    slab_feats = jnp.concatenate([from_head(pieces, head, h) for h in range(n_head)], axis=1)
    own_donor = slab_feats[:, :slab_sites]
    own_acceptor = slab_feats[:, slab_sites:]

    n_dp = lax.axis_size("dp")
    assert n_dp & (n_dp - 1) == 0 and n_dp >= 2
    dp = lax.axis_index("dp")
    pair = dp % 2
    channels = embed.shape[2]
    half = channels // 2
    part = width // n_seq
    def over_dp_bits(value):
        bit = 2
        while bit < n_dp:
            held = value.astype(jnp.bfloat16)
            perm = [(i, i ^ bit) for i in range(n_dp)]
            value = held.astype(jnp.float32) + lax.ppermute(held, "dp", perm).astype(jnp.float32)
            bit *= 2
        return value

    if n_seq == 2:
        target_own = lax.dynamic_slice_in_dim(target, slab * slab_sites, slab_sites, 2)
        scores_own = (
            jnp.einsum("bip,bjp->bij", own_donor, own_acceptor, preferred_element_type=jnp.float32)
            * scale
        )
        allowed_own = (donor_pos[:, :, None] >= 0) & (acceptor_pos[:, None, :] > donor_pos[:, :, None])
        slope_own = pair_slope(scores_own, target_own, allowed_own)
        own_part_acceptor = jnp.einsum(
            "bij,bip->bjp", slope_own, own_donor, preferred_element_type=jnp.float32
        )
        own_part_donor = jnp.einsum(
            "bij,bjp->bip", slope_own, own_acceptor, preferred_element_type=jnp.float32
        )
        early_acceptor = (own_part_acceptor * scale).astype(jnp.bfloat16)
        early_donor = (own_part_donor * scale).astype(jnp.bfloat16)
        first = slab == 0
        own_part_late = jnp.where(first, own_part_donor, own_part_acceptor)
        grad_early = jnp.where(first, early_acceptor, early_donor)
        rows_early = jnp.where(first, acceptor_rows, donor_rows)

        def to_seq_partner(rows, grad):
            local = jnp.einsum("bnc,bnp->pc", rows, grad, preferred_element_type=jnp.float32)
            local = local.astype(jnp.bfloat16)
            kept = lax.dynamic_slice_in_dim(local, pair * half, half, 1).astype(jnp.float32)
            outgoing = lax.dynamic_slice_in_dim(local, (1 - pair) * half, half, 1)
            kept = kept + lax.ppermute(outgoing, "dp", [(i, i ^ 1) for i in range(n_dp)]).astype(
                jnp.float32
            )
            held = kept.astype(jnp.bfloat16)
            own = lax.dynamic_slice_in_dim(held, slab * part, part, 0).astype(jnp.float32)
            return own, lax.dynamic_slice_in_dim(held, (1 - slab) * part, part, 0)

        def from_seq_partner(outgoing):
            return lax.ppermute(outgoing, "seq", [(0, 1), (1, 0)]).astype(jnp.float32)

        own_early, out_early = to_seq_partner(rows_early, grad_early)

    assert slab_sites <= width
    flags = jnp.zeros((batch, 8, width), jnp.bfloat16)
    flags = flags.at[:, 0, :slab_sites].set((donor_pos >= 0).astype(jnp.bfloat16))
    flags = flags.at[:, 1, :slab_sites].set((acceptor_pos >= 0).astype(jnp.bfloat16))
    donor_feat_all = jnp.zeros((batch, sites, width), jnp.bfloat16)
    acceptor_feat_all = jnp.zeros((batch, sites, width), jnp.bfloat16)
    donor_feat_all = lax.dynamic_update_slice_in_dim(donor_feat_all, own_donor, slab * slab_sites, 1)
    acceptor_feat_all = lax.dynamic_update_slice_in_dim(
        acceptor_feat_all, own_acceptor, slab * slab_sites, 1
    )
    donor_ok_all = jnp.zeros((batch, sites), jnp.bool_)
    acceptor_ok_all = jnp.zeros((batch, sites), jnp.bool_)
    for k in range(1, n_seq):
        sent = jnp.where(slab + k < n_seq, own_donor, own_acceptor)
        payload = jnp.concatenate([sent, flags], axis=1)
        perm = [(i, (i + k) % n_seq) for i in range(n_seq)]
        arrived = lax.ppermute(payload, "seq", perm)
        source = (slab - k) % n_seq
        earlier = slab >= k
        feat_in = arrived[:, :slab_sites]
        donor_feat_all = jnp.where(
            earlier,
            lax.dynamic_update_slice_in_dim(donor_feat_all, feat_in, source * slab_sites, 1),
            donor_feat_all,
        )
        acceptor_feat_all = jnp.where(
            earlier,
            acceptor_feat_all,
            lax.dynamic_update_slice_in_dim(acceptor_feat_all, feat_in, source * slab_sites, 1),
        )
        donor_in = arrived[:, slab_sites, :slab_sites] > 0
        acceptor_in = arrived[:, slab_sites + 1, :slab_sites] > 0
        donor_ok_all = jnp.where(
            earlier,
            lax.dynamic_update_slice_in_dim(donor_ok_all, donor_in, source * slab_sites, 1),
            donor_ok_all,
        )
        acceptor_ok_all = jnp.where(
            earlier,
            acceptor_ok_all,
            lax.dynamic_update_slice_in_dim(acceptor_ok_all, acceptor_in, source * slab_sites, 1),
        )

    if n_seq == 2:
        out_early, arrived = lax.optimization_barrier((out_early, arrived))
        from_early = from_seq_partner(out_early)

    site_slab = jnp.arange(sites, dtype=jnp.int32) // slab_sites
    big = jnp.int32(1 << 30)
    acceptor_tiled = jnp.tile(acceptor_pos, (1, n_seq))
    acceptor_eff = jnp.where(
        site_slab[None, :] == slab,
        acceptor_tiled,
        jnp.where(
            (site_slab[None, :] > slab) & acceptor_ok_all, (slab + 1) * slab_rows, -1
        ),
    )
    donor_tiled = jnp.tile(donor_pos, (1, n_seq))
    donor_eff = jnp.where(
        site_slab[None, :] == slab,
        donor_tiled,
        jnp.where(
            site_slab[None, :] > slab,
            big,
            jnp.where(donor_ok_all, slab * slab_rows - 1, -1),
        ),
    )

    donor_feat = own_donor
    acceptor_feat = own_acceptor

    if n_seq == 2:
        first = slab == 0
        queries = jnp.where(first, own_donor, own_acceptor)
        scores_cross = (
            jnp.einsum("bip,bjp->bij", queries, feat_in, preferred_element_type=jnp.float32) * scale
        )
        own_ok = jnp.where(first, donor_pos >= 0, acceptor_pos >= 0)
        other_ok = jnp.where(first, acceptor_in, donor_in)
        allowed_cross = own_ok[:, :, None] & other_ok[:, None, :]
        target_cross = jnp.where(
            first,
            lax.dynamic_slice_in_dim(target, (1 - slab) * slab_sites, slab_sites, 2),
            jnp.swapaxes(target_in, 1, 2),
        )
        slope_cross = pair_slope(scores_cross, target_cross, allowed_cross)
        cross = jnp.einsum("bij,bjp->bip", slope_cross, feat_in, preferred_element_type=jnp.float32)
        grad_late = ((own_part_late + cross) * scale).astype(jnp.bfloat16)
    else:
        scores_row = (
            jnp.einsum("bip,bjp->bij", donor_feat, acceptor_feat_all, preferred_element_type=jnp.float32)
            * scale
        )
        allowed_row = (donor_pos[:, :, None] >= 0) & (acceptor_eff[:, None, :] > donor_pos[:, :, None])
        slope_row = pair_slope(scores_row, target, allowed_row)
        donor_grad = (
            jnp.einsum("bij,bjp->bip", slope_row, acceptor_feat_all, preferred_element_type=jnp.float32)
            * scale
        ).astype(jnp.bfloat16)

        scores_col = (
            jnp.einsum("bip,bjp->bij", donor_feat_all, acceptor_feat, preferred_element_type=jnp.float32)
            * scale
        )
        allowed_col = (donor_eff[:, :, None] >= 0) & (acceptor_pos[:, None, :] > donor_eff[:, :, None])
        slope_col = pair_slope(scores_col, target_col, allowed_col)
        acceptor_grad = (
            jnp.einsum("bij,bip->bjp", slope_col, donor_feat_all, preferred_element_type=jnp.float32)
            * scale
        ).astype(jnp.bfloat16)

    if n_seq == 2:
        grad_early = jnp.where(first, early_acceptor, early_donor)
        rows_early = jnp.where(first, acceptor_rows, donor_rows)
        rows_late = jnp.where(first, donor_rows, acceptor_rows)
        donor_grad = jnp.where(first, grad_late, grad_early)
        acceptor_grad = jnp.where(first, grad_early, grad_late)

        own_late, out_late = to_seq_partner(rows_late, grad_late)
        from_late = from_seq_partner(out_late)
        sum_early = own_early + from_late
        sum_late = own_late + from_early
        sum_late = over_dp_bits(sum_late)
        sum_early = over_dp_bits(sum_early)
        mine = jnp.stack(
            [jnp.where(first, sum_late, sum_early), jnp.where(first, sum_early, sum_late)]
        )
    else:
        local_dw = jnp.einsum(
            "bnc,bnp->pc", donor_rows, donor_grad, preferred_element_type=jnp.float32
        )
        local_aw = jnp.einsum(
            "bnc,bnp->pc", acceptor_rows, acceptor_grad, preferred_element_type=jnp.float32
        )
        blocks = jnp.stack([local_dw, local_aw]).astype(jnp.bfloat16)
        mine = lax.dynamic_slice_in_dim(blocks, pair * half, half, 2).astype(jnp.float32)
        outgoing = lax.dynamic_slice_in_dim(blocks, (1 - pair) * half, half, 2)
        mine = mine + lax.ppermute(outgoing, "dp", [(i, i ^ 1) for i in range(n_dp)]).astype(
            jnp.float32
        )
        held = mine.astype(jnp.bfloat16)
        mine = lax.dynamic_slice_in_dim(held, slab * part, part, 1).astype(jnp.float32)
        for k in range(1, n_seq):
            outgoing = lax.dynamic_slice_in_dim(held, ((slab + k) % n_seq) * part, part, 1)
            perm = [(i, (i + k) % n_seq) for i in range(n_seq)]
            mine = mine + lax.ppermute(outgoing, "seq", perm).astype(jnp.float32)
    donor_site = jnp.einsum("bnp,cp->bnc", donor_grad, donor_w, preferred_element_type=jnp.float32)
    acceptor_site = jnp.einsum(
        "bnp,cp->bnc", acceptor_grad, acceptor_w, preferred_element_type=jnp.float32
    )
    row_grad = place_rows(donor_match, donor_site) + place_rows(acceptor_match, acceptor_site)
    if n_seq != 2:
        mine = over_dp_bits(mine)
    other = lax.ppermute(mine, "dp", [(i, i ^ 1) for i in range(n_dp)])
    mine = jnp.where(pair == 0, jnp.concatenate([mine, other], 2), jnp.concatenate([other, mine], 2))
    mine = jnp.swapaxes(mine, 1, 2)
    column_major = Layout(major_to_minor=(1, 0))
    grad_dw = with_layout_constraint(mine[0], column_major)
    grad_aw = with_layout_constraint(mine[1], column_major)
    return (row_grad.astype(jnp.bfloat16), grad_dw, grad_aw)


def solution(mesh):
    in_specs = (
        P("dp", "seq", "head"),
        P("dp", "seq"),
        P("dp", "seq"),
        P("dp", "seq", None),
        P("head", None),
        P("head", None),
    )
    out_specs = (P("dp", "seq", "head"), P("head", "seq"), P("head", "seq"))
    return jax.shard_map(shards, mesh=mesh, in_specs=in_specs, out_specs=out_specs, check_vma=False)
```
